128 devices in a mesh: seg: 8 (over x, core), leaf: 16 (over z, y).
Axes of the slice: x: 4, y: 4, z: 4, core: 2. Of those that a mesh axis runs over, the one named last changes fastest.
Arguments:
- queries: bfloat16 [32, 512, 5120], P('seg', 'leaf'), may hold values from -160 to 160
- leaf_keys: bfloat16 [32, 512, 1024], P('seg', 'leaf'), may hold values from -5 to 5
- leaf_values: bfloat16 [32, 512, 1024], P('seg', 'leaf'), may hold values from -6 to 6
- inner_keys: bfloat16 [16, 512, 1024], P('seg', 'leaf'), may hold values from -6 to 6
- inner_values: bfloat16 [16, 512, 1024], P('seg', 'leaf'), may hold values from -6 to 6
- out_grad: bfloat16 [32, 512, 5120], P('seg', 'leaf'), may hold values from -6 to 6
- ancestors: int32 [32, 4], replicated, may hold values from 0 to 15, as said below
- depths: int32 [32], replicated, may hold values from 3 to 4, as said below
Outputs:
- attention: bfloat16 [32, 512, 5120], P('seg', 'leaf')
- query_grad: bfloat16 [32, 512, 5120], P('seg', 'leaf')
- leaf_key_grad: bfloat16 [32, 512, 1024], P('seg', 'leaf')
- leaf_value_grad: bfloat16 [32, 512, 1024], P('seg', 'leaf')
- inner_key_grad: bfloat16 [16, 512, 1024], P('seg', 'leaf')
- inner_value_grad: bfloat16 [16, 512, 1024], P('seg', 'leaf')
The draws below stay inside these ranges and needn't reach their ends.
Inputs may be any that keep to these rules, and one draw needn't show every extreme that they name: `ancestors`: leaves l and m with l // 4 == m // 4 have the same row. Entry k of a row is the leaf's ancestor at tree level k, entry 0 the prompt's segment; entries at or past the leaf's depth are 0. The live entries of one row have different values of i // 2. `depths`: equal within each aligned block of 4 leaves; some leaf has 4.
All inputs are finite; a program needn't handle non-finite values.
Results may differ from the reference program's by a relative error of at most 0.03.
Values may be sent and summed in bfloat16 or wider, within the bound.
No kernel may reach another device: no remote copies, remote signals or barrier semaphores. Data moves between devices by JAX's collectives and lax.ppermute only.
A program may use at most 128 MiB of HBM per device.

```python
import math
import jax
import jax.numpy as jnp
from jax import lax

H = 40
KVH = 8
HD = 128
SEG_LEN = 512
LEAF_DEV = 4
MAXA = 4
SEG_DEV = 2
LEAVES = 32
INNER = 16


def tree_lists(key):
    group_count = LEAVES // LEAF_DEV
    owner_count = INNER // SEG_DEV
    root_count = max(1, group_count // 4)
    base_key = jax.random.fold_in(key, 101)
    deep_key, force_key, owner_key, root_key = jax.random.split(base_key, 4)
    extra = jax.random.randint(deep_key, (group_count,), 0, 2)
    forced = jax.random.randint(force_key, (), 0, group_count)
    extra = jnp.where(jnp.arange(group_count) == forced, 1, extra)
    counts = (MAXA - 1 + extra).astype(jnp.int32)
    tree_index = jax.random.randint(root_key, (group_count,), 0, root_count)
    order_keys = jax.random.split(owner_key, group_count)
    orders = jax.vmap(lambda one_key: jax.random.permutation(one_key, owner_count - 1))(order_keys)
    mid_owner = (tree_index[:, None] + 1 + orders[:, :MAXA - 1]) % owner_count
    mid_segment = mid_owner * SEG_DEV + (SEG_DEV - 1)
    lists = jnp.concatenate([(tree_index * SEG_DEV)[:, None], mid_segment], axis=1)
    level_ids = jnp.arange(MAXA)
    lists = jnp.where(level_ids[None, :] < counts[:, None], lists, 0).astype(jnp.int32)
    return (jnp.repeat(lists, LEAF_DEV, axis=0), jnp.repeat(counts, LEAF_DEV, axis=0))


def draw_ancestors(key, part):
    return tree_lists(key)[0]


def draw_depths(key, part):
    return tree_lists(key)[1]


def drawn_draw(key):
    base_key = jax.random.fold_in(key, 202)
    query_seed, keys_seed = jax.random.split(base_key, 2)
    group_heads = H // KVH
    keys = jnp.clip(jax.random.normal(keys_seed, (LEAVES, SEG_LEN, KVH, HD), jnp.float32), -4.5, 4.5)
    queries = jnp.clip(jax.random.normal(query_seed, (LEAVES, SEG_LEN, KVH, group_heads, HD), jnp.float32), -4.5, 4.5)
    return (queries.reshape(LEAVES, SEG_LEN, H * HD), keys.reshape(LEAVES, SEG_LEN, KVH * HD))


def draw_queries(key, part):
    return drawn_draw(key)[0].astype(jnp.bfloat16)


def draw_leaf_keys(key, part):
    return drawn_draw(key)[1].astype(jnp.bfloat16)


def block_levels(key, dims, cuts, low, high):
    level, own = 1.0, jax.random.fold_in(key, 6)
    for position, blocks in cuts:
        steps = jnp.exp(jax.random.uniform(jax.random.fold_in(own, position), (blocks,), jnp.float32, low / len(cuts), high / len(cuts)))
        level = level * jnp.repeat(steps, dims[position] // blocks).reshape([-1 if axis == position else 1 for axis in range(len(dims))])
    return level


def scatter_about(own_key, shape, width, most, shards=(), kind=jnp.bfloat16):
    entries = jax.random.normal(own_key, shape, jnp.float32) * width
    if len(shards) > 0:
        entries = block_levels(own_key, shape, shards, -0.22, 0.18) * entries
    return jnp.clip(entries, min=-most, max=most).astype(kind)


def setup_inputs(seed: int = 0) -> dict:
    seeds = jax.random.split(jax.random.key(seed), 9)
    queries = draw_queries(jax.random.fold_in(seeds[8], 71), 0)
    leaf_keys = draw_leaf_keys(jax.random.fold_in(seeds[8], 71), 0)
    leaf_values = scatter_about(seeds[2], (LEAVES, SEG_LEN, KVH * HD), 1.0, 6.0, ((0, 8), (1, 16)))
    inner_keys = scatter_about(seeds[3], (INNER, SEG_LEN, KVH * HD), 1.0, 6.0, ((0, 8), (1, 16)))
    inner_values = scatter_about(seeds[4], (INNER, SEG_LEN, KVH * HD), 1.0, 6.0, ((0, 8), (1, 16)))
    out_grad = scatter_about(seeds[5], (LEAVES, SEG_LEN, H * HD), 1.0, 6.0, ((0, 8), (1, 16)))
    ancestors = draw_ancestors(jax.random.fold_in(seeds[8], 71), 0)
    depths = draw_depths(jax.random.fold_in(seeds[8], 71), 0)
    return {"queries": queries, "leaf_keys": leaf_keys, "leaf_values": leaf_values, "inner_keys": inner_keys, "inner_values": inner_values, "out_grad": out_grad, "ancestors": ancestors, "depths": depths}


NEG_FILL = -1e+30

def rounded(values):
    return lax.optimization_barrier(values.astype(jnp.bfloat16)).astype(jnp.float32)

def attend_exact(queries_head, grads_head, key_anc, value_anc, private_keys, private_values, anc_visible, own_visible):
    logit_scale = 1.0 / math.sqrt(HD)
    batch_size = queries_head.shape[0]
    complete_queries = queries_head.astype(jnp.float32)
    complete_gradient = grads_head.astype(jnp.float32)
    every_key_row = jnp.concatenate([jnp.broadcast_to(key_anc[None], (batch_size,) + key_anc.shape), private_keys], axis=1).astype(jnp.float32)
    every_value_row = jnp.concatenate([jnp.broadcast_to(value_anc[None], (batch_size,) + value_anc.shape), private_values], axis=1).astype(jnp.float32)
    visible = jnp.concatenate([jnp.broadcast_to(anc_visible[None, :], (own_visible.shape[0], anc_visible.shape[0])), own_visible], axis=1)
    attention_logits = jnp.einsum('flh,feh->fle', complete_queries, every_key_row) * logit_scale
    attention_logits = jnp.where(visible[None], attention_logits, NEG_FILL)
    highest = lax.optimization_barrier(jnp.max(attention_logits, axis=-1, keepdims=True))
    weights = jnp.exp(attention_logits - highest)
    probs_full = weights / lax.optimization_barrier(jnp.sum(weights, axis=-1, keepdims=True))
    round_probabilities = rounded(probs_full)
    attention_result = jnp.einsum('oiz,ozv->oiv', round_probabilities, every_value_row)
    result_round = rounded(attention_result)
    delta_rows = lax.optimization_barrier(jnp.sum(complete_gradient * result_round, axis=-1, keepdims=True))
    probability_grads = jnp.einsum('flh,feh->fle', complete_gradient, every_value_row)
    score_grads = rounded(probs_full * (probability_grads - delta_rows))
    query_portion = jnp.einsum('oiz,ozv->oiv', score_grads, every_key_row) * logit_scale
    key_portion = jnp.einsum('ers,erc->esc', score_grads, complete_queries) * logit_scale
    value_portion = jnp.einsum('ers,erc->esc', round_probabilities, complete_gradient)
    anc_span = key_anc.shape[0]
    return (result_round.astype(jnp.bfloat16), query_portion.astype(jnp.bfloat16), lax.optimization_barrier(jnp.sum(key_portion[:, :anc_span], axis=0)), lax.optimization_barrier(jnp.sum(value_portion[:, :anc_span], axis=0)), key_portion[:, anc_span:], value_portion[:, anc_span:])

def reference(queries, leaf_keys, leaf_values, inner_keys, inner_values, out_grad, ancestors, depths):
    group_count = LEAVES // LEAF_DEV
    group_heads = H // KVH
    key_width = KVH * HD
    anc_span = MAXA * SEG_LEN
    level_ids = jnp.arange(MAXA, dtype=jnp.int32)
    positions = jnp.arange(SEG_LEN, dtype=jnp.int32)
    own_visible = jnp.tile(positions[None, :] <= positions[:, None], (group_heads, 1))

    def group_pass(running, group_index):
        acc_keys, acc_values = running
        first_leaf = group_index * LEAF_DEV
        anc_ids = lax.dynamic_index_in_dim(ancestors, first_leaf, 0, keepdims=False).astype(jnp.int32)
        level_count = lax.dynamic_index_in_dim(depths, first_leaf, 0, keepdims=False)
        anc_visible = jnp.repeat(level_ids < level_count, SEG_LEN)
        key_anc = jnp.take(inner_keys, anc_ids, axis=0).reshape(anc_span, KVH, HD)
        value_anc = jnp.take(inner_values, anc_ids, axis=0).reshape(anc_span, KVH, HD)
        query_group = lax.dynamic_slice_in_dim(queries, first_leaf, LEAF_DEV, 0).reshape(LEAF_DEV, SEG_LEN, KVH, group_heads, HD)
        grad_group = lax.dynamic_slice_in_dim(out_grad, first_leaf, LEAF_DEV, 0).reshape(LEAF_DEV, SEG_LEN, KVH, group_heads, HD)
        key_group = lax.dynamic_slice_in_dim(leaf_keys, first_leaf, LEAF_DEV, 0).reshape(LEAF_DEV, SEG_LEN, KVH, HD)
        value_group = lax.dynamic_slice_in_dim(leaf_values, first_leaf, LEAF_DEV, 0).reshape(LEAF_DEV, SEG_LEN, KVH, HD)

        def per_head(head_index):
            query_head = jnp.take(query_group, head_index, axis=2).transpose(0, 2, 1, 3).reshape(LEAF_DEV, group_heads * SEG_LEN, HD)
            grad_head = jnp.take(grad_group, head_index, axis=2).transpose(0, 2, 1, 3).reshape(LEAF_DEV, group_heads * SEG_LEN, HD)
            return attend_exact(query_head, grad_head, jnp.take(key_anc, head_index, axis=1), jnp.take(value_anc, head_index, axis=1), jnp.take(key_group, head_index, axis=2), jnp.take(value_group, head_index, axis=2), anc_visible, own_visible)
        result_heads, dquery_heads, dkey_anc, dvalue_anc, dkey_own, dvalue_own = lax.map(per_head, jnp.arange(KVH, dtype=jnp.int32))
        result_rows = result_heads.reshape(KVH, LEAF_DEV, group_heads, SEG_LEN, HD).transpose(1, 3, 0, 2, 4).reshape(LEAF_DEV, SEG_LEN, H * HD)
        dquery_rows = dquery_heads.reshape(KVH, LEAF_DEV, group_heads, SEG_LEN, HD).transpose(1, 3, 0, 2, 4).reshape(LEAF_DEV, SEG_LEN, H * HD)
        dkey_rows = dkey_own.transpose(1, 2, 0, 3).reshape(LEAF_DEV, SEG_LEN, key_width).astype(jnp.bfloat16)
        dvalue_rows = dvalue_own.transpose(1, 2, 0, 3).reshape(LEAF_DEV, SEG_LEN, key_width).astype(jnp.bfloat16)
        key_partial = rounded(dkey_anc.reshape(KVH, MAXA, SEG_LEN, HD).transpose(1, 2, 0, 3).reshape(MAXA, SEG_LEN, key_width))
        value_partial = rounded(dvalue_anc.reshape(KVH, MAXA, SEG_LEN, HD).transpose(1, 2, 0, 3).reshape(MAXA, SEG_LEN, key_width))
        acc_keys = acc_keys.at[anc_ids].add(key_partial)
        acc_values = acc_values.at[anc_ids].add(value_partial)
        return ((acc_keys, acc_values), (result_rows, dquery_rows, dkey_rows, dvalue_rows))
    zero_grads = jnp.zeros((INNER, SEG_LEN, key_width), jnp.float32)
    (acc_keys, acc_values), stacked = lax.scan(group_pass, (zero_grads, zero_grads), jnp.arange(group_count, dtype=jnp.int32))
    attention = stacked[0].reshape(LEAVES, SEG_LEN, H * HD)
    query_grad = stacked[1].reshape(LEAVES, SEG_LEN, H * HD)
    leaf_key_grad = stacked[2].reshape(LEAVES, SEG_LEN, key_width)
    leaf_value_grad = stacked[3].reshape(LEAVES, SEG_LEN, key_width)
    return (attention, query_grad, leaf_key_grad, leaf_value_grad, acc_keys.astype(jnp.bfloat16), acc_values.astype(jnp.bfloat16))
```

```python
import math

import jax
import jax.numpy as jnp
from jax import lax
from jax.sharding import PartitionSpec as P

HD = 128


NEG_FILL = -1e30


def attend_leaf(query_rows, grad_rows, key_anc, value_anc, own_keys, own_values, anc_visible, own_visible):
    logit_scale = 1.0 / math.sqrt(query_rows.shape[-1])
    score_anc = jnp.einsum("md,ad->ma", query_rows, key_anc, preferred_element_type=jnp.float32) * logit_scale
    score_own = jnp.einsum("md,sd->ms", query_rows, own_keys, preferred_element_type=jnp.float32) * logit_scale
    score_anc = jnp.where(anc_visible[None, :], score_anc, NEG_FILL)
    score_own = jnp.where(own_visible, score_own, NEG_FILL)
    highest = jnp.maximum(jnp.max(score_anc, axis=-1, keepdims=True), jnp.max(score_own, axis=-1, keepdims=True))
    weight_anc = jnp.exp(score_anc - highest)
    weight_own = jnp.exp(score_own - highest)
    denom_sum = jnp.sum(weight_anc, axis=-1, keepdims=True) + jnp.sum(weight_own, axis=-1, keepdims=True)
    prob_anc = weight_anc / denom_sum
    prob_own = weight_own / denom_sum
    round_anc = prob_anc.astype(jnp.bfloat16)
    round_own = prob_own.astype(jnp.bfloat16)
    result = jnp.einsum("ma,ad->md", round_anc, value_anc, preferred_element_type=jnp.float32) + jnp.einsum(
        "ms,sd->md", round_own, own_values, preferred_element_type=jnp.float32
    )
    result_round = result.astype(jnp.bfloat16)
    delta_rows = jnp.sum(grad_rows.astype(jnp.float32) * result_round.astype(jnp.float32), axis=-1, keepdims=True)
    dprob_anc = jnp.einsum("md,ad->ma", grad_rows, value_anc, preferred_element_type=jnp.float32)
    dprob_own = jnp.einsum("md,sd->ms", grad_rows, own_values, preferred_element_type=jnp.float32)
    dscore_anc = (prob_anc * (dprob_anc - delta_rows)).astype(jnp.bfloat16)
    dscore_own = (prob_own * (dprob_own - delta_rows)).astype(jnp.bfloat16)
    query_portion = (
        jnp.einsum("ma,ad->md", dscore_anc, key_anc, preferred_element_type=jnp.float32)
        + jnp.einsum("ms,sd->md", dscore_own, own_keys, preferred_element_type=jnp.float32)
    ) * logit_scale
    dkey_anc = jnp.einsum("ma,md->ad", dscore_anc, query_rows, preferred_element_type=jnp.float32) * logit_scale
    dvalue_anc = jnp.einsum("ma,md->ad", round_anc, grad_rows, preferred_element_type=jnp.float32)
    dkey_own = jnp.einsum("ms,md->sd", dscore_own, query_rows, preferred_element_type=jnp.float32) * logit_scale
    dvalue_own = jnp.einsum("ms,md->sd", round_own, grad_rows, preferred_element_type=jnp.float32)
    return result_round, query_portion.astype(jnp.bfloat16), dkey_anc, dvalue_anc, dkey_own, dvalue_own


def on_device(queries, leaf_keys, leaf_values, inner_keys, inner_values, out_grad, ancestors, depths):
    seg_count = lax.axis_size("seg")
    leaf_count = lax.axis_size("leaf")
    seg_here = lax.axis_index("seg")
    leaf_here = lax.axis_index("leaf")
    leaf_dev, rows_here, query_width = queries.shape
    slot_count = inner_keys.shape[0]
    key_width = leaf_keys.shape[2]
    kv_heads = key_width // HD
    group_heads = query_width // key_width
    head_width = group_heads * HD
    seg_len = rows_here * leaf_count
    levels = ancestors.shape[1]
    pair_count = leaf_count // kv_heads
    pair_leaves = leaf_dev // pair_count
    my_pair = leaf_here % pair_count

    group_lists = ancestors[::leaf_dev]
    group_depth = depths[::leaf_dev]
    owners = group_lists // slot_count
    slot_of = group_lists % slot_count
    level_ids = jnp.arange(levels, dtype=jnp.int32)
    alive_levels = level_ids[None, :] < group_depth[:, None]
    served = alive_levels & (owners == seg_here)
    slot_ids = jnp.arange(slot_count, dtype=jnp.int32)
    serve_pick = jnp.sum(
        (served[:, :, None] & (slot_of[:, :, None] == slot_ids[None, None, :])).astype(jnp.float32),
        axis=1,
    ).astype(jnp.bfloat16)
    stored = jnp.concatenate([inner_keys, inner_values], axis=2)
    outgoing = jnp.einsum("gs,src->grc", serve_pick, stored, preferred_element_type=jnp.float32).astype(
        jnp.bfloat16
    )
    arrived = lax.all_to_all(outgoing, "seg", split_axis=0, concat_axis=0, tiled=True)
    my_owners = jnp.take(owners, seg_here, axis=0)
    my_alive = jnp.take(alive_levels, seg_here, axis=0)
    ancestor_rows = jnp.where(
        my_alive[:, None, None], jnp.take(arrived, my_owners, axis=0), jnp.zeros((), jnp.bfloat16)
    )

    def to_heads(x, width):
        shaped = x.reshape(pair_count, pair_leaves, rows_here, kv_heads, width)
        return shaped.transpose(3, 0, 1, 2, 4).reshape(leaf_count, pair_leaves, rows_here, width)

    packed = jnp.concatenate(
        [to_heads(queries, head_width), to_heads(out_grad, head_width), to_heads(leaf_keys, HD), to_heads(leaf_values, HD)],
        axis=3,
    )
    got = lax.all_to_all(packed, "leaf", split_axis=0, concat_axis=0, tiled=True)
    got = got.transpose(1, 0, 2, 3).reshape(pair_leaves, seg_len, packed.shape[3])
    q_here = got[:, :, :head_width]
    g_here = got[:, :, head_width : 2 * head_width]
    k_own = got[:, :, 2 * head_width : 2 * head_width + HD]
    v_own = got[:, :, 2 * head_width + HD :]

    anc_k = ancestor_rows[:, :, :key_width].reshape(levels, rows_here, kv_heads, HD)
    anc_v = ancestor_rows[:, :, key_width:].reshape(levels, rows_here, kv_heads, HD)
    anc_heads = jnp.concatenate([anc_k, anc_v], axis=3).transpose(2, 0, 1, 3)
    anc_send = jnp.broadcast_to(anc_heads[:, None], (kv_heads, pair_count) + anc_heads.shape[1:]).reshape(
        (leaf_count,) + anc_heads.shape[1:]
    )
    anc_got = lax.all_to_all(anc_send, "leaf", split_axis=0, concat_axis=0, tiled=True)
    anc_got = anc_got.transpose(1, 0, 2, 3).reshape(levels * seg_len, 2 * HD)
    key_anc = anc_got[:, :HD]
    value_anc = anc_got[:, HD:]
    anc_visible = jnp.repeat(my_alive, seg_len)
    positions = jnp.arange(seg_len, dtype=jnp.int32)
    own_visible = jnp.tile(positions[None, :] <= positions[:, None], (group_heads, 1))

    def leaf_step(operands):
        q_leaf, g_leaf, k_leaf, v_leaf = operands
        q_rows = q_leaf.reshape(seg_len, group_heads, HD).transpose(1, 0, 2).reshape(group_heads * seg_len, HD)
        g_rows = g_leaf.reshape(seg_len, group_heads, HD).transpose(1, 0, 2).reshape(group_heads * seg_len, HD)
        res, dq, dka, dva, dko, dvo = attend_leaf(q_rows, g_rows, key_anc, value_anc, k_leaf, v_leaf, anc_visible, own_visible)
        res = res.reshape(group_heads, seg_len, HD).transpose(1, 0, 2).reshape(seg_len, head_width)
        dq = dq.reshape(group_heads, seg_len, HD).transpose(1, 0, 2).reshape(seg_len, head_width)
        return res, dq, dka, dva, dko, dvo

    res, dq, dka, dva, dko, dvo = lax.map(leaf_step, (q_here, g_here, k_own, v_own))
    anc_partial = jnp.concatenate([jnp.sum(dka, axis=0), jnp.sum(dva, axis=0)], axis=1)

    back = jnp.concatenate([res, dq, dko.astype(jnp.bfloat16), dvo.astype(jnp.bfloat16)], axis=2)
    back = back.reshape(pair_leaves, leaf_count, rows_here, back.shape[2]).transpose(1, 0, 2, 3)
    home = lax.all_to_all(back, "leaf", split_axis=0, concat_axis=0, tiled=True)
    home = home.reshape(kv_heads, pair_count, pair_leaves, rows_here, home.shape[3])

    def to_rows(x):
        width = x.shape[-1]
        return x.transpose(1, 2, 3, 0, 4).reshape(leaf_dev, rows_here, kv_heads * width)

    attention = to_rows(home[..., :head_width])
    query_grad = to_rows(home[..., head_width : 2 * head_width])
    leaf_key_grad = to_rows(home[..., 2 * head_width : 2 * head_width + HD])
    leaf_value_grad = to_rows(home[..., 2 * head_width + HD :])

    anc_back = anc_partial.astype(jnp.bfloat16).reshape(levels, leaf_count, rows_here, 2 * HD).transpose(1, 0, 2, 3)
    anc_home = lax.all_to_all(anc_back, "leaf", split_axis=0, concat_axis=0, tiled=True)
    anc_home = anc_home.astype(jnp.float32).reshape(kv_heads, pair_count, levels, rows_here, 2 * HD).sum(axis=1)
    part_keys = anc_home[..., :HD].transpose(1, 2, 0, 3).reshape(levels, rows_here, key_width)
    part_values = anc_home[..., HD:].transpose(1, 2, 0, 3).reshape(levels, rows_here, key_width)
    part_round = jnp.concatenate([part_keys, part_values], axis=2).astype(jnp.bfloat16)

    seg_ids = jnp.arange(seg_count, dtype=jnp.int32)
    homeward_pick = ((my_owners[None, :] == seg_ids[:, None]) & my_alive[None, :]).astype(jnp.bfloat16)
    homeward = jnp.einsum("ok,krc->orc", homeward_pick, part_round, preferred_element_type=jnp.float32).astype(
        jnp.bfloat16
    )
    returned = lax.all_to_all(homeward, "seg", split_axis=0, concat_axis=0, tiled=True)
    collected = jnp.einsum("gs,grc->src", serve_pick, returned, preferred_element_type=jnp.float32).astype(
        jnp.bfloat16
    )
    return (
        attention,
        query_grad,
        leaf_key_grad,
        leaf_value_grad,
        collected[:, :, :key_width],
        collected[:, :, key_width:],
    )


def solution(mesh):
    spec = P("seg", "leaf", None)
    return jax.shard_map(
        on_device,
        mesh=mesh,
        in_specs=(spec, spec, spec, spec, spec, spec, P(), P()),
        out_specs=(spec, spec, spec, spec, spec, spec),
        check_vma=False,
    )
```

```python
import math

import jax
import jax.numpy as jnp
from jax import lax
from jax.experimental import pallas as pl
from jax.experimental.pallas import tpu as pltpu
from jax.sharding import PartitionSpec as P

HD = 128


NEG_FILL = -1e30


def attend_kernel(mask_ref, q_ref, g_ref, ko_ref, vo_ref, ka_ref, va_ref,
                  o_ref, dq_ref, dko_ref, dvo_ref, dka_ref, dva_ref, dko_acc, dvo_acc):
    leaf_i = pl.program_id(0)
    head_i = pl.program_id(1)
    row_i = pl.program_id(2)
    head_count = pl.num_programs(1)
    row_count = pl.num_programs(2)
    block_rows = q_ref.shape[0]
    seg_len = ko_ref.shape[0]
    scale = 1.0 / math.sqrt(q_ref.shape[-1])

    @pl.when((leaf_i == 0) & (head_i == 0) & (row_i == 0))
    def _():
        dka_ref[...] = jnp.zeros_like(dka_ref)
        dva_ref[...] = jnp.zeros_like(dva_ref)

    @pl.when((head_i == 0) & (row_i == 0))
    def _():
        dko_acc[...] = jnp.zeros_like(dko_acc)
        dvo_acc[...] = jnp.zeros_like(dvo_acc)

    nt = (((1,), (1,)), ((), ()))
    tn = (((0,), (0,)), ((), ()))
    q = q_ref[...]
    g = g_ref[...]
    ka = ka_ref[...]
    va = va_ref[...]
    ko = ko_ref[...]
    vo = vo_ref[...]
    s_a = lax.dot_general(q, ka, nt, preferred_element_type=jnp.float32) * scale
    s_o = lax.dot_general(q, ko, nt, preferred_element_type=jnp.float32) * scale
    s_a = jnp.where(mask_ref[...] > 0.5, s_a, NEG_FILL)
    rows = row_i * block_rows + lax.broadcasted_iota(jnp.int32, (block_rows, seg_len), 0)
    cols = lax.broadcasted_iota(jnp.int32, (block_rows, seg_len), 1)
    s_o = jnp.where(cols <= rows, s_o, NEG_FILL)
    m = jnp.maximum(jnp.max(s_a, axis=1, keepdims=True), jnp.max(s_o, axis=1, keepdims=True))
    w_a = jnp.exp(s_a - m)
    w_o = jnp.exp(s_o - m)
    total = jnp.sum(w_a, axis=1, keepdims=True) + jnp.sum(w_o, axis=1, keepdims=True)
    inv = 1.0 / total
    p_a = w_a * inv
    p_o = w_o * inv
    pb_a = p_a.astype(jnp.bfloat16)
    pb_o = p_o.astype(jnp.bfloat16)
    o = jnp.dot(pb_a, va, preferred_element_type=jnp.float32) + jnp.dot(pb_o, vo, preferred_element_type=jnp.float32)
    o_b = o.astype(jnp.bfloat16)
    o_ref[...] = o_b
    delta = jnp.sum(g.astype(jnp.float32) * o_b.astype(jnp.float32), axis=1, keepdims=True)
    dp_a = lax.dot_general(g, va, nt, preferred_element_type=jnp.float32)
    dp_o = lax.dot_general(g, vo, nt, preferred_element_type=jnp.float32)
    ds_a = (p_a * (dp_a - delta)).astype(jnp.bfloat16)
    ds_o = (p_o * (dp_o - delta)).astype(jnp.bfloat16)
    dq = (jnp.dot(ds_a, ka, preferred_element_type=jnp.float32) + jnp.dot(ds_o, ko, preferred_element_type=jnp.float32)) * scale
    dq_ref[...] = dq.astype(jnp.bfloat16)
    dka_ref[...] += lax.dot_general(ds_a, q, tn, preferred_element_type=jnp.float32)
    dva_ref[...] += lax.dot_general(pb_a, g, tn, preferred_element_type=jnp.float32)
    dko_acc[...] += lax.dot_general(ds_o, q, tn, preferred_element_type=jnp.float32)
    dvo_acc[...] += lax.dot_general(pb_o, g, tn, preferred_element_type=jnp.float32)

    @pl.when((head_i == head_count - 1) & (row_i == row_count - 1))
    def _():
        dko_ref[...] = dko_acc[...] * scale
        dvo_ref[...] = dvo_acc[...]

    @pl.when((leaf_i == pl.num_programs(0) - 1) & (head_i == head_count - 1) & (row_i == row_count - 1))
    def _():
        dka_ref[...] = dka_ref[...] * scale


def attend_all(anc_mask, packed, anc_rows, heads, block_rows=256):
    leaves, seg_len, _ = packed.shape
    anc = anc_rows.shape[0]
    grid = (leaves, heads, seg_len // block_rows)
    qspec = pl.BlockSpec((None, block_rows, HD), lambda l, h, r: (l, r, h))
    gspec = pl.BlockSpec((None, block_rows, HD), lambda l, h, r: (l, r, heads + h))
    kospec = pl.BlockSpec((None, seg_len, HD), lambda l, h, r: (l, 0, 2 * heads))
    vospec = pl.BlockSpec((None, seg_len, HD), lambda l, h, r: (l, 0, 2 * heads + 1))
    kaspec = pl.BlockSpec((anc, HD), lambda l, h, r: (0, 0))
    vaspec = pl.BlockSpec((anc, HD), lambda l, h, r: (0, 1))
    maskspec = pl.BlockSpec((1, anc), lambda l, h, r: (0, 0))
    ownspec = pl.BlockSpec((None, seg_len, HD), lambda l, h, r: (l, 0, 0))
    ancspec = pl.BlockSpec((anc, HD), lambda l, h, r: (0, 0))
    out_rows = jax.ShapeDtypeStruct((leaves, seg_len, heads * HD), jnp.bfloat16)
    own_grad = jax.ShapeDtypeStruct((leaves, seg_len, HD), jnp.float32)
    anc_grad = jax.ShapeDtypeStruct((anc, HD), jnp.float32)
    return pl.pallas_call(
        attend_kernel,
        grid=grid,
        in_specs=[maskspec, qspec, gspec, kospec, vospec, kaspec, vaspec],
        out_specs=[qspec, qspec, ownspec, ownspec, ancspec, ancspec],
        out_shape=[out_rows, out_rows, own_grad, own_grad, anc_grad, anc_grad],
        scratch_shapes=[pltpu.VMEM((seg_len, HD), jnp.float32), pltpu.VMEM((seg_len, HD), jnp.float32)],
        compiler_params=pltpu.CompilerParams(dimension_semantics=("arbitrary", "arbitrary", "arbitrary")),
    )(anc_mask, packed, packed, packed, packed, anc_rows, anc_rows)


def on_device(queries, leaf_keys, leaf_values, inner_keys, inner_values, out_grad, ancestors, depths):
    seg_count = lax.axis_size("seg")
    leaf_count = lax.axis_size("leaf")
    seg_here = lax.axis_index("seg")
    leaf_here = lax.axis_index("leaf")
    leaf_dev, rows_here, query_width = queries.shape
    slot_count = inner_keys.shape[0]
    key_width = leaf_keys.shape[2]
    kv_heads = key_width // HD
    group_heads = query_width // key_width
    head_width = group_heads * HD
    seg_len = rows_here * leaf_count
    levels = ancestors.shape[1]
    pair_count = leaf_count // kv_heads
    pair_leaves = leaf_dev // pair_count
    my_pair = leaf_here % pair_count

    group_lists = ancestors[::leaf_dev]
    group_depth = depths[::leaf_dev]
    owners = group_lists // slot_count
    slot_of = group_lists % slot_count
    level_ids = jnp.arange(levels, dtype=jnp.int32)
    alive_levels = level_ids[None, :] < group_depth[:, None]
    served = alive_levels & (owners == seg_here)
    slot_ids = jnp.arange(slot_count, dtype=jnp.int32)
    serve_pick = jnp.sum(
        (served[:, :, None] & (slot_of[:, :, None] == slot_ids[None, None, :])).astype(jnp.float32),
        axis=1,
    ).astype(jnp.bfloat16)
    stored = jnp.concatenate([inner_keys, inner_values], axis=2)
    outgoing = jnp.einsum("gs,src->grc", serve_pick, stored, preferred_element_type=jnp.float32).astype(
        jnp.bfloat16
    )
    arrived = lax.all_to_all(outgoing, "seg", split_axis=0, concat_axis=0, tiled=True)
    my_owners = jnp.take(owners, seg_here, axis=0)
    my_alive = jnp.take(alive_levels, seg_here, axis=0)
    ancestor_rows = jnp.where(
        my_alive[:, None, None], jnp.take(arrived, my_owners, axis=0), jnp.zeros((), jnp.bfloat16)
    )

    def to_heads(x, width):
        shaped = x.reshape(pair_count, pair_leaves, rows_here, kv_heads, width)
        return shaped.transpose(3, 0, 1, 2, 4).reshape(leaf_count, pair_leaves, rows_here, width)

    packed = jnp.concatenate(
        [to_heads(queries, head_width), to_heads(out_grad, head_width), to_heads(leaf_keys, HD), to_heads(leaf_values, HD)],
        axis=3,
    )
    got = lax.all_to_all(packed, "leaf", split_axis=0, concat_axis=0, tiled=True)
    got = got.transpose(1, 0, 2, 3).reshape(pair_leaves, seg_len, packed.shape[3])

    anc_k = ancestor_rows[:, :, :key_width].reshape(levels, rows_here, kv_heads, HD)
    anc_v = ancestor_rows[:, :, key_width:].reshape(levels, rows_here, kv_heads, HD)
    anc_heads = jnp.concatenate([anc_k, anc_v], axis=3).transpose(2, 0, 1, 3)
    anc_send = jnp.broadcast_to(anc_heads[:, None], (kv_heads, pair_count) + anc_heads.shape[1:]).reshape(
        (leaf_count,) + anc_heads.shape[1:]
    )
    anc_got = lax.all_to_all(anc_send, "leaf", split_axis=0, concat_axis=0, tiled=True)
    anc_got = anc_got.transpose(1, 0, 2, 3).reshape(levels * seg_len, 2 * HD)
    anc_mask = jnp.repeat(my_alive, seg_len).astype(jnp.float32)[None, :]

    res, dq, dko, dvo, dka, dva = attend_all(anc_mask, got, anc_got, group_heads)
    anc_partial = jnp.concatenate([dka, dva], axis=1)

    back = jnp.concatenate([res, dq, dko.astype(jnp.bfloat16), dvo.astype(jnp.bfloat16)], axis=2)
    back = back.reshape(pair_leaves, leaf_count, rows_here, back.shape[2]).transpose(1, 0, 2, 3)
    home = lax.all_to_all(back, "leaf", split_axis=0, concat_axis=0, tiled=True)
    home = home.reshape(kv_heads, pair_count, pair_leaves, rows_here, home.shape[3])

    def to_rows(x):
        width = x.shape[-1]
        return x.transpose(1, 2, 3, 0, 4).reshape(leaf_dev, rows_here, kv_heads * width)

    attention = to_rows(home[..., :head_width])
    query_grad = to_rows(home[..., head_width : 2 * head_width])
    leaf_key_grad = to_rows(home[..., 2 * head_width : 2 * head_width + HD])
    leaf_value_grad = to_rows(home[..., 2 * head_width + HD :])

    anc_back = anc_partial.astype(jnp.bfloat16).reshape(levels, leaf_count, rows_here, 2 * HD).transpose(1, 0, 2, 3)
    anc_home = lax.all_to_all(anc_back, "leaf", split_axis=0, concat_axis=0, tiled=True)
    anc_home = anc_home.astype(jnp.float32).reshape(kv_heads, pair_count, levels, rows_here, 2 * HD).sum(axis=1)
    part_keys = anc_home[..., :HD].transpose(1, 2, 0, 3).reshape(levels, rows_here, key_width)
    part_values = anc_home[..., HD:].transpose(1, 2, 0, 3).reshape(levels, rows_here, key_width)
    part_round = jnp.concatenate([part_keys, part_values], axis=2).astype(jnp.bfloat16)

    seg_ids = jnp.arange(seg_count, dtype=jnp.int32)
    homeward_pick = ((my_owners[None, :] == seg_ids[:, None]) & my_alive[None, :]).astype(jnp.bfloat16)
    homeward = jnp.einsum("ok,krc->orc", homeward_pick, part_round, preferred_element_type=jnp.float32).astype(
        jnp.bfloat16
    )
    returned = lax.all_to_all(homeward, "seg", split_axis=0, concat_axis=0, tiled=True)
    collected = jnp.einsum("gs,grc->src", serve_pick, returned, preferred_element_type=jnp.float32).astype(
        jnp.bfloat16
    )
    return (
        attention,
        query_grad,
        leaf_key_grad,
        leaf_value_grad,
        collected[:, :, :key_width],
        collected[:, :, key_width:],
    )


def solution(mesh):
    spec = P("seg", "leaf", None)
    return jax.shard_map(
        on_device,
        mesh=mesh,
        in_specs=(spec, spec, spec, spec, spec, spec, P(), P()),
        out_specs=(spec, spec, spec, spec, spec, spec),
        check_vma=False,
    )
```

```python
import math

import jax
import jax.numpy as jnp
from jax import lax
from jax.experimental import pallas as pl
from jax.experimental.pallas import tpu as pltpu
from jax.sharding import PartitionSpec as P

HD = 128


NEG_FILL = -1e30


def attend_kernel(mask_ref, q_ref, g_ref, ko_ref, vo_ref, ka_ref, va_ref,
                  o_ref, dq_ref, dko_ref, dvo_ref, dka_ref, dva_ref, dko_acc, dvo_acc):
    leaf_i = pl.program_id(0)
    head_i = pl.program_id(1)
    row_i = pl.program_id(2)
    head_count = pl.num_programs(1)
    row_count = pl.num_programs(2)
    block_rows = q_ref.shape[0]
    seg_len = ko_ref.shape[0]
    scale = 1.0 / math.sqrt(q_ref.shape[-1])

    @pl.when((leaf_i == 0) & (head_i == 0) & (row_i == 0))
    def _():
        dka_ref[...] = jnp.zeros_like(dka_ref)
        dva_ref[...] = jnp.zeros_like(dva_ref)

    @pl.when((head_i == 0) & (row_i == 0))
    def _():
        dko_acc[...] = jnp.zeros_like(dko_acc)
        dvo_acc[...] = jnp.zeros_like(dvo_acc)

    nt = (((1,), (1,)), ((), ()))
    tn = (((0,), (0,)), ((), ()))
    q = q_ref[...]
    g = g_ref[...]
    ka = ka_ref[...]
    va = va_ref[...]
    ko = ko_ref[...]
    vo = vo_ref[...]
    s_a = lax.dot_general(q, ka, nt, preferred_element_type=jnp.float32) * scale
    s_o = lax.dot_general(q, ko, nt, preferred_element_type=jnp.float32) * scale
    s_a = jnp.where(mask_ref[...] > 0.5, s_a, NEG_FILL)
    rows = row_i * block_rows + lax.broadcasted_iota(jnp.int32, (block_rows, seg_len), 0)
    cols = lax.broadcasted_iota(jnp.int32, (block_rows, seg_len), 1)
    s_o = jnp.where(cols <= rows, s_o, NEG_FILL)
    m = jnp.maximum(jnp.max(s_a, axis=1, keepdims=True), jnp.max(s_o, axis=1, keepdims=True))
    w_a = jnp.exp(s_a - m)
    w_o = jnp.exp(s_o - m)
    total = jnp.sum(w_a, axis=1, keepdims=True) + jnp.sum(w_o, axis=1, keepdims=True)
    inv = 1.0 / total
    p_a = w_a * inv
    p_o = w_o * inv
    pb_a = p_a.astype(jnp.bfloat16)
    pb_o = p_o.astype(jnp.bfloat16)
    o = jnp.dot(pb_a, va, preferred_element_type=jnp.float32) + jnp.dot(pb_o, vo, preferred_element_type=jnp.float32)
    o_b = o.astype(jnp.bfloat16)
    o_ref[...] = o_b
    delta = jnp.sum(g.astype(jnp.float32) * o_b.astype(jnp.float32), axis=1, keepdims=True)
    dp_a = lax.dot_general(g, va, nt, preferred_element_type=jnp.float32)
    dp_o = lax.dot_general(g, vo, nt, preferred_element_type=jnp.float32)
    ds_a = (p_a * (dp_a - delta)).astype(jnp.bfloat16)
    ds_o = (p_o * (dp_o - delta)).astype(jnp.bfloat16)
    dq = (jnp.dot(ds_a, ka, preferred_element_type=jnp.float32) + jnp.dot(ds_o, ko, preferred_element_type=jnp.float32)) * scale
    dq_ref[...] = dq.astype(jnp.bfloat16)
    dka_ref[...] += lax.dot_general(ds_a, q, tn, preferred_element_type=jnp.float32)
    dva_ref[...] += lax.dot_general(pb_a, g, tn, preferred_element_type=jnp.float32)
    dko_acc[...] += lax.dot_general(ds_o, q, tn, preferred_element_type=jnp.float32)
    dvo_acc[...] += lax.dot_general(pb_o, g, tn, preferred_element_type=jnp.float32)

    @pl.when((head_i == head_count - 1) & (row_i == row_count - 1))
    def _():
        dko_ref[...] = dko_acc[...] * scale
        dvo_ref[...] = dvo_acc[...]

    @pl.when((leaf_i == pl.num_programs(0) - 1) & (head_i == head_count - 1) & (row_i == row_count - 1))
    def _():
        dka_ref[...] = dka_ref[...] * scale


def attend_all(anc_mask, packed, anc_rows, heads, block_rows=256):
    leaves, seg_len, _ = packed.shape
    anc = anc_rows.shape[0]
    grid = (leaves, heads, seg_len // block_rows)
    qspec = pl.BlockSpec((None, block_rows, HD), lambda l, h, r: (l, r, h))
    gspec = pl.BlockSpec((None, block_rows, HD), lambda l, h, r: (l, r, heads + h))
    kospec = pl.BlockSpec((None, seg_len, HD), lambda l, h, r: (l, 0, 2 * heads))
    vospec = pl.BlockSpec((None, seg_len, HD), lambda l, h, r: (l, 0, 2 * heads + 1))
    kaspec = pl.BlockSpec((anc, HD), lambda l, h, r: (0, 0))
    vaspec = pl.BlockSpec((anc, HD), lambda l, h, r: (0, 1))
    maskspec = pl.BlockSpec((1, anc), lambda l, h, r: (0, 0))
    ownspec = pl.BlockSpec((None, seg_len, HD), lambda l, h, r: (l, 0, 0))
    ancspec = pl.BlockSpec((anc, HD), lambda l, h, r: (0, 0))
    out_rows = jax.ShapeDtypeStruct((leaves, seg_len, heads * HD), jnp.bfloat16)
    own_grad = jax.ShapeDtypeStruct((leaves, seg_len, HD), jnp.float32)
    anc_grad = jax.ShapeDtypeStruct((anc, HD), jnp.float32)
    return pl.pallas_call(
        attend_kernel,
        grid=grid,
        in_specs=[maskspec, qspec, gspec, kospec, vospec, kaspec, vaspec],
        out_specs=[qspec, qspec, ownspec, ownspec, ancspec, ancspec],
        out_shape=[out_rows, out_rows, own_grad, own_grad, anc_grad, anc_grad],
        scratch_shapes=[pltpu.VMEM((seg_len, HD), jnp.float32), pltpu.VMEM((seg_len, HD), jnp.float32)],
        compiler_params=pltpu.CompilerParams(dimension_semantics=("arbitrary", "arbitrary", "arbitrary")),
    )(anc_mask, packed, packed, packed, packed, anc_rows, anc_rows)


def on_device(queries, leaf_keys, leaf_values, inner_keys, inner_values, out_grad, ancestors, depths):
    seg_count = lax.axis_size("seg")
    leaf_count = lax.axis_size("leaf")
    seg_here = lax.axis_index("seg")
    leaf_here = lax.axis_index("leaf")
    leaf_dev, rows_here, query_width = queries.shape
    slot_count = inner_keys.shape[0]
    key_width = leaf_keys.shape[2]
    kv_heads = key_width // HD
    group_heads = query_width // key_width
    head_width = group_heads * HD
    seg_len = rows_here * leaf_count
    levels = ancestors.shape[1]
    pair_count = leaf_count // kv_heads
    pair_leaves = leaf_dev // pair_count
    my_pair = leaf_here % pair_count

    group_lists = ancestors[::leaf_dev]
    group_depth = depths[::leaf_dev]
    owners = group_lists // slot_count
    slot_of = group_lists % slot_count
    level_ids = jnp.arange(levels, dtype=jnp.int32)
    alive_levels = level_ids[None, :] < group_depth[:, None]
    served = alive_levels & (owners == seg_here)
    slot_ids = jnp.arange(slot_count, dtype=jnp.int32)
    serve_pick = jnp.sum(
        (served[:, :, None] & (slot_of[:, :, None] == slot_ids[None, None, :])).astype(jnp.float32),
        axis=1,
    ).astype(jnp.bfloat16)
    stored = jnp.concatenate([inner_keys, inner_values], axis=2)
    outgoing = jnp.einsum("gs,src->grc", serve_pick, stored, preferred_element_type=jnp.float32).astype(
        jnp.bfloat16
    )
    arrived = lax.all_to_all(outgoing, "seg", split_axis=0, concat_axis=0, tiled=True)
    my_owners = jnp.take(owners, seg_here, axis=0)
    my_alive = jnp.take(alive_levels, seg_here, axis=0)
    ancestor_rows = jnp.where(
        my_alive[:, None, None], jnp.take(arrived, my_owners, axis=0), jnp.zeros((), jnp.bfloat16)
    )

    def to_heads(x, width):
        shaped = x.reshape(pair_count, pair_leaves, rows_here, kv_heads, width)
        return shaped.transpose(3, 0, 1, 2, 4).reshape(leaf_count, pair_leaves, rows_here, width)

    packed = jnp.concatenate(
        [to_heads(queries, head_width), to_heads(out_grad, head_width), to_heads(leaf_keys, HD), to_heads(leaf_values, HD)],
        axis=3,
    )
    anc_k = ancestor_rows[:, :, :key_width].reshape(levels, rows_here, kv_heads, HD)
    anc_v = ancestor_rows[:, :, key_width:].reshape(levels, rows_here, kv_heads, HD)
    anc_heads = jnp.concatenate([anc_k, anc_v], axis=3).transpose(2, 0, 1, 3)
    anc_send = jnp.broadcast_to(anc_heads[:, None], (kv_heads, pair_count) + anc_heads.shape[1:]).reshape(
        (leaf_count,) + anc_heads.shape[1:]
    )
    anc_got = lax.all_to_all(anc_send, "leaf", split_axis=0, concat_axis=0, tiled=True)
    anc_got = anc_got.transpose(1, 0, 2, 3).reshape(levels * seg_len, 2 * HD)
    anc_mask = jnp.repeat(my_alive, seg_len).astype(jnp.float32)[None, :]

    homes = []
    anc_partial = None
    for chunk in range(pair_leaves):
        got = lax.all_to_all(packed[:, chunk], "leaf", split_axis=0, concat_axis=0, tiled=True)
        got = got.reshape(1, seg_len, packed.shape[3])
        res, dq, dko, dvo, dka, dva = attend_all(anc_mask, got, anc_got, group_heads)
        part = jnp.concatenate([dka, dva], axis=1)
        anc_partial = part if anc_partial is None else anc_partial + part
        back = jnp.concatenate([res, dq, dko.astype(jnp.bfloat16), dvo.astype(jnp.bfloat16)], axis=2)
        back = back.reshape(leaf_count, rows_here, back.shape[2])
        homes.append(lax.all_to_all(back, "leaf", split_axis=0, concat_axis=0, tiled=True))
    home = jnp.stack(homes, axis=1)
    home = home.reshape(kv_heads, pair_count, pair_leaves, rows_here, home.shape[3])

    def to_rows(x):
        width = x.shape[-1]
        return x.transpose(1, 2, 3, 0, 4).reshape(leaf_dev, rows_here, kv_heads * width)

    attention = to_rows(home[..., :head_width])
    query_grad = to_rows(home[..., head_width : 2 * head_width])
    leaf_key_grad = to_rows(home[..., 2 * head_width : 2 * head_width + HD])
    leaf_value_grad = to_rows(home[..., 2 * head_width + HD :])

    anc_back = anc_partial.astype(jnp.bfloat16).reshape(levels, leaf_count, rows_here, 2 * HD).transpose(1, 0, 2, 3)
    anc_home = lax.all_to_all(anc_back, "leaf", split_axis=0, concat_axis=0, tiled=True)
    anc_home = anc_home.astype(jnp.float32).reshape(kv_heads, pair_count, levels, rows_here, 2 * HD).sum(axis=1)
    part_keys = anc_home[..., :HD].transpose(1, 2, 0, 3).reshape(levels, rows_here, key_width)
    part_values = anc_home[..., HD:].transpose(1, 2, 0, 3).reshape(levels, rows_here, key_width)
    part_round = jnp.concatenate([part_keys, part_values], axis=2).astype(jnp.bfloat16)

    seg_ids = jnp.arange(seg_count, dtype=jnp.int32)
    homeward_pick = ((my_owners[None, :] == seg_ids[:, None]) & my_alive[None, :]).astype(jnp.bfloat16)
    homeward = jnp.einsum("ok,krc->orc", homeward_pick, part_round, preferred_element_type=jnp.float32).astype(
        jnp.bfloat16
    )
    returned = lax.all_to_all(homeward, "seg", split_axis=0, concat_axis=0, tiled=True)
    collected = jnp.einsum("gs,grc->src", serve_pick, returned, preferred_element_type=jnp.float32).astype(
        jnp.bfloat16
    )
    return (
        attention,
        query_grad,
        leaf_key_grad,
        leaf_value_grad,
        collected[:, :, :key_width],
        collected[:, :, key_width:],
    )


def solution(mesh):
    spec = P("seg", "leaf", None)
    return jax.shard_map(
        on_device,
        mesh=mesh,
        in_specs=(spec, spec, spec, spec, spec, spec, P(), P()),
        out_specs=(spec, spec, spec, spec, spec, spec),
        check_vma=False,
    )
```

```python
import math

import jax
import jax.numpy as jnp
from jax import lax
from jax.experimental import pallas as pl
from jax.experimental.pallas import tpu as pltpu
from jax.sharding import PartitionSpec as P

HD = 128


NEG_FILL = -1e30


def attend_kernel(mask_ref, q_ref, g_ref, ko_ref, vo_ref, ka_ref, va_ref, dka_in, dva_in, dko_in, dvo_in,
                  o_ref, dq_ref, dka_ref, dva_ref, dko_ref, dvo_ref):
    leaf_i = pl.program_id(0)
    row_i = pl.program_id(1)
    block_rows = q_ref.shape[0]
    seg_len = ko_ref.shape[0]
    scale = 1.0 / math.sqrt(q_ref.shape[-1])

    @pl.when((leaf_i == 0) & (row_i == 0))
    def _():
        dka_ref[...] = dka_in[...]
        dva_ref[...] = dva_in[...]

    @pl.when(row_i == 0)
    def _():
        dko_ref[...] = dko_in[...]
        dvo_ref[...] = dvo_in[...]

    nt = (((1,), (1,)), ((), ()))
    tn = (((0,), (0,)), ((), ()))
    q = q_ref[...]
    g = g_ref[...]
    ka = ka_ref[...]
    va = va_ref[...]
    ko = ko_ref[...]
    vo = vo_ref[...]
    s_a = lax.dot_general(q, ka, nt, preferred_element_type=jnp.float32) * scale
    s_o = lax.dot_general(q, ko, nt, preferred_element_type=jnp.float32) * scale
    s_a = jnp.where(mask_ref[...] > 0.5, s_a, NEG_FILL)
    rows = row_i * block_rows + lax.broadcasted_iota(jnp.int32, (block_rows, seg_len), 0)
    cols = lax.broadcasted_iota(jnp.int32, (block_rows, seg_len), 1)
    s_o = jnp.where(cols <= rows, s_o, NEG_FILL)
    m = jnp.maximum(jnp.max(s_a, axis=1, keepdims=True), jnp.max(s_o, axis=1, keepdims=True))
    w_a = jnp.exp(s_a - m)
    w_o = jnp.exp(s_o - m)
    total = jnp.sum(w_a, axis=1, keepdims=True) + jnp.sum(w_o, axis=1, keepdims=True)
    inv = 1.0 / total
    p_a = w_a * inv
    p_o = w_o * inv
    pb_a = p_a.astype(jnp.bfloat16)
    pb_o = p_o.astype(jnp.bfloat16)
    o = jnp.dot(pb_a, va, preferred_element_type=jnp.float32) + jnp.dot(pb_o, vo, preferred_element_type=jnp.float32)
    o_b = o.astype(jnp.bfloat16)
    o_ref[...] = o_b
    delta = jnp.sum(g.astype(jnp.float32) * o_b.astype(jnp.float32), axis=1, keepdims=True)
    dp_a = lax.dot_general(g, va, nt, preferred_element_type=jnp.float32)
    dp_o = lax.dot_general(g, vo, nt, preferred_element_type=jnp.float32)
    ds_a = (p_a * (dp_a - delta)).astype(jnp.bfloat16)
    ds_o = (p_o * (dp_o - delta)).astype(jnp.bfloat16)
    dq = (jnp.dot(ds_a, ka, preferred_element_type=jnp.float32) + jnp.dot(ds_o, ko, preferred_element_type=jnp.float32)) * scale
    dq_ref[...] = dq.astype(jnp.bfloat16)
    dka_ref[...] += lax.dot_general(ds_a, q, tn, preferred_element_type=jnp.float32)
    dva_ref[...] += lax.dot_general(pb_a, g, tn, preferred_element_type=jnp.float32)
    dko_ref[...] += lax.dot_general(ds_o, q, tn, preferred_element_type=jnp.float32)
    dvo_ref[...] += lax.dot_general(pb_o, g, tn, preferred_element_type=jnp.float32)


def attend_head(anc_mask, q, g, own, anc_rows, accs, block_rows=256):
    leaves, seg_len, _ = q.shape
    anc = anc_rows.shape[0]
    grid = (leaves, seg_len // block_rows)
    qspec = pl.BlockSpec((None, block_rows, HD), lambda l, r: (l, r, 0))
    kospec = pl.BlockSpec((None, seg_len, HD), lambda l, r: (l, 0, 0))
    vospec = pl.BlockSpec((None, seg_len, HD), lambda l, r: (l, 0, 1))
    kaspec = pl.BlockSpec((anc, HD), lambda l, r: (0, 0))
    vaspec = pl.BlockSpec((anc, HD), lambda l, r: (0, 1))
    maskspec = pl.BlockSpec((1, anc), lambda l, r: (0, 0))
    ownspec = pl.BlockSpec((None, seg_len, HD), lambda l, r: (l, 0, 0))
    out_rows = jax.ShapeDtypeStruct(q.shape, jnp.bfloat16)
    return pl.pallas_call(
        attend_kernel,
        grid=grid,
        in_specs=[maskspec, qspec, qspec, kospec, vospec, kaspec, vaspec, kaspec, kaspec, ownspec, ownspec],
        out_specs=[qspec, qspec, kaspec, kaspec, ownspec, ownspec],
        out_shape=[out_rows, out_rows] + [jax.ShapeDtypeStruct(a.shape, jnp.float32) for a in accs],
        input_output_aliases={7: 2, 8: 3, 9: 4, 10: 5},
        compiler_params=pltpu.CompilerParams(dimension_semantics=("arbitrary", "arbitrary")),
    )(anc_mask, q, g, own, own, anc_rows, anc_rows, *accs)


def on_device(queries, leaf_keys, leaf_values, inner_keys, inner_values, out_grad, ancestors, depths):
    seg_count = lax.axis_size("seg")
    leaf_count = lax.axis_size("leaf")
    seg_here = lax.axis_index("seg")
    leaf_here = lax.axis_index("leaf")
    leaf_dev, rows_here, query_width = queries.shape
    slot_count = inner_keys.shape[0]
    key_width = leaf_keys.shape[2]
    kv_heads = key_width // HD
    group_heads = query_width // key_width
    head_width = group_heads * HD
    seg_len = rows_here * leaf_count
    levels = ancestors.shape[1]
    pair_count = leaf_count // kv_heads
    pair_leaves = leaf_dev // pair_count
    my_pair = leaf_here % pair_count

    group_lists = ancestors[::leaf_dev]
    group_depth = depths[::leaf_dev]
    owners = group_lists // slot_count
    slot_of = group_lists % slot_count
    level_ids = jnp.arange(levels, dtype=jnp.int32)
    alive_levels = level_ids[None, :] < group_depth[:, None]
    served = alive_levels & (owners == seg_here)
    slot_ids = jnp.arange(slot_count, dtype=jnp.int32)
    serve_pick = jnp.sum(
        (served[:, :, None] & (slot_of[:, :, None] == slot_ids[None, None, :])).astype(jnp.float32),
        axis=1,
    ).astype(jnp.bfloat16)
    stored = jnp.concatenate([inner_keys, inner_values], axis=2)
    outgoing = jnp.einsum("gs,src->grc", serve_pick, stored, preferred_element_type=jnp.float32).astype(
        jnp.bfloat16
    )
    arrived = lax.all_to_all(outgoing, "seg", split_axis=0, concat_axis=0, tiled=True)
    my_owners = jnp.take(owners, seg_here, axis=0)
    my_alive = jnp.take(alive_levels, seg_here, axis=0)
    ancestor_rows = jnp.where(
        my_alive[:, None, None], jnp.take(arrived, my_owners, axis=0), jnp.zeros((), jnp.bfloat16)
    )

    def to_heads(x, width):
        shaped = x.reshape(pair_count, pair_leaves, rows_here, kv_heads, width)
        return shaped.transpose(3, 0, 1, 2, 4).reshape(leaf_count, pair_leaves, rows_here, width)

    q_send = to_heads(queries, head_width)
    g_send = to_heads(out_grad, head_width)
    own_send = jnp.concatenate([to_heads(leaf_keys, HD), to_heads(leaf_values, HD)], axis=3)
    anc_k = ancestor_rows[:, :, :key_width].reshape(levels, rows_here, kv_heads, HD)
    anc_v = ancestor_rows[:, :, key_width:].reshape(levels, rows_here, kv_heads, HD)
    anc_heads = jnp.concatenate([anc_k, anc_v], axis=3).transpose(2, 0, 1, 3)
    anc_send = jnp.broadcast_to(anc_heads[:, None], (kv_heads, pair_count) + anc_heads.shape[1:]).reshape(
        (leaf_count,) + anc_heads.shape[1:]
    )
    anc_mask = jnp.repeat(my_alive, seg_len).astype(jnp.float32)[None, :]

    def head_in(head):
        cols = slice(head * HD, (head + 1) * HD)
        return jnp.concatenate([q_send[..., cols], g_send[..., cols]], axis=3)

    def rows_of(x):
        return x.transpose(1, 0, 2, 3).reshape(x.shape[1], seg_len, x.shape[3])

    def to_dest(x):
        return x.reshape(x.shape[0], leaf_count, rows_here, x.shape[2]).transpose(1, 0, 2, 3)

    first = lax.all_to_all(
        jnp.concatenate([own_send, anc_send, head_in(0)], axis=1), "leaf", split_axis=0, concat_axis=0, tiled=True
    )
    own_rows = rows_of(first[:, :pair_leaves])
    anc_got = rows_of(first[:, pair_leaves : pair_leaves + levels]).reshape(levels * seg_len, 2 * HD)
    inputs = {0: rows_of(first[:, pair_leaves + levels :])}
    outputs = {}
    homes = {}
    accs = (
        jnp.zeros((levels * seg_len, HD), jnp.float32),
        jnp.zeros((levels * seg_len, HD), jnp.float32),
        jnp.zeros((pair_leaves, seg_len, HD), jnp.float32),
        jnp.zeros((pair_leaves, seg_len, HD), jnp.float32),
    )
    for step in range(1, group_heads + 1):
        head = step - 1
        qg = inputs.pop(head)
        res, dq, *accs = attend_head(anc_mask, qg[..., :HD], qg[..., HD:], own_rows, anc_got, accs)
        outputs[head] = jnp.concatenate([res, dq], axis=2)
        parts = []
        if step < group_heads:
            parts.append(head_in(step))
        if step - 2 >= 0:
            parts.append(to_dest(outputs.pop(step - 2)))
        if step == group_heads:
            if parts:
                homes[step - 2] = lax.all_to_all(
                    jnp.concatenate(parts, axis=1), "leaf", split_axis=0, concat_axis=0, tiled=True
                )
            break
        got = lax.all_to_all(jnp.concatenate(parts, axis=1), "leaf", split_axis=0, concat_axis=0, tiled=True)
        inputs[step] = rows_of(got[:, :pair_leaves])
        if step - 2 >= 0:
            homes[step - 2] = got[:, pair_leaves:]
    dka, dva, dko, dvo = accs
    logit_scale = 1.0 / math.sqrt(HD)
    own_grads = jnp.concatenate([dko * logit_scale, dvo], axis=2).astype(jnp.bfloat16)
    anc_partial = jnp.concatenate([dka * logit_scale, dva], axis=1).astype(jnp.bfloat16)
    last_head = group_heads - 1
    tail = lax.all_to_all(
        jnp.concatenate(
            [to_dest(outputs.pop(last_head)), to_dest(own_grads), to_dest(anc_partial.reshape(levels, seg_len, 2 * HD))],
            axis=1,
        ),
        "leaf",
        split_axis=0,
        concat_axis=0,
        tiled=True,
    )
    homes[last_head] = tail[:, :pair_leaves]
    own_home = tail[:, pair_leaves : 2 * pair_leaves]
    anc_home = tail[:, 2 * pair_leaves :]
    out_heads = jnp.stack([homes[h] for h in range(group_heads)], axis=3)
    out_heads = out_heads.reshape(kv_heads, pair_count, pair_leaves, rows_here, group_heads, 2 * HD)

    def to_rows(x):
        width = x.shape[-1]
        return x.transpose(1, 2, 3, 0, 4).reshape(leaf_dev, rows_here, kv_heads * width)

    attention = to_rows(out_heads[..., :HD].reshape(kv_heads, pair_count, pair_leaves, rows_here, head_width))
    query_grad = to_rows(out_heads[..., HD:].reshape(kv_heads, pair_count, pair_leaves, rows_here, head_width))
    own_home = own_home.reshape(kv_heads, pair_count, pair_leaves, rows_here, 2 * HD)
    leaf_key_grad = to_rows(own_home[..., :HD])
    leaf_value_grad = to_rows(own_home[..., HD:])

    anc_home = anc_home.astype(jnp.float32).reshape(kv_heads, pair_count, levels, rows_here, 2 * HD).sum(axis=1)
    part_keys = anc_home[..., :HD].transpose(1, 2, 0, 3).reshape(levels, rows_here, key_width)
    part_values = anc_home[..., HD:].transpose(1, 2, 0, 3).reshape(levels, rows_here, key_width)
    part_round = jnp.concatenate([part_keys, part_values], axis=2).astype(jnp.bfloat16)

    seg_ids = jnp.arange(seg_count, dtype=jnp.int32)
    homeward_pick = ((my_owners[None, :] == seg_ids[:, None]) & my_alive[None, :]).astype(jnp.bfloat16)
    homeward = jnp.einsum("ok,krc->orc", homeward_pick, part_round, preferred_element_type=jnp.float32).astype(
        jnp.bfloat16
    )
    returned = lax.all_to_all(homeward, "seg", split_axis=0, concat_axis=0, tiled=True)
    collected = jnp.einsum("gs,grc->src", serve_pick, returned, preferred_element_type=jnp.float32).astype(
        jnp.bfloat16
    )
    return (
        attention,
        query_grad,
        leaf_key_grad,
        leaf_value_grad,
        collected[:, :, :key_width],
        collected[:, :, key_width:],
    )


def solution(mesh):
    spec = P("seg", "leaf", None)
    return jax.shard_map(
        on_device,
        mesh=mesh,
        in_specs=(spec, spec, spec, spec, spec, spec, P(), P()),
        out_specs=(spec, spec, spec, spec, spec, spec),
        check_vma=False,
    )
```

```python
import functools
import math

import jax
import jax.numpy as jnp
from jax import lax
from jax.experimental import pallas as pl
from jax.experimental.pallas import tpu as pltpu
from jax.sharding import PartitionSpec as P

HD = 128


NEG_FILL = -1e30


def attend_kernel(row_half, half_rows, mask_ref, qg_ref, ko_ref, vo_ref, ka_ref, va_ref,
                  dka_in, dva_in, dko_in, dvo_in, out_ref, dka_ref, dva_ref, dko_ref, dvo_ref):
    head_i = pl.program_id(0)
    sources = qg_ref.shape[0]
    block_rows = sources * half_rows
    seg_len = ko_ref.shape[0] * ko_ref.shape[1]
    scale = 1.0 / math.sqrt(HD)

    @pl.when(head_i == 0)
    def _():
        dka_ref[...] = dka_in[...]
        dva_ref[...] = dva_in[...]
        dko_ref[...] = dko_in[...]
        dvo_ref[...] = dvo_in[...]

    nt = (((1,), (1,)), ((), ()))
    tn = (((0,), (0,)), ((), ()))
    qg = qg_ref[...]
    q = qg[:, :, :HD].reshape(block_rows, HD)
    g = qg[:, :, HD:].reshape(block_rows, HD)
    ka = ka_ref[...]
    va = va_ref[...]
    ko = ko_ref[...].reshape(seg_len, HD)
    vo = vo_ref[...].reshape(seg_len, HD)
    s_a = lax.dot_general(q, ka, nt, preferred_element_type=jnp.float32) * scale
    s_o = lax.dot_general(q, ko, nt, preferred_element_type=jnp.float32) * scale
    s_a = jnp.where(mask_ref[...] > 0.5, s_a, NEG_FILL)
    local = lax.broadcasted_iota(jnp.int32, (block_rows, seg_len), 0)
    rows = (local // half_rows) * (2 * half_rows) + row_half * half_rows + local % half_rows
    cols = lax.broadcasted_iota(jnp.int32, (block_rows, seg_len), 1)
    s_o = jnp.where(cols <= rows, s_o, NEG_FILL)
    m = jnp.maximum(jnp.max(s_a, axis=1, keepdims=True), jnp.max(s_o, axis=1, keepdims=True))
    w_a = jnp.exp(s_a - m)
    w_o = jnp.exp(s_o - m)
    total = jnp.sum(w_a, axis=1, keepdims=True) + jnp.sum(w_o, axis=1, keepdims=True)
    inv = 1.0 / total
    p_a = w_a * inv
    p_o = w_o * inv
    pb_a = p_a.astype(jnp.bfloat16)
    pb_o = p_o.astype(jnp.bfloat16)
    o = jnp.dot(pb_a, va, preferred_element_type=jnp.float32) + jnp.dot(pb_o, vo, preferred_element_type=jnp.float32)
    o_b = o.astype(jnp.bfloat16)
    delta = jnp.sum(g.astype(jnp.float32) * o_b.astype(jnp.float32), axis=1, keepdims=True)
    dp_a = lax.dot_general(g, va, nt, preferred_element_type=jnp.float32)
    dp_o = lax.dot_general(g, vo, nt, preferred_element_type=jnp.float32)
    ds_a = (p_a * (dp_a - delta)).astype(jnp.bfloat16)
    ds_o = (p_o * (dp_o - delta)).astype(jnp.bfloat16)
    dq = (jnp.dot(ds_a, ka, preferred_element_type=jnp.float32) + jnp.dot(ds_o, ko, preferred_element_type=jnp.float32)) * scale
    out_ref[:, :, :HD] = o_b.reshape(sources, half_rows, HD)
    out_ref[:, :, HD:] = dq.astype(jnp.bfloat16).reshape(sources, half_rows, HD)
    dka_ref[...] += lax.dot_general(ds_a, q, tn, preferred_element_type=jnp.float32)
    dva_ref[...] += lax.dot_general(pb_a, g, tn, preferred_element_type=jnp.float32)
    dko_ref[...] += lax.dot_general(ds_o, q, tn, preferred_element_type=jnp.float32).reshape(dko_ref.shape)
    dvo_ref[...] += lax.dot_general(pb_o, g, tn, preferred_element_type=jnp.float32).reshape(dvo_ref.shape)


def attend_chunk(row_half, leaf, anc_mask, qg, own, anc_rows, accs):
    sources, heads, half_rows, _ = qg.shape
    rows_here = own.shape[2]
    anc = anc_rows.shape[0]
    qgspec = pl.BlockSpec((sources, None, half_rows, 2 * HD), lambda h: (0, h, 0, 0))
    kospec = pl.BlockSpec((sources, None, rows_here, HD), lambda h: (0, leaf, 0, 0))
    vospec = pl.BlockSpec((sources, None, rows_here, HD), lambda h: (0, leaf, 0, 1))
    kaspec = pl.BlockSpec((anc, HD), lambda h: (0, 0))
    vaspec = pl.BlockSpec((anc, HD), lambda h: (0, 1))
    maskspec = pl.BlockSpec((1, anc), lambda h: (0, 0))
    ownspec = pl.BlockSpec((sources, rows_here, HD), lambda h: (0, 0, 0))
    return pl.pallas_call(
        functools.partial(attend_kernel, row_half, half_rows),
        grid=(heads,),
        in_specs=[maskspec, qgspec, kospec, vospec, kaspec, vaspec, kaspec, kaspec, ownspec, ownspec],
        out_specs=[qgspec, kaspec, kaspec, ownspec, ownspec],
        out_shape=[jax.ShapeDtypeStruct(qg.shape, jnp.bfloat16)] + [jax.ShapeDtypeStruct(a.shape, jnp.float32) for a in accs],
        input_output_aliases={6: 1, 7: 2, 8: 3, 9: 4},
        compiler_params=pltpu.CompilerParams(dimension_semantics=("arbitrary",)),
    )(anc_mask, qg, own, own, anc_rows, anc_rows, *accs)


def on_device(queries, leaf_keys, leaf_values, inner_keys, inner_values, out_grad, ancestors, depths):
    seg_count = lax.axis_size("seg")
    leaf_count = lax.axis_size("leaf")
    seg_here = lax.axis_index("seg")
    leaf_dev, rows_here, query_width = queries.shape
    slot_count = inner_keys.shape[0]
    key_width = leaf_keys.shape[2]
    kv_heads = key_width // HD
    group_heads = query_width // key_width
    seg_len = rows_here * leaf_count
    levels = ancestors.shape[1]
    pair_count = leaf_count // kv_heads
    pair_leaves = leaf_dev // pair_count
    halves = 2
    half_rows = rows_here // halves

    group_lists = ancestors[::leaf_dev]
    group_depth = depths[::leaf_dev]
    owners = group_lists // slot_count
    slot_of = group_lists % slot_count
    level_ids = jnp.arange(levels, dtype=jnp.int32)
    alive_levels = level_ids[None, :] < group_depth[:, None]
    served = alive_levels & (owners == seg_here)
    slot_ids = jnp.arange(slot_count, dtype=jnp.int32)
    serve_pick = jnp.sum(
        (served[:, :, None] & (slot_of[:, :, None] == slot_ids[None, None, :])).astype(jnp.float32),
        axis=1,
    ).astype(jnp.bfloat16)
    stored = jnp.concatenate([inner_keys, inner_values], axis=2)
    outgoing = jnp.einsum("gs,src->grc", serve_pick, stored, preferred_element_type=jnp.float32).astype(
        jnp.bfloat16
    )
    arrived = lax.all_to_all(outgoing, "seg", split_axis=0, concat_axis=0, tiled=True)
    my_owners = jnp.take(owners, seg_here, axis=0)
    my_alive = jnp.take(alive_levels, seg_here, axis=0)
    ancestor_rows = jnp.where(
        my_alive[:, None, None], jnp.take(arrived, my_owners, axis=0), jnp.zeros((), jnp.bfloat16)
    )

    def exchange(x):
        return lax.all_to_all(x, "leaf", split_axis=0, concat_axis=0, tiled=True)

    own_kv = jnp.concatenate(
        [leaf_keys.reshape(leaf_dev, rows_here, kv_heads, 1, HD), leaf_values.reshape(leaf_dev, rows_here, kv_heads, 1, HD)],
        axis=3,
    ).reshape(pair_count, pair_leaves, rows_here, kv_heads, 2 * HD)
    own_send = own_kv.transpose(3, 0, 1, 2, 4).reshape(leaf_count, pair_leaves * rows_here, 2 * HD)
    anc_kv = jnp.concatenate(
        [
            ancestor_rows[:, :, :key_width].reshape(levels, rows_here, kv_heads, 1, HD),
            ancestor_rows[:, :, key_width:].reshape(levels, rows_here, kv_heads, 1, HD),
        ],
        axis=3,
    ).reshape(levels, rows_here, kv_heads, 2 * HD)
    anc_heads = anc_kv.transpose(2, 0, 1, 3)
    anc_send = jnp.broadcast_to(anc_heads[:, None], (kv_heads, pair_count) + anc_heads.shape[1:]).reshape(
        leaf_count, levels * rows_here, 2 * HD
    )
    qg_all = jnp.concatenate(
        [
            queries.reshape(pair_count, pair_leaves, halves, half_rows, kv_heads, group_heads, 1, HD),
            out_grad.reshape(pair_count, pair_leaves, halves, half_rows, kv_heads, group_heads, 1, HD),
        ],
        axis=6,
    )
    qg_send = qg_all.transpose(1, 2, 4, 0, 5, 3, 6, 7).reshape(
        pair_leaves, halves, leaf_count, group_heads * half_rows, 2 * HD
    )
    chunks = [(leaf, half) for leaf in range(pair_leaves) for half in range(halves)]
    chunk_rows = group_heads * half_rows

    own_rows_n = pair_leaves * rows_here
    anc_rows_n = levels * rows_here
    first = exchange(jnp.concatenate([own_send, anc_send, qg_send[0, 0]], axis=1))
    own_got = first[:, :own_rows_n].reshape(leaf_count, pair_leaves, rows_here, 2 * HD)
    anc_got = first[:, own_rows_n : own_rows_n + anc_rows_n].reshape(leaf_count * anc_rows_n, 2 * HD)
    inputs = {0: first[:, own_rows_n + anc_rows_n :]}
    anc_mask = jnp.broadcast_to(
        jnp.repeat(my_alive, rows_here).astype(jnp.float32)[None, :], (leaf_count, anc_rows_n)
    ).reshape(1, leaf_count * anc_rows_n)

    accs_anc = [jnp.zeros((leaf_count * anc_rows_n, HD), jnp.float32)] * 2
    accs_own = {leaf: [jnp.zeros((leaf_count, rows_here, HD), jnp.float32)] * 2 for leaf in range(pair_leaves)}
    outputs = {}
    homes = {}
    count = len(chunks)
    for t in range(count):
        leaf, half = chunks[t]
        qg = inputs.pop(t).reshape(leaf_count, group_heads, half_rows, 2 * HD)
        out, dka, dva, dko, dvo = attend_chunk(half, leaf, anc_mask, qg, own_got, anc_got, accs_anc + accs_own[leaf])
        accs_anc = [dka, dva]
        accs_own[leaf] = [dko, dvo]
        outputs[t] = out.reshape(leaf_count, chunk_rows, 2 * HD)
        nxt = t + 1
        parts = []
        if nxt < count:
            parts.append(qg_send[chunks[nxt][0], chunks[nxt][1]])
        if nxt - 2 >= 0:
            parts.append(outputs.pop(nxt - 2))
        if nxt < count:
            got = exchange(jnp.concatenate(parts, axis=1))
            inputs[nxt] = got[:, :chunk_rows]
            if nxt - 2 >= 0:
                homes[nxt - 2] = got[:, chunk_rows:]
        else:
            homes[nxt - 2] = exchange(parts[0])
    logit_scale = 1.0 / math.sqrt(HD)
    own_back = jnp.concatenate(
        [
            jnp.concatenate([accs_own[leaf][0] * logit_scale, accs_own[leaf][1]], axis=2).astype(jnp.bfloat16)
            for leaf in range(pair_leaves)
        ],
        axis=1,
    )
    anc_back = jnp.concatenate([accs_anc[0] * logit_scale, accs_anc[1]], axis=1).astype(jnp.bfloat16)
    anc_back = anc_back.reshape(leaf_count, anc_rows_n, 2 * HD)
    last = exchange(jnp.concatenate([outputs.pop(count - 1), own_back, anc_back], axis=1))
    homes[count - 1] = last[:, :chunk_rows]
    own_home = last[:, chunk_rows : chunk_rows + own_rows_n]
    anc_home = last[:, chunk_rows + own_rows_n :]

    stacked = jnp.stack([homes[t] for t in range(count)], axis=0).reshape(
        pair_leaves, halves, kv_heads, pair_count, group_heads, half_rows, 2, HD
    )

    def to_rows(x):
        return x.transpose(3, 0, 1, 5, 2, 4, 6).reshape(leaf_dev, rows_here, query_width)

    attention = to_rows(stacked[..., 0, :])
    query_grad = to_rows(stacked[..., 1, :])
    own_home = own_home.reshape(kv_heads, pair_count, pair_leaves, rows_here, 2, HD)
    leaf_key_grad = own_home[..., 0, :].transpose(1, 2, 3, 0, 4).reshape(leaf_dev, rows_here, key_width)
    leaf_value_grad = own_home[..., 1, :].transpose(1, 2, 3, 0, 4).reshape(leaf_dev, rows_here, key_width)

    anc_home = anc_home.astype(jnp.float32).reshape(kv_heads, pair_count, levels, rows_here, 2 * HD).sum(axis=1)
    part_keys = anc_home[..., :HD].transpose(1, 2, 0, 3).reshape(levels, rows_here, key_width)
    part_values = anc_home[..., HD:].transpose(1, 2, 0, 3).reshape(levels, rows_here, key_width)
    part_round = jnp.concatenate([part_keys, part_values], axis=2).astype(jnp.bfloat16)

    seg_ids = jnp.arange(seg_count, dtype=jnp.int32)
    homeward_pick = ((my_owners[None, :] == seg_ids[:, None]) & my_alive[None, :]).astype(jnp.bfloat16)
    homeward = jnp.einsum("ok,krc->orc", homeward_pick, part_round, preferred_element_type=jnp.float32).astype(
        jnp.bfloat16
    )
    returned = lax.all_to_all(homeward, "seg", split_axis=0, concat_axis=0, tiled=True)
    collected = jnp.einsum("gs,grc->src", serve_pick, returned, preferred_element_type=jnp.float32).astype(
        jnp.bfloat16
    )
    return (
        attention,
        query_grad,
        leaf_key_grad,
        leaf_value_grad,
        collected[:, :, :key_width],
        collected[:, :, key_width:],
    )


def solution(mesh):
    spec = P("seg", "leaf", None)
    return jax.shard_map(
        on_device,
        mesh=mesh,
        in_specs=(spec, spec, spec, spec, spec, spec, P(), P()),
        out_specs=(spec, spec, spec, spec, spec, spec),
        check_vma=False,
    )
```

```python
import math

import jax
import jax.numpy as jnp
from jax import lax
from jax.experimental import pallas as pl
from jax.experimental.pallas import tpu as pltpu
from jax.sharding import PartitionSpec as P

HD = 128


NEG_FILL = -1e30


def attend_kernel(mask_ref, q_ref, g_ref, ko_ref, vo_ref, ka_ref, va_ref,
                  o_ref, dq_ref, dko_ref, dvo_ref, dka_ref, dva_ref, dko_acc, dvo_acc):
    leaf_i = pl.program_id(0)
    head_i = pl.program_id(1)
    row_i = pl.program_id(2)
    head_count = pl.num_programs(1)
    row_count = pl.num_programs(2)
    block_rows = q_ref.shape[0]
    seg_len = ko_ref.shape[0]
    scale = 1.0 / math.sqrt(q_ref.shape[-1])

    @pl.when((leaf_i == 0) & (head_i == 0) & (row_i == 0))
    def _():
        dka_ref[...] = jnp.zeros_like(dka_ref)
        dva_ref[...] = jnp.zeros_like(dva_ref)

    @pl.when((head_i == 0) & (row_i == 0))
    def _():
        dko_acc[...] = jnp.zeros_like(dko_acc)
        dvo_acc[...] = jnp.zeros_like(dvo_acc)

    nt = (((1,), (1,)), ((), ()))
    tn = (((0,), (0,)), ((), ()))
    q = q_ref[...]
    g = g_ref[...]
    ka = ka_ref[...]
    va = va_ref[...]
    ko = ko_ref[...]
    vo = vo_ref[...]
    s_a = lax.dot_general(q, ka, nt, preferred_element_type=jnp.float32) * scale
    s_o = lax.dot_general(q, ko, nt, preferred_element_type=jnp.float32) * scale
    s_a = jnp.where(mask_ref[...] > 0.5, s_a, NEG_FILL)
    rows = row_i * block_rows + lax.broadcasted_iota(jnp.int32, (block_rows, seg_len), 0)
    cols = lax.broadcasted_iota(jnp.int32, (block_rows, seg_len), 1)
    s_o = jnp.where(cols <= rows, s_o, NEG_FILL)
    m = jnp.maximum(jnp.max(s_a, axis=1, keepdims=True), jnp.max(s_o, axis=1, keepdims=True))
    w_a = jnp.exp(s_a - m)
    w_o = jnp.exp(s_o - m)
    total = jnp.sum(w_a, axis=1, keepdims=True) + jnp.sum(w_o, axis=1, keepdims=True)
    inv = 1.0 / total
    p_a = w_a * inv
    p_o = w_o * inv
    pb_a = p_a.astype(jnp.bfloat16)
    pb_o = p_o.astype(jnp.bfloat16)
    o = jnp.dot(pb_a, va, preferred_element_type=jnp.float32) + jnp.dot(pb_o, vo, preferred_element_type=jnp.float32)
    o_b = o.astype(jnp.bfloat16)
    o_ref[...] = o_b
    delta = jnp.sum(g.astype(jnp.float32) * o_b.astype(jnp.float32), axis=1, keepdims=True)
    dp_a = lax.dot_general(g, va, nt, preferred_element_type=jnp.float32)
    dp_o = lax.dot_general(g, vo, nt, preferred_element_type=jnp.float32)
    ds_a = (p_a * (dp_a - delta)).astype(jnp.bfloat16)
    ds_o = (p_o * (dp_o - delta)).astype(jnp.bfloat16)
    dq = (jnp.dot(ds_a, ka, preferred_element_type=jnp.float32) + jnp.dot(ds_o, ko, preferred_element_type=jnp.float32)) * scale
    dq_ref[...] = dq.astype(jnp.bfloat16)
    dka_ref[...] += lax.dot_general(ds_a, q, tn, preferred_element_type=jnp.float32)
    dva_ref[...] += lax.dot_general(pb_a, g, tn, preferred_element_type=jnp.float32)
    dko_acc[...] += lax.dot_general(ds_o, q, tn, preferred_element_type=jnp.float32)
    dvo_acc[...] += lax.dot_general(pb_o, g, tn, preferred_element_type=jnp.float32)

    @pl.when((head_i == head_count - 1) & (row_i == row_count - 1))
    def _():
        dko_ref[...] = dko_acc[...] * scale
        dvo_ref[...] = dvo_acc[...]

    @pl.when((leaf_i == pl.num_programs(0) - 1) & (head_i == head_count - 1) & (row_i == row_count - 1))
    def _():
        dka_ref[...] = dka_ref[...] * scale


def attend_all(anc_mask, packed, anc_rows, heads, block_rows=256):
    leaves, seg_len, _ = packed.shape
    anc = anc_rows.shape[0]
    grid = (leaves, heads, seg_len // block_rows)
    qspec = pl.BlockSpec((None, block_rows, HD), lambda l, h, r: (l, r, h))
    gspec = pl.BlockSpec((None, block_rows, HD), lambda l, h, r: (l, r, heads + h))
    kospec = pl.BlockSpec((None, seg_len, HD), lambda l, h, r: (l, 0, 2 * heads))
    vospec = pl.BlockSpec((None, seg_len, HD), lambda l, h, r: (l, 0, 2 * heads + 1))
    kaspec = pl.BlockSpec((anc, HD), lambda l, h, r: (0, 0))
    vaspec = pl.BlockSpec((anc, HD), lambda l, h, r: (0, 1))
    maskspec = pl.BlockSpec((1, anc), lambda l, h, r: (0, 0))
    ownspec = pl.BlockSpec((None, seg_len, HD), lambda l, h, r: (l, 0, 0))
    ancspec = pl.BlockSpec((anc, HD), lambda l, h, r: (0, 0))
    out_rows = jax.ShapeDtypeStruct((leaves, seg_len, heads * HD), jnp.bfloat16)
    own_grad = jax.ShapeDtypeStruct((leaves, seg_len, HD), jnp.float32)
    anc_grad = jax.ShapeDtypeStruct((anc, HD), jnp.float32)
    return pl.pallas_call(
        attend_kernel,
        grid=grid,
        in_specs=[maskspec, qspec, gspec, kospec, vospec, kaspec, vaspec],
        out_specs=[qspec, qspec, ownspec, ownspec, ancspec, ancspec],
        out_shape=[out_rows, out_rows, own_grad, own_grad, anc_grad, anc_grad],
        scratch_shapes=[pltpu.VMEM((seg_len, HD), jnp.float32), pltpu.VMEM((seg_len, HD), jnp.float32)],
        compiler_params=pltpu.CompilerParams(dimension_semantics=("arbitrary", "arbitrary", "arbitrary")),
    )(anc_mask, packed, packed, packed, packed, anc_rows, anc_rows)


def seg_shift(blocks, seg_here, seg_count):
    got = [jnp.take(blocks, seg_here, axis=0)]
    for shift in range(1, seg_count):
        piece = jnp.take(blocks, (seg_here + shift) % seg_count, axis=0)
        pairs = [(i, (i + shift) % seg_count) for i in range(seg_count)]
        got.append(lax.ppermute(piece, "seg", pairs))
    return jnp.stack(got, axis=0)


def on_device(queries, leaf_keys, leaf_values, inner_keys, inner_values, out_grad, ancestors, depths):
    seg_count = lax.axis_size("seg")
    leaf_count = lax.axis_size("leaf")
    seg_here = lax.axis_index("seg")
    leaf_here = lax.axis_index("leaf")
    leaf_dev, rows_here, query_width = queries.shape
    slot_count = inner_keys.shape[0]
    key_width = leaf_keys.shape[2]
    kv_heads = key_width // HD
    group_heads = query_width // key_width
    head_width = group_heads * HD
    seg_len = rows_here * leaf_count
    levels = ancestors.shape[1]
    pair_count = leaf_count // kv_heads
    pair_leaves = leaf_dev // pair_count
    my_pair = leaf_here % pair_count

    group_lists = ancestors[::leaf_dev]
    group_depth = depths[::leaf_dev]
    owners = group_lists // slot_count
    slot_of = group_lists % slot_count
    level_ids = jnp.arange(levels, dtype=jnp.int32)
    alive_levels = level_ids[None, :] < group_depth[:, None]
    served = alive_levels & (owners == seg_here)
    slot_ids = jnp.arange(slot_count, dtype=jnp.int32)
    serve_pick = jnp.sum(
        (served[:, :, None] & (slot_of[:, :, None] == slot_ids[None, None, :])).astype(jnp.float32),
        axis=1,
    ).astype(jnp.bfloat16)
    stored = jnp.concatenate([inner_keys, inner_values], axis=2)
    outgoing = jnp.einsum("gs,src->grc", serve_pick, stored, preferred_element_type=jnp.float32).astype(
        jnp.bfloat16
    )
    arrived_by_shift = seg_shift(outgoing, seg_here, seg_count)
    my_owners = jnp.take(owners, seg_here, axis=0)
    my_alive = jnp.take(alive_levels, seg_here, axis=0)
    ancestor_rows = jnp.where(
        my_alive[:, None, None],
        jnp.take(arrived_by_shift, (seg_here - my_owners) % seg_count, axis=0),
        jnp.zeros((), jnp.bfloat16),
    )

    def to_heads(x, width):
        shaped = x.reshape(pair_count, pair_leaves, rows_here, kv_heads, width)
        return shaped.transpose(3, 0, 1, 2, 4).reshape(leaf_count, pair_leaves, rows_here, width)

    packed = jnp.concatenate(
        [to_heads(queries, head_width), to_heads(out_grad, head_width), to_heads(leaf_keys, HD), to_heads(leaf_values, HD)],
        axis=3,
    )
    anc_k = ancestor_rows[:, :, :key_width].reshape(levels, rows_here, kv_heads, HD)
    anc_v = ancestor_rows[:, :, key_width:].reshape(levels, rows_here, kv_heads, HD)
    anc_heads = jnp.concatenate([anc_k, anc_v], axis=3).transpose(2, 0, 1, 3)
    anc_send = jnp.broadcast_to(anc_heads[:, None], (kv_heads, pair_count) + anc_heads.shape[1:]).reshape(
        (leaf_count,) + anc_heads.shape[1:]
    )
    anc_got = lax.all_to_all(anc_send, "leaf", split_axis=0, concat_axis=0, tiled=True)
    anc_got = anc_got.transpose(1, 0, 2, 3).reshape(levels * seg_len, 2 * HD)
    anc_mask = jnp.repeat(my_alive, seg_len).astype(jnp.float32)[None, :]

    homes = []
    anc_partial = None
    for chunk in range(pair_leaves):
        got = lax.all_to_all(packed[:, chunk], "leaf", split_axis=0, concat_axis=0, tiled=True)
        got = got.reshape(1, seg_len, packed.shape[3])
        res, dq, dko, dvo, dka, dva = attend_all(anc_mask, got, anc_got, group_heads)
        part = jnp.concatenate([dka, dva], axis=1)
        anc_partial = part if anc_partial is None else anc_partial + part
        back = jnp.concatenate([res, dq, dko.astype(jnp.bfloat16), dvo.astype(jnp.bfloat16)], axis=2)
        back = back.reshape(leaf_count, rows_here, back.shape[2])
        homes.append(lax.all_to_all(back, "leaf", split_axis=0, concat_axis=0, tiled=True))
    home = jnp.stack(homes, axis=1)
    home = home.reshape(kv_heads, pair_count, pair_leaves, rows_here, home.shape[3])

    def to_rows(x):
        width = x.shape[-1]
        return x.transpose(1, 2, 3, 0, 4).reshape(leaf_dev, rows_here, kv_heads * width)

    attention = to_rows(home[..., :head_width])
    query_grad = to_rows(home[..., head_width : 2 * head_width])
    leaf_key_grad = to_rows(home[..., 2 * head_width : 2 * head_width + HD])
    leaf_value_grad = to_rows(home[..., 2 * head_width + HD :])

    anc_back = anc_partial.astype(jnp.bfloat16).reshape(levels, leaf_count, rows_here, 2 * HD).transpose(1, 0, 2, 3)
    anc_home = lax.all_to_all(anc_back, "leaf", split_axis=0, concat_axis=0, tiled=True)
    anc_home = anc_home.astype(jnp.float32).reshape(kv_heads, pair_count, levels, rows_here, 2 * HD).sum(axis=1)
    part_keys = anc_home[..., :HD].transpose(1, 2, 0, 3).reshape(levels, rows_here, key_width)
    part_values = anc_home[..., HD:].transpose(1, 2, 0, 3).reshape(levels, rows_here, key_width)
    part_round = jnp.concatenate([part_keys, part_values], axis=2).astype(jnp.bfloat16)

    seg_ids = jnp.arange(seg_count, dtype=jnp.int32)
    homeward_pick = ((my_owners[None, :] == seg_ids[:, None]) & my_alive[None, :]).astype(jnp.bfloat16)
    homeward = jnp.einsum("ok,krc->orc", homeward_pick, part_round, preferred_element_type=jnp.float32).astype(
        jnp.bfloat16
    )
    returned_by_shift = seg_shift(homeward, seg_here, seg_count)
    returned = jnp.take(returned_by_shift, (seg_here - seg_ids) % seg_count, axis=0)
    collected = jnp.einsum("gs,grc->src", serve_pick, returned, preferred_element_type=jnp.float32).astype(
        jnp.bfloat16
    )
    return (
        attention,
        query_grad,
        leaf_key_grad,
        leaf_value_grad,
        collected[:, :, :key_width],
        collected[:, :, key_width:],
    )


def solution(mesh):
    spec = P("seg", "leaf", None)
    return jax.shard_map(
        on_device,
        mesh=mesh,
        in_specs=(spec, spec, spec, spec, spec, spec, P(), P()),
        out_specs=(spec, spec, spec, spec, spec, spec),
        check_vma=False,
    )
```

```python
import math

import jax
import jax.numpy as jnp
from jax import lax
from jax.experimental import pallas as pl
from jax.experimental.pallas import tpu as pltpu
from jax.sharding import PartitionSpec as P

HD = 128


NEG_FILL = -1e30


def attend_kernel(mask_ref, q_ref, g_ref, ko_ref, vo_ref, ka_ref, va_ref,
                  o_ref, dq_ref, dko_ref, dvo_ref, dka_ref, dva_ref, dko_acc, dvo_acc):
    leaf_i = pl.program_id(0)
    head_i = pl.program_id(1)
    row_i = pl.program_id(2)
    head_count = pl.num_programs(1)
    row_count = pl.num_programs(2)
    block_rows = q_ref.shape[0]
    seg_len = ko_ref.shape[0]
    scale = 1.0 / math.sqrt(q_ref.shape[-1])

    @pl.when((leaf_i == 0) & (head_i == 0) & (row_i == 0))
    def _():
        dka_ref[...] = jnp.zeros_like(dka_ref)
        dva_ref[...] = jnp.zeros_like(dva_ref)

    @pl.when((head_i == 0) & (row_i == 0))
    def _():
        dko_acc[...] = jnp.zeros_like(dko_acc)
        dvo_acc[...] = jnp.zeros_like(dvo_acc)

    nt = (((1,), (1,)), ((), ()))
    tn = (((0,), (0,)), ((), ()))
    q = q_ref[...]
    g = g_ref[...]
    ka = ka_ref[...]
    va = va_ref[...]
    ko = ko_ref[...]
    vo = vo_ref[...]
    s_a = lax.dot_general(q, ka, nt, preferred_element_type=jnp.float32) * scale
    s_o = lax.dot_general(q, ko, nt, preferred_element_type=jnp.float32) * scale
    s_a = jnp.where(mask_ref[...] > 0.5, s_a, NEG_FILL)
    rows = row_i * block_rows + lax.broadcasted_iota(jnp.int32, (block_rows, seg_len), 0)
    cols = lax.broadcasted_iota(jnp.int32, (block_rows, seg_len), 1)
    s_o = jnp.where(cols <= rows, s_o, NEG_FILL)
    m = jnp.maximum(jnp.max(s_a, axis=1, keepdims=True), jnp.max(s_o, axis=1, keepdims=True))
    w_a = jnp.exp(s_a - m)
    w_o = jnp.exp(s_o - m)
    total = jnp.sum(w_a, axis=1, keepdims=True) + jnp.sum(w_o, axis=1, keepdims=True)
    inv = 1.0 / total
    p_a = w_a * inv
    p_o = w_o * inv
    pb_a = p_a.astype(jnp.bfloat16)
    pb_o = p_o.astype(jnp.bfloat16)
    o = jnp.dot(pb_a, va, preferred_element_type=jnp.float32) + jnp.dot(pb_o, vo, preferred_element_type=jnp.float32)
    o_b = o.astype(jnp.bfloat16)
    o_ref[...] = o_b
    delta = jnp.sum(g.astype(jnp.float32) * o_b.astype(jnp.float32), axis=1, keepdims=True)
    dp_a = lax.dot_general(g, va, nt, preferred_element_type=jnp.float32)
    dp_o = lax.dot_general(g, vo, nt, preferred_element_type=jnp.float32)
    ds_a = (p_a * (dp_a - delta)).astype(jnp.bfloat16)
    ds_o = (p_o * (dp_o - delta)).astype(jnp.bfloat16)
    dq = (jnp.dot(ds_a, ka, preferred_element_type=jnp.float32) + jnp.dot(ds_o, ko, preferred_element_type=jnp.float32)) * scale
    dq_ref[...] = dq.astype(jnp.bfloat16)
    dka_ref[...] += lax.dot_general(ds_a, q, tn, preferred_element_type=jnp.float32)
    dva_ref[...] += lax.dot_general(pb_a, g, tn, preferred_element_type=jnp.float32)
    dko_acc[...] += lax.dot_general(ds_o, q, tn, preferred_element_type=jnp.float32)
    dvo_acc[...] += lax.dot_general(pb_o, g, tn, preferred_element_type=jnp.float32)

    @pl.when((head_i == head_count - 1) & (row_i == row_count - 1))
    def _():
        dko_ref[...] = dko_acc[...] * scale
        dvo_ref[...] = dvo_acc[...]

    @pl.when((leaf_i == pl.num_programs(0) - 1) & (head_i == head_count - 1) & (row_i == row_count - 1))
    def _():
        dka_ref[...] = dka_ref[...] * scale


def attend_all(anc_mask, packed, anc_rows, heads, block_rows=512):
    leaves, seg_len, _ = packed.shape
    anc = anc_rows.shape[0]
    grid = (leaves, heads, seg_len // block_rows)
    qspec = pl.BlockSpec((None, block_rows, HD), lambda l, h, r: (l, r, h))
    gspec = pl.BlockSpec((None, block_rows, HD), lambda l, h, r: (l, r, heads + h))
    kospec = pl.BlockSpec((None, seg_len, HD), lambda l, h, r: (l, 0, 2 * heads))
    vospec = pl.BlockSpec((None, seg_len, HD), lambda l, h, r: (l, 0, 2 * heads + 1))
    kaspec = pl.BlockSpec((anc, HD), lambda l, h, r: (0, 0))
    vaspec = pl.BlockSpec((anc, HD), lambda l, h, r: (0, 1))
    maskspec = pl.BlockSpec((1, anc), lambda l, h, r: (0, 0))
    ownspec = pl.BlockSpec((None, seg_len, HD), lambda l, h, r: (l, 0, 0))
    ancspec = pl.BlockSpec((anc, HD), lambda l, h, r: (0, 0))
    out_rows = jax.ShapeDtypeStruct((leaves, seg_len, heads * HD), jnp.bfloat16)
    own_grad = jax.ShapeDtypeStruct((leaves, seg_len, HD), jnp.float32)
    anc_grad = jax.ShapeDtypeStruct((anc, HD), jnp.float32)
    return pl.pallas_call(
        attend_kernel,
        grid=grid,
        in_specs=[maskspec, qspec, gspec, kospec, vospec, kaspec, vaspec],
        out_specs=[qspec, qspec, ownspec, ownspec, ancspec, ancspec],
        out_shape=[out_rows, out_rows, own_grad, own_grad, anc_grad, anc_grad],
        scratch_shapes=[pltpu.VMEM((seg_len, HD), jnp.float32), pltpu.VMEM((seg_len, HD), jnp.float32)],
        compiler_params=pltpu.CompilerParams(dimension_semantics=("arbitrary", "arbitrary", "arbitrary")),
    )(anc_mask, packed, packed, packed, packed, anc_rows, anc_rows)


def on_device(queries, leaf_keys, leaf_values, inner_keys, inner_values, out_grad, ancestors, depths):
    seg_count = lax.axis_size("seg")
    leaf_count = lax.axis_size("leaf")
    seg_here = lax.axis_index("seg")
    leaf_here = lax.axis_index("leaf")
    leaf_dev, rows_here, query_width = queries.shape
    slot_count = inner_keys.shape[0]
    key_width = leaf_keys.shape[2]
    kv_heads = key_width // HD
    group_heads = query_width // key_width
    head_width = group_heads * HD
    seg_len = rows_here * leaf_count
    levels = ancestors.shape[1]
    pair_count = leaf_count // kv_heads
    pair_leaves = leaf_dev // pair_count
    my_pair = leaf_here % pair_count

    group_lists = ancestors[::leaf_dev]
    group_depth = depths[::leaf_dev]
    owners = group_lists // slot_count
    slot_of = group_lists % slot_count
    level_ids = jnp.arange(levels, dtype=jnp.int32)
    alive_levels = level_ids[None, :] < group_depth[:, None]
    served = alive_levels & (owners == seg_here)
    slot_ids = jnp.arange(slot_count, dtype=jnp.int32)
    serve_pick = jnp.sum(
        (served[:, :, None] & (slot_of[:, :, None] == slot_ids[None, None, :])).astype(jnp.float32),
        axis=1,
    ).astype(jnp.bfloat16)
    stored = jnp.concatenate([inner_keys, inner_values], axis=2)
    outgoing = jnp.einsum("gs,src->grc", serve_pick, stored, preferred_element_type=jnp.float32).astype(
        jnp.bfloat16
    )
    arrived = lax.all_to_all(outgoing, "seg", split_axis=0, concat_axis=0, tiled=True)
    my_owners = jnp.take(owners, seg_here, axis=0)
    my_alive = jnp.take(alive_levels, seg_here, axis=0)
    ancestor_rows = jnp.where(
        my_alive[:, None, None], jnp.take(arrived, my_owners, axis=0), jnp.zeros((), jnp.bfloat16)
    )

    def to_heads(x, width):
        shaped = x.reshape(pair_count, pair_leaves, rows_here, kv_heads, width)
        return shaped.transpose(3, 0, 1, 2, 4).reshape(leaf_count, pair_leaves, rows_here, width)

    packed = jnp.concatenate(
        [to_heads(queries, head_width), to_heads(out_grad, head_width), to_heads(leaf_keys, HD), to_heads(leaf_values, HD)],
        axis=3,
    )
    anc_k = ancestor_rows[:, :, :key_width].reshape(levels, rows_here, kv_heads, HD)
    anc_v = ancestor_rows[:, :, key_width:].reshape(levels, rows_here, kv_heads, HD)
    anc_heads = jnp.concatenate([anc_k, anc_v], axis=3).transpose(2, 0, 1, 3)
    anc_send = jnp.broadcast_to(anc_heads[:, None], (kv_heads, pair_count) + anc_heads.shape[1:]).reshape(
        (leaf_count,) + anc_heads.shape[1:]
    )
    anc_got = lax.all_to_all(anc_send, "leaf", split_axis=0, concat_axis=0, tiled=True)
    anc_got = anc_got.transpose(1, 0, 2, 3).reshape(levels * seg_len, 2 * HD)
    anc_mask = jnp.repeat(my_alive, seg_len).astype(jnp.float32)[None, :]

    homes = []
    anc_partial = None
    for chunk in range(pair_leaves):
        got = lax.all_to_all(packed[:, chunk], "leaf", split_axis=0, concat_axis=0, tiled=True)
        got = got.reshape(1, seg_len, packed.shape[3])
        res, dq, dko, dvo, dka, dva = attend_all(anc_mask, got, anc_got, group_heads)
        part = jnp.concatenate([dka, dva], axis=1)
        anc_partial = part if anc_partial is None else anc_partial + part
        back = jnp.concatenate([res, dq, dko.astype(jnp.bfloat16), dvo.astype(jnp.bfloat16)], axis=2)
        back = back.reshape(leaf_count, rows_here, back.shape[2])
        if chunk < pair_leaves - 1:
            homes.append(lax.all_to_all(back, "leaf", split_axis=0, concat_axis=0, tiled=True))
    width = back.shape[2]
    anc_back = anc_partial.astype(jnp.bfloat16).reshape(levels, leaf_count, rows_here, 2 * HD).transpose(1, 2, 0, 3)
    tail = lax.all_to_all(
        jnp.concatenate([back, anc_back.reshape(leaf_count, rows_here, levels * 2 * HD)], axis=2),
        "leaf",
        split_axis=0,
        concat_axis=0,
        tiled=True,
    )
    homes.append(tail[..., :width])
    anc_home = tail[..., width:].reshape(leaf_count, rows_here, levels, 2 * HD).transpose(0, 2, 1, 3)
    home = jnp.stack(homes, axis=1)
    home = home.reshape(kv_heads, pair_count, pair_leaves, rows_here, home.shape[3])

    def to_rows(x):
        width = x.shape[-1]
        return x.transpose(1, 2, 3, 0, 4).reshape(leaf_dev, rows_here, kv_heads * width)

    attention = to_rows(home[..., :head_width])
    query_grad = to_rows(home[..., head_width : 2 * head_width])
    leaf_key_grad = to_rows(home[..., 2 * head_width : 2 * head_width + HD])
    leaf_value_grad = to_rows(home[..., 2 * head_width + HD :])

    anc_home = anc_home.astype(jnp.float32).reshape(kv_heads, pair_count, levels, rows_here, 2 * HD).sum(axis=1)
    part_keys = anc_home[..., :HD].transpose(1, 2, 0, 3).reshape(levels, rows_here, key_width)
    part_values = anc_home[..., HD:].transpose(1, 2, 0, 3).reshape(levels, rows_here, key_width)
    part_round = jnp.concatenate([part_keys, part_values], axis=2).astype(jnp.bfloat16)

    seg_ids = jnp.arange(seg_count, dtype=jnp.int32)
    homeward_pick = ((my_owners[None, :] == seg_ids[:, None]) & my_alive[None, :]).astype(jnp.bfloat16)
    homeward = jnp.einsum("ok,krc->orc", homeward_pick, part_round, preferred_element_type=jnp.float32).astype(
        jnp.bfloat16
    )
    returned = lax.all_to_all(homeward, "seg", split_axis=0, concat_axis=0, tiled=True)
    collected = jnp.einsum("gs,grc->src", serve_pick, returned, preferred_element_type=jnp.float32).astype(
        jnp.bfloat16
    )
    return (
        attention,
        query_grad,
        leaf_key_grad,
        leaf_value_grad,
        collected[:, :, :key_width],
        collected[:, :, key_width:],
    )


def solution(mesh):
    spec = P("seg", "leaf", None)
    return jax.shard_map(
        on_device,
        mesh=mesh,
        in_specs=(spec, spec, spec, spec, spec, spec, P(), P()),
        out_specs=(spec, spec, spec, spec, spec, spec),
        check_vma=False,
    )
```

```python
import math

import jax
import jax.numpy as jnp
from jax import lax
from jax.experimental import pallas as pl
from jax.experimental.pallas import tpu as pltpu
from jax.sharding import PartitionSpec as P

HD = 128


NEG_FILL = -1e30


def attend_kernel(mask_ref, q_ref, g_ref, ko_ref, vo_ref, ka_ref, va_ref,
                  o_ref, dq_ref, dko_ref, dvo_ref, dka_ref, dva_ref, dko_acc, dvo_acc):
    leaf_i = pl.program_id(0)
    head_i = pl.program_id(1)
    row_i = pl.program_id(2)
    head_count = pl.num_programs(1)
    row_count = pl.num_programs(2)
    block_rows = q_ref.shape[0]
    seg_len = ko_ref.shape[0]
    scale = 1.0 / math.sqrt(q_ref.shape[-1])

    @pl.when((leaf_i == 0) & (head_i == 0) & (row_i == 0))
    def _():
        dka_ref[...] = jnp.zeros_like(dka_ref)
        dva_ref[...] = jnp.zeros_like(dva_ref)

    @pl.when((head_i == 0) & (row_i == 0))
    def _():
        dko_acc[...] = jnp.zeros_like(dko_acc)
        dvo_acc[...] = jnp.zeros_like(dvo_acc)

    nt = (((1,), (1,)), ((), ()))
    tn = (((0,), (0,)), ((), ()))
    q = q_ref[...]
    g = g_ref[...]
    ka = ka_ref[...]
    va = va_ref[...]
    ko = ko_ref[...]
    vo = vo_ref[...]
    s_a = lax.dot_general(q, ka, nt, preferred_element_type=jnp.float32) * scale
    s_o = lax.dot_general(q, ko, nt, preferred_element_type=jnp.float32) * scale
    s_a = jnp.where(mask_ref[...] > 0.5, s_a, NEG_FILL)
    rows = row_i * block_rows + lax.broadcasted_iota(jnp.int32, (block_rows, seg_len), 0)
    cols = lax.broadcasted_iota(jnp.int32, (block_rows, seg_len), 1)
    s_o = jnp.where(cols <= rows, s_o, NEG_FILL)
    m = jnp.maximum(jnp.max(s_a, axis=1, keepdims=True), jnp.max(s_o, axis=1, keepdims=True))
    w_a = jnp.exp(s_a - m)
    w_o = jnp.exp(s_o - m)
    total = jnp.sum(w_a, axis=1, keepdims=True) + jnp.sum(w_o, axis=1, keepdims=True)
    inv = 1.0 / total
    p_a = w_a * inv
    p_o = w_o * inv
    pb_a = p_a.astype(jnp.bfloat16)
    pb_o = p_o.astype(jnp.bfloat16)
    o = jnp.dot(pb_a, va, preferred_element_type=jnp.float32) + jnp.dot(pb_o, vo, preferred_element_type=jnp.float32)
    o_b = o.astype(jnp.bfloat16)
    o_ref[...] = o_b
    delta = jnp.sum(g.astype(jnp.float32) * o_b.astype(jnp.float32), axis=1, keepdims=True)
    dp_a = lax.dot_general(g, va, nt, preferred_element_type=jnp.float32)
    dp_o = lax.dot_general(g, vo, nt, preferred_element_type=jnp.float32)
    ds_a = (p_a * (dp_a - delta)).astype(jnp.bfloat16)
    ds_o = (p_o * (dp_o - delta)).astype(jnp.bfloat16)
    dq = (jnp.dot(ds_a, ka, preferred_element_type=jnp.float32) + jnp.dot(ds_o, ko, preferred_element_type=jnp.float32)) * scale
    dq_ref[...] = dq.astype(jnp.bfloat16)
    dka_ref[...] += lax.dot_general(ds_a, q, tn, preferred_element_type=jnp.float32)
    dva_ref[...] += lax.dot_general(pb_a, g, tn, preferred_element_type=jnp.float32)
    dko_acc[...] += lax.dot_general(ds_o, q, tn, preferred_element_type=jnp.float32)
    dvo_acc[...] += lax.dot_general(pb_o, g, tn, preferred_element_type=jnp.float32)

    @pl.when((head_i == head_count - 1) & (row_i == row_count - 1))
    def _():
        dko_ref[...] = dko_acc[...] * scale
        dvo_ref[...] = dvo_acc[...]

    @pl.when((leaf_i == pl.num_programs(0) - 1) & (head_i == head_count - 1) & (row_i == row_count - 1))
    def _():
        dka_ref[...] = dka_ref[...] * scale


def attend_all(anc_mask, packed, anc_rows, heads, block_rows=512):
    leaves, seg_len, _ = packed.shape
    anc = anc_rows.shape[0]
    grid = (leaves, heads, seg_len // block_rows)
    qspec = pl.BlockSpec((None, block_rows, HD), lambda l, h, r: (l, r, h))
    gspec = pl.BlockSpec((None, block_rows, HD), lambda l, h, r: (l, r, heads + h))
    kospec = pl.BlockSpec((None, seg_len, HD), lambda l, h, r: (l, 0, 2 * heads))
    vospec = pl.BlockSpec((None, seg_len, HD), lambda l, h, r: (l, 0, 2 * heads + 1))
    kaspec = pl.BlockSpec((anc, HD), lambda l, h, r: (0, 0))
    vaspec = pl.BlockSpec((anc, HD), lambda l, h, r: (0, 1))
    maskspec = pl.BlockSpec((1, anc), lambda l, h, r: (0, 0))
    ownspec = pl.BlockSpec((None, seg_len, HD), lambda l, h, r: (l, 0, 0))
    ancspec = pl.BlockSpec((anc, HD), lambda l, h, r: (0, 0))
    out_rows = jax.ShapeDtypeStruct((leaves, seg_len, heads * HD), jnp.bfloat16)
    own_grad = jax.ShapeDtypeStruct((leaves, seg_len, HD), jnp.float32)
    anc_grad = jax.ShapeDtypeStruct((anc, HD), jnp.float32)
    return pl.pallas_call(
        attend_kernel,
        grid=grid,
        in_specs=[maskspec, qspec, gspec, kospec, vospec, kaspec, vaspec],
        out_specs=[qspec, qspec, ownspec, ownspec, ancspec, ancspec],
        out_shape=[out_rows, out_rows, own_grad, own_grad, anc_grad, anc_grad],
        scratch_shapes=[pltpu.VMEM((seg_len, HD), jnp.float32), pltpu.VMEM((seg_len, HD), jnp.float32)],
        compiler_params=pltpu.CompilerParams(dimension_semantics=("arbitrary", "arbitrary", "arbitrary")),
    )(anc_mask, packed, packed, packed, packed, anc_rows, anc_rows)


def on_device(queries, leaf_keys, leaf_values, inner_keys, inner_values, out_grad, ancestors, depths):
    seg_count = lax.axis_size("seg")
    leaf_count = lax.axis_size("leaf")
    seg_here = lax.axis_index("seg")
    leaf_here = lax.axis_index("leaf")
    leaf_dev, rows_here, query_width = queries.shape
    slot_count = inner_keys.shape[0]
    key_width = leaf_keys.shape[2]
    kv_heads = key_width // HD
    group_heads = query_width // key_width
    head_width = group_heads * HD
    seg_len = rows_here * leaf_count
    levels = ancestors.shape[1]
    pair_count = leaf_count // kv_heads
    pair_leaves = leaf_dev // pair_count
    my_pair = leaf_here % pair_count

    group_lists = ancestors[::leaf_dev]
    group_depth = depths[::leaf_dev]
    owners = group_lists // slot_count
    slot_of = group_lists % slot_count
    level_ids = jnp.arange(levels, dtype=jnp.int32)
    alive_levels = level_ids[None, :] < group_depth[:, None]
    served = alive_levels & (owners == seg_here)
    slot_ids = jnp.arange(slot_count, dtype=jnp.int32)
    serve_pick = jnp.sum(
        (served[:, :, None] & (slot_of[:, :, None] == slot_ids[None, None, :])).astype(jnp.float32),
        axis=1,
    ).astype(jnp.bfloat16)
    stored = jnp.concatenate([inner_keys, inner_values], axis=2)
    outgoing = jnp.einsum("gs,src->grc", serve_pick, stored, preferred_element_type=jnp.float32).astype(
        jnp.bfloat16
    )
    arrived = lax.all_to_all(outgoing, "seg", split_axis=0, concat_axis=0, tiled=True)
    my_owners = jnp.take(owners, seg_here, axis=0)
    my_alive = jnp.take(alive_levels, seg_here, axis=0)
    ancestor_rows = jnp.where(
        my_alive[:, None, None], jnp.take(arrived, my_owners, axis=0), jnp.zeros((), jnp.bfloat16)
    )

    def to_heads(x, width):
        shaped = x.reshape(pair_count, pair_leaves, rows_here, kv_heads, width)
        return shaped.transpose(3, 0, 1, 2, 4).reshape(leaf_count, pair_leaves, rows_here, width)

    anc_k = ancestor_rows[:, :, :key_width].reshape(levels, rows_here, kv_heads, HD)
    anc_v = ancestor_rows[:, :, key_width:].reshape(levels, rows_here, kv_heads, HD)
    anc_heads = jnp.concatenate([anc_k, anc_v], axis=3).transpose(2, 0, 1, 3)
    anc_send = jnp.broadcast_to(anc_heads[:, None], (kv_heads, pair_count) + anc_heads.shape[1:]).reshape(
        (leaf_count,) + anc_heads.shape[1:]
    )
    anc_cols = anc_send.transpose(0, 2, 1, 3).reshape(leaf_count, rows_here, levels * 2 * HD)
    anc_mask = jnp.repeat(my_alive, seg_len).astype(jnp.float32)[None, :]

    packed = jnp.concatenate(
        [to_heads(queries, head_width), to_heads(out_grad, head_width), to_heads(leaf_keys, HD), to_heads(leaf_values, HD)],
        axis=3,
    )
    homes = []
    anc_partial = None
    for chunk in range(pair_leaves):
        if chunk == 0:
            first = lax.all_to_all(
                jnp.concatenate([packed[:, 0], anc_cols], axis=2), "leaf", split_axis=0, concat_axis=0, tiled=True
            )
            got = first[..., : packed.shape[3]]
            anc_got = first[..., packed.shape[3] :].reshape(leaf_count, rows_here, levels, 2 * HD)
            anc_got = anc_got.transpose(2, 0, 1, 3).reshape(levels * seg_len, 2 * HD)
        else:
            got = lax.all_to_all(packed[:, chunk], "leaf", split_axis=0, concat_axis=0, tiled=True)
        got = got.reshape(1, seg_len, packed.shape[3])
        res, dq, dko, dvo, dka, dva = attend_all(anc_mask, got, anc_got, group_heads)
        part = jnp.concatenate([dka, dva], axis=1)
        anc_partial = part if anc_partial is None else anc_partial + part
        back = jnp.concatenate([res, dq, dko.astype(jnp.bfloat16), dvo.astype(jnp.bfloat16)], axis=2)
        back = back.reshape(leaf_count, rows_here, back.shape[2])
        if chunk < pair_leaves - 1:
            homes.append(lax.all_to_all(back, "leaf", split_axis=0, concat_axis=0, tiled=True))
    width = back.shape[2]
    anc_back = anc_partial.astype(jnp.bfloat16).reshape(levels, leaf_count, rows_here, 2 * HD).transpose(1, 2, 0, 3)
    tail = lax.all_to_all(
        jnp.concatenate([back, anc_back.reshape(leaf_count, rows_here, levels * 2 * HD)], axis=2),
        "leaf",
        split_axis=0,
        concat_axis=0,
        tiled=True,
    )
    homes.append(tail[..., :width])
    anc_home = tail[..., width:].reshape(leaf_count, rows_here, levels, 2 * HD).transpose(0, 2, 1, 3)
    home = jnp.stack(homes, axis=1)
    home = home.reshape(kv_heads, pair_count, pair_leaves, rows_here, home.shape[3])

    def to_rows(x):
        width = x.shape[-1]
        return x.transpose(1, 2, 3, 0, 4).reshape(leaf_dev, rows_here, kv_heads * width)

    attention = to_rows(home[..., :head_width])
    query_grad = to_rows(home[..., head_width : 2 * head_width])
    leaf_key_grad = to_rows(home[..., 2 * head_width : 2 * head_width + HD])
    leaf_value_grad = to_rows(home[..., 2 * head_width + HD :])

    anc_home = anc_home.astype(jnp.float32).reshape(kv_heads, pair_count, levels, rows_here, 2 * HD).sum(axis=1)
    part_keys = anc_home[..., :HD].transpose(1, 2, 0, 3).reshape(levels, rows_here, key_width)
    part_values = anc_home[..., HD:].transpose(1, 2, 0, 3).reshape(levels, rows_here, key_width)
    part_round = jnp.concatenate([part_keys, part_values], axis=2).astype(jnp.bfloat16)

    seg_ids = jnp.arange(seg_count, dtype=jnp.int32)
    homeward_pick = ((my_owners[None, :] == seg_ids[:, None]) & my_alive[None, :]).astype(jnp.bfloat16)
    homeward = jnp.einsum("ok,krc->orc", homeward_pick, part_round, preferred_element_type=jnp.float32).astype(
        jnp.bfloat16
    )
    returned = lax.all_to_all(homeward, "seg", split_axis=0, concat_axis=0, tiled=True)
    collected = jnp.einsum("gs,grc->src", serve_pick, returned, preferred_element_type=jnp.float32).astype(
        jnp.bfloat16
    )
    return (
        attention,
        query_grad,
        leaf_key_grad,
        leaf_value_grad,
        collected[:, :, :key_width],
        collected[:, :, key_width:],
    )


def solution(mesh):
    spec = P("seg", "leaf", None)
    return jax.shard_map(
        on_device,
        mesh=mesh,
        in_specs=(spec, spec, spec, spec, spec, spec, P(), P()),
        out_specs=(spec, spec, spec, spec, spec, spec),
        check_vma=False,
    )
```

```python
import math

import jax
import jax.numpy as jnp
from jax import lax
from jax.experimental import pallas as pl
from jax.experimental.pallas import tpu as pltpu
from jax.sharding import PartitionSpec as P

HD = 128


NEG_FILL = -1e30


def attend_kernel(mask_ref, q_ref, g_ref, ko_ref, vo_ref, ka_ref, va_ref,
                  o_ref, dq_ref, dko_ref, dvo_ref, dka_ref, dva_ref, dko_acc, dvo_acc):
    leaf_i = pl.program_id(0)
    head_i = pl.program_id(1)
    row_i = pl.program_id(2)
    head_count = pl.num_programs(1)
    row_count = pl.num_programs(2)
    block_rows = q_ref.shape[0]
    seg_len = ko_ref.shape[0]
    scale = 1.0 / math.sqrt(q_ref.shape[-1])

    @pl.when((leaf_i == 0) & (head_i == 0) & (row_i == 0))
    def _():
        dka_ref[...] = jnp.zeros_like(dka_ref)
        dva_ref[...] = jnp.zeros_like(dva_ref)

    @pl.when((head_i == 0) & (row_i == 0))
    def _():
        dko_acc[...] = jnp.zeros_like(dko_acc)
        dvo_acc[...] = jnp.zeros_like(dvo_acc)

    nt = (((1,), (1,)), ((), ()))
    tn = (((0,), (0,)), ((), ()))
    q = q_ref[...]
    g = g_ref[...]
    ka = ka_ref[...]
    va = va_ref[...]
    ko = ko_ref[...]
    vo = vo_ref[...]
    s_a = lax.dot_general(q, ka, nt, preferred_element_type=jnp.float32) * scale
    s_o = lax.dot_general(q, ko, nt, preferred_element_type=jnp.float32) * scale
    s_a = jnp.where(mask_ref[...] > 0.5, s_a, NEG_FILL)
    rows = row_i * block_rows + lax.broadcasted_iota(jnp.int32, (block_rows, seg_len), 0)
    cols = lax.broadcasted_iota(jnp.int32, (block_rows, seg_len), 1)
    s_o = jnp.where(cols <= rows, s_o, NEG_FILL)
    m = jnp.maximum(jnp.max(s_a, axis=1, keepdims=True), jnp.max(s_o, axis=1, keepdims=True))
    w_a = jnp.exp(s_a - m)
    w_o = jnp.exp(s_o - m)
    total = jnp.sum(w_a, axis=1, keepdims=True) + jnp.sum(w_o, axis=1, keepdims=True)
    inv = 1.0 / total
    p_a = w_a * inv
    p_o = w_o * inv
    pb_a = p_a.astype(jnp.bfloat16)
    pb_o = p_o.astype(jnp.bfloat16)
    o = jnp.dot(pb_a, va, preferred_element_type=jnp.float32) + jnp.dot(pb_o, vo, preferred_element_type=jnp.float32)
    o_b = o.astype(jnp.bfloat16)
    o_ref[...] = o_b
    delta = jnp.sum(g.astype(jnp.float32) * o_b.astype(jnp.float32), axis=1, keepdims=True)
    dp_a = lax.dot_general(g, va, nt, preferred_element_type=jnp.float32)
    dp_o = lax.dot_general(g, vo, nt, preferred_element_type=jnp.float32)
    ds_a = (p_a * (dp_a - delta)).astype(jnp.bfloat16)
    ds_o = (p_o * (dp_o - delta)).astype(jnp.bfloat16)
    dq = (jnp.dot(ds_a, ka, preferred_element_type=jnp.float32) + jnp.dot(ds_o, ko, preferred_element_type=jnp.float32)) * scale
    dq_ref[...] = dq.astype(jnp.bfloat16)
    dka_ref[...] += lax.dot_general(ds_a, q, tn, preferred_element_type=jnp.float32)
    dva_ref[...] += lax.dot_general(pb_a, g, tn, preferred_element_type=jnp.float32)
    dko_acc[...] += lax.dot_general(ds_o, q, tn, preferred_element_type=jnp.float32)
    dvo_acc[...] += lax.dot_general(pb_o, g, tn, preferred_element_type=jnp.float32)

    @pl.when((head_i == head_count - 1) & (row_i == row_count - 1))
    def _():
        dko_ref[...] = dko_acc[...] * scale
        dvo_ref[...] = dvo_acc[...]

    @pl.when((leaf_i == pl.num_programs(0) - 1) & (head_i == head_count - 1) & (row_i == row_count - 1))
    def _():
        dka_ref[...] = dka_ref[...] * scale


def attend_all(anc_mask, packed, anc_rows, heads, block_rows=512):
    leaves, seg_len, _ = packed.shape
    anc = anc_rows.shape[0]
    grid = (leaves, heads, seg_len // block_rows)
    qspec = pl.BlockSpec((None, block_rows, HD), lambda l, h, r: (l, r, h))
    gspec = pl.BlockSpec((None, block_rows, HD), lambda l, h, r: (l, r, heads + h))
    kospec = pl.BlockSpec((None, seg_len, HD), lambda l, h, r: (l, 0, 2 * heads))
    vospec = pl.BlockSpec((None, seg_len, HD), lambda l, h, r: (l, 0, 2 * heads + 1))
    kaspec = pl.BlockSpec((anc, HD), lambda l, h, r: (0, 0))
    vaspec = pl.BlockSpec((anc, HD), lambda l, h, r: (0, 1))
    maskspec = pl.BlockSpec((1, anc), lambda l, h, r: (0, 0))
    ownspec = pl.BlockSpec((None, seg_len, HD), lambda l, h, r: (l, 0, 0))
    ancspec = pl.BlockSpec((anc, HD), lambda l, h, r: (0, 0))
    out_rows = jax.ShapeDtypeStruct((leaves, seg_len, heads * HD), jnp.bfloat16)
    own_grad = jax.ShapeDtypeStruct((leaves, seg_len, HD), jnp.float32)
    anc_grad = jax.ShapeDtypeStruct((anc, HD), jnp.float32)
    return pl.pallas_call(
        attend_kernel,
        grid=grid,
        in_specs=[maskspec, qspec, gspec, kospec, vospec, kaspec, vaspec],
        out_specs=[qspec, qspec, ownspec, ownspec, ancspec, ancspec],
        out_shape=[out_rows, out_rows, own_grad, own_grad, anc_grad, anc_grad],
        scratch_shapes=[pltpu.VMEM((seg_len, HD), jnp.float32), pltpu.VMEM((seg_len, HD), jnp.float32)],
        compiler_params=pltpu.CompilerParams(dimension_semantics=("arbitrary", "arbitrary", "arbitrary")),
    )(anc_mask, packed, packed, packed, packed, anc_rows, anc_rows)


def on_device(queries, leaf_keys, leaf_values, inner_keys, inner_values, out_grad, ancestors, depths):
    seg_count = lax.axis_size("seg")
    leaf_count = lax.axis_size("leaf")
    seg_here = lax.axis_index("seg")
    leaf_here = lax.axis_index("leaf")
    leaf_dev, rows_here, query_width = queries.shape
    slot_count = inner_keys.shape[0]
    key_width = leaf_keys.shape[2]
    kv_heads = key_width // HD
    group_heads = query_width // key_width
    head_width = group_heads * HD
    seg_len = rows_here * leaf_count
    levels = ancestors.shape[1]
    pair_count = leaf_count // kv_heads
    pair_leaves = leaf_dev // pair_count
    my_pair = leaf_here % pair_count

    group_lists = ancestors[::leaf_dev]
    group_depth = depths[::leaf_dev]
    owners = group_lists // slot_count
    slot_of = group_lists % slot_count
    level_ids = jnp.arange(levels, dtype=jnp.int32)
    alive_levels = level_ids[None, :] < group_depth[:, None]
    served = alive_levels & (owners == seg_here)
    slot_ids = jnp.arange(slot_count, dtype=jnp.int32)
    serve_pick = jnp.sum(
        (served[:, :, None] & (slot_of[:, :, None] == slot_ids[None, None, :])).astype(jnp.float32),
        axis=1,
    ).astype(jnp.bfloat16)
    stored = jnp.concatenate([inner_keys, inner_values], axis=2)
    outgoing = jnp.einsum("gs,src->grc", serve_pick, stored, preferred_element_type=jnp.float32).astype(
        jnp.bfloat16
    )
    my_owners = jnp.take(owners, seg_here, axis=0)
    my_alive = jnp.take(alive_levels, seg_here, axis=0)
    out_heads = jnp.concatenate(
        [
            outgoing[:, :, :key_width].reshape(seg_count, rows_here, kv_heads, 1, HD),
            outgoing[:, :, key_width:].reshape(seg_count, rows_here, kv_heads, 1, HD),
        ],
        axis=3,
    ).reshape(seg_count, rows_here, kv_heads, 2 * HD).transpose(0, 2, 1, 3)
    anc_send = jnp.broadcast_to(
        out_heads[:, :, None], (seg_count, kv_heads, pair_count, rows_here, 2 * HD)
    ).reshape(seg_count * leaf_count, rows_here, 2 * HD)
    anc_arrived = lax.all_to_all(anc_send, ("seg", "leaf"), split_axis=0, concat_axis=0, tiled=True)
    anc_arrived = anc_arrived.reshape(seg_count, leaf_count * rows_here, 2 * HD)
    anc_got = jnp.where(
        my_alive[:, None, None], jnp.take(anc_arrived, my_owners, axis=0), jnp.zeros((), jnp.bfloat16)
    ).reshape(levels * seg_len, 2 * HD)
    anc_mask = jnp.repeat(my_alive, seg_len).astype(jnp.float32)[None, :]

    def to_heads(x, width):
        shaped = x.reshape(pair_count, pair_leaves, rows_here, kv_heads, width)
        return shaped.transpose(3, 0, 1, 2, 4).reshape(leaf_count, pair_leaves, rows_here, width)

    packed = jnp.concatenate(
        [to_heads(queries, head_width), to_heads(out_grad, head_width), to_heads(leaf_keys, HD), to_heads(leaf_values, HD)],
        axis=3,
    )
    homes = []
    anc_partial = None
    for chunk in range(pair_leaves):
        got = lax.all_to_all(packed[:, chunk], "leaf", split_axis=0, concat_axis=0, tiled=True)
        got = got.reshape(1, seg_len, packed.shape[3])
        res, dq, dko, dvo, dka, dva = attend_all(anc_mask, got, anc_got, group_heads)
        part = jnp.concatenate([dka, dva], axis=1)
        anc_partial = part if anc_partial is None else anc_partial + part
        back = jnp.concatenate([res, dq, dko.astype(jnp.bfloat16), dvo.astype(jnp.bfloat16)], axis=2)
        back = back.reshape(leaf_count, rows_here, back.shape[2])
        homes.append(lax.all_to_all(back, "leaf", split_axis=0, concat_axis=0, tiled=True))
    home = jnp.stack(homes, axis=1)
    home = home.reshape(kv_heads, pair_count, pair_leaves, rows_here, home.shape[3])

    def to_rows(x):
        width = x.shape[-1]
        return x.transpose(1, 2, 3, 0, 4).reshape(leaf_dev, rows_here, kv_heads * width)

    attention = to_rows(home[..., :head_width])
    query_grad = to_rows(home[..., head_width : 2 * head_width])
    leaf_key_grad = to_rows(home[..., 2 * head_width : 2 * head_width + HD])
    leaf_value_grad = to_rows(home[..., 2 * head_width + HD :])

    seg_ids = jnp.arange(seg_count, dtype=jnp.int32)
    homeward_pick = ((my_owners[None, :] == seg_ids[:, None]) & my_alive[None, :]).astype(jnp.bfloat16)
    partial_rows = anc_partial.astype(jnp.bfloat16).reshape(levels, seg_len, 2 * HD)
    homeward = jnp.einsum("ok,krc->orc", homeward_pick, partial_rows, preferred_element_type=jnp.float32).astype(
        jnp.bfloat16
    )
    homeward = homeward.reshape(seg_count * leaf_count, rows_here, 2 * HD)
    returned = lax.all_to_all(homeward, ("seg", "leaf"), split_axis=0, concat_axis=0, tiled=True)
    returned = returned.astype(jnp.float32).reshape(seg_count, kv_heads, pair_count, rows_here, 2 * HD).sum(axis=2)
    collected = jnp.einsum(
        "gs,ghrc->shrc", serve_pick.astype(jnp.float32), returned, preferred_element_type=jnp.float32
    )
    inner_key_grad = collected[..., :HD].transpose(0, 2, 1, 3).reshape(slot_count, rows_here, key_width)
    inner_value_grad = collected[..., HD:].transpose(0, 2, 1, 3).reshape(slot_count, rows_here, key_width)
    return (
        attention,
        query_grad,
        leaf_key_grad,
        leaf_value_grad,
        inner_key_grad.astype(jnp.bfloat16),
        inner_value_grad.astype(jnp.bfloat16),
    )


def solution(mesh):
    spec = P("seg", "leaf", None)
    return jax.shard_map(
        on_device,
        mesh=mesh,
        in_specs=(spec, spec, spec, spec, spec, spec, P(), P()),
        out_specs=(spec, spec, spec, spec, spec, spec),
        check_vma=False,
    )
```

```python
import math

import jax
import jax.numpy as jnp
from jax import lax
from jax.experimental import pallas as pl
from jax.experimental.pallas import tpu as pltpu
from jax.sharding import PartitionSpec as P

HD = 128


NEG_FILL = -1e30


def attend_kernel(mask_ref, q_ref, g_ref, ko_ref, vo_ref, ka_ref, va_ref,
                  o_ref, dq_ref, dko_ref, dvo_ref, dka_ref, dva_ref, dko_acc, dvo_acc):
    leaf_i = pl.program_id(0)
    head_i = pl.program_id(1)
    row_i = pl.program_id(2)
    head_count = pl.num_programs(1)
    row_count = pl.num_programs(2)
    block_rows = q_ref.shape[0]
    seg_len = ko_ref.shape[0]
    scale = 1.0 / math.sqrt(q_ref.shape[-1])

    @pl.when((leaf_i == 0) & (head_i == 0) & (row_i == 0))
    def _():
        dka_ref[...] = jnp.zeros_like(dka_ref)
        dva_ref[...] = jnp.zeros_like(dva_ref)

    @pl.when((head_i == 0) & (row_i == 0))
    def _():
        dko_acc[...] = jnp.zeros_like(dko_acc)
        dvo_acc[...] = jnp.zeros_like(dvo_acc)

    nt = (((1,), (1,)), ((), ()))
    tn = (((0,), (0,)), ((), ()))
    q = q_ref[...]
    g = g_ref[...]
    ka = ka_ref[...]
    va = va_ref[...]
    ko = ko_ref[...]
    vo = vo_ref[...]
    s_a = lax.dot_general(q, ka, nt, preferred_element_type=jnp.float32) * scale
    s_o = lax.dot_general(q, ko, nt, preferred_element_type=jnp.float32) * scale
    s_a = jnp.where(mask_ref[...] > 0.5, s_a, NEG_FILL)
    rows = row_i * block_rows + lax.broadcasted_iota(jnp.int32, (block_rows, seg_len), 0)
    cols = lax.broadcasted_iota(jnp.int32, (block_rows, seg_len), 1)
    s_o = jnp.where(cols <= rows, s_o, NEG_FILL)
    m = jnp.maximum(jnp.max(s_a, axis=1, keepdims=True), jnp.max(s_o, axis=1, keepdims=True))
    w_a = jnp.exp(s_a - m)
    w_o = jnp.exp(s_o - m)
    total = jnp.sum(w_a, axis=1, keepdims=True) + jnp.sum(w_o, axis=1, keepdims=True)
    inv = 1.0 / total
    p_a = w_a * inv
    p_o = w_o * inv
    pb_a = p_a.astype(jnp.bfloat16)
    pb_o = p_o.astype(jnp.bfloat16)
    o = jnp.dot(pb_a, va, preferred_element_type=jnp.float32) + jnp.dot(pb_o, vo, preferred_element_type=jnp.float32)
    o_b = o.astype(jnp.bfloat16)
    o_ref[...] = o_b
    delta = jnp.sum(g.astype(jnp.float32) * o_b.astype(jnp.float32), axis=1, keepdims=True)
    dp_a = lax.dot_general(g, va, nt, preferred_element_type=jnp.float32)
    dp_o = lax.dot_general(g, vo, nt, preferred_element_type=jnp.float32)
    ds_a = (p_a * (dp_a - delta)).astype(jnp.bfloat16)
    ds_o = (p_o * (dp_o - delta)).astype(jnp.bfloat16)
    dq = (jnp.dot(ds_a, ka, preferred_element_type=jnp.float32) + jnp.dot(ds_o, ko, preferred_element_type=jnp.float32)) * scale
    dq_ref[...] = dq.astype(jnp.bfloat16)
    dka_ref[...] += lax.dot_general(ds_a, q, tn, preferred_element_type=jnp.float32)
    dva_ref[...] += lax.dot_general(pb_a, g, tn, preferred_element_type=jnp.float32)
    dko_acc[...] += lax.dot_general(ds_o, q, tn, preferred_element_type=jnp.float32)
    dvo_acc[...] += lax.dot_general(pb_o, g, tn, preferred_element_type=jnp.float32)

    @pl.when((head_i == head_count - 1) & (row_i == row_count - 1))
    def _():
        dko_ref[...] = dko_acc[...] * scale
        dvo_ref[...] = dvo_acc[...]

    @pl.when((leaf_i == pl.num_programs(0) - 1) & (head_i == head_count - 1) & (row_i == row_count - 1))
    def _():
        dka_ref[...] = dka_ref[...] * scale


def attend_all(anc_mask, packed, anc_rows, heads, block_rows=512):
    leaves, seg_len, _ = packed.shape
    anc = anc_rows.shape[0]
    grid = (leaves, heads, seg_len // block_rows)
    qspec = pl.BlockSpec((None, block_rows, HD), lambda l, h, r: (l, r, h))
    gspec = pl.BlockSpec((None, block_rows, HD), lambda l, h, r: (l, r, heads + h))
    kospec = pl.BlockSpec((None, seg_len, HD), lambda l, h, r: (l, 0, 2 * heads))
    vospec = pl.BlockSpec((None, seg_len, HD), lambda l, h, r: (l, 0, 2 * heads + 1))
    kaspec = pl.BlockSpec((anc, HD), lambda l, h, r: (0, 0))
    vaspec = pl.BlockSpec((anc, HD), lambda l, h, r: (0, 1))
    maskspec = pl.BlockSpec((1, anc), lambda l, h, r: (0, 0))
    ownspec = pl.BlockSpec((None, seg_len, HD), lambda l, h, r: (l, 0, 0))
    ancspec = pl.BlockSpec((anc, HD), lambda l, h, r: (0, 0))
    out_rows = jax.ShapeDtypeStruct((leaves, seg_len, heads * HD), jnp.bfloat16)
    own_grad = jax.ShapeDtypeStruct((leaves, seg_len, HD), jnp.float32)
    anc_grad = jax.ShapeDtypeStruct((anc, HD), jnp.float32)
    return pl.pallas_call(
        attend_kernel,
        grid=grid,
        in_specs=[maskspec, qspec, gspec, kospec, vospec, kaspec, vaspec],
        out_specs=[qspec, qspec, ownspec, ownspec, ancspec, ancspec],
        out_shape=[out_rows, out_rows, own_grad, own_grad, anc_grad, anc_grad],
        scratch_shapes=[pltpu.VMEM((seg_len, HD), jnp.float32), pltpu.VMEM((seg_len, HD), jnp.float32)],
        compiler_params=pltpu.CompilerParams(dimension_semantics=("arbitrary", "arbitrary", "arbitrary")),
    )(anc_mask, packed, packed, packed, packed, anc_rows, anc_rows)


def leaf_shift(blocks, leaf_here, leaf_count):
    pieces = [jnp.take(blocks, leaf_here, axis=0)]
    for shift in range(1, leaf_count):
        piece = jnp.take(blocks, (leaf_here + shift) % leaf_count, axis=0)
        pairs = [(i, (i + shift) % leaf_count) for i in range(leaf_count)]
        pieces.append(lax.ppermute(piece, "leaf", pairs))
    by_shift = jnp.stack(pieces, axis=0)
    sources = jnp.arange(leaf_count, dtype=jnp.int32)
    return jnp.take(by_shift, (leaf_here - sources) % leaf_count, axis=0)


def on_device(queries, leaf_keys, leaf_values, inner_keys, inner_values, out_grad, ancestors, depths):
    seg_count = lax.axis_size("seg")
    leaf_count = lax.axis_size("leaf")
    seg_here = lax.axis_index("seg")
    leaf_here = lax.axis_index("leaf")
    leaf_dev, rows_here, query_width = queries.shape
    slot_count = inner_keys.shape[0]
    key_width = leaf_keys.shape[2]
    kv_heads = key_width // HD
    group_heads = query_width // key_width
    head_width = group_heads * HD
    seg_len = rows_here * leaf_count
    levels = ancestors.shape[1]
    pair_count = leaf_count // kv_heads
    pair_leaves = leaf_dev // pair_count
    my_pair = leaf_here % pair_count

    group_lists = ancestors[::leaf_dev]
    group_depth = depths[::leaf_dev]
    owners = group_lists // slot_count
    slot_of = group_lists % slot_count
    level_ids = jnp.arange(levels, dtype=jnp.int32)
    alive_levels = level_ids[None, :] < group_depth[:, None]
    served = alive_levels & (owners == seg_here)
    slot_ids = jnp.arange(slot_count, dtype=jnp.int32)
    serve_pick = jnp.sum(
        (served[:, :, None] & (slot_of[:, :, None] == slot_ids[None, None, :])).astype(jnp.float32),
        axis=1,
    ).astype(jnp.bfloat16)
    stored = jnp.concatenate([inner_keys, inner_values], axis=2)
    outgoing = jnp.einsum("gs,src->grc", serve_pick, stored, preferred_element_type=jnp.float32).astype(
        jnp.bfloat16
    )
    my_owners = jnp.take(owners, seg_here, axis=0)
    my_alive = jnp.take(alive_levels, seg_here, axis=0)
    out_heads = jnp.concatenate(
        [
            outgoing[:, :, :key_width].reshape(seg_count, rows_here, kv_heads, 1, HD),
            outgoing[:, :, key_width:].reshape(seg_count, rows_here, kv_heads, 1, HD),
        ],
        axis=3,
    ).reshape(seg_count, rows_here, kv_heads, 2 * HD).transpose(0, 2, 1, 3)
    anc_send = jnp.broadcast_to(
        out_heads[:, :, None], (seg_count, kv_heads, pair_count, rows_here, 2 * HD)
    ).reshape(seg_count * leaf_count, rows_here, 2 * HD)
    anc_arrived = lax.all_to_all(anc_send, ("seg", "leaf"), split_axis=0, concat_axis=0, tiled=True)
    anc_arrived = anc_arrived.reshape(seg_count, leaf_count * rows_here, 2 * HD)
    anc_got = jnp.where(
        my_alive[:, None, None], jnp.take(anc_arrived, my_owners, axis=0), jnp.zeros((), jnp.bfloat16)
    ).reshape(levels * seg_len, 2 * HD)
    anc_mask = jnp.repeat(my_alive, seg_len).astype(jnp.float32)[None, :]

    def to_heads(x, width):
        shaped = x.reshape(pair_count, pair_leaves, rows_here, kv_heads, width)
        return shaped.transpose(3, 0, 1, 2, 4).reshape(leaf_count, pair_leaves, rows_here, width)

    packed = jnp.concatenate(
        [to_heads(queries, head_width), to_heads(out_grad, head_width), to_heads(leaf_keys, HD), to_heads(leaf_values, HD)],
        axis=3,
    )
    homes = []
    anc_partial = None
    for chunk in range(pair_leaves):
        if chunk == 0:
            got = leaf_shift(packed[:, chunk], leaf_here, leaf_count)
        else:
            got = lax.all_to_all(packed[:, chunk], "leaf", split_axis=0, concat_axis=0, tiled=True)
        got = got.reshape(1, seg_len, packed.shape[3])
        res, dq, dko, dvo, dka, dva = attend_all(anc_mask, got, anc_got, group_heads)
        part = jnp.concatenate([dka, dva], axis=1)
        anc_partial = part if anc_partial is None else anc_partial + part
        back = jnp.concatenate([res, dq, dko.astype(jnp.bfloat16), dvo.astype(jnp.bfloat16)], axis=2)
        back = back.reshape(leaf_count, rows_here, back.shape[2])
        homes.append(lax.all_to_all(back, "leaf", split_axis=0, concat_axis=0, tiled=True))
    home = jnp.stack(homes, axis=1)
    home = home.reshape(kv_heads, pair_count, pair_leaves, rows_here, home.shape[3])

    def to_rows(x):
        width = x.shape[-1]
        return x.transpose(1, 2, 3, 0, 4).reshape(leaf_dev, rows_here, kv_heads * width)

    attention = to_rows(home[..., :head_width])
    query_grad = to_rows(home[..., head_width : 2 * head_width])
    leaf_key_grad = to_rows(home[..., 2 * head_width : 2 * head_width + HD])
    leaf_value_grad = to_rows(home[..., 2 * head_width + HD :])

    seg_ids = jnp.arange(seg_count, dtype=jnp.int32)
    homeward_pick = ((my_owners[None, :] == seg_ids[:, None]) & my_alive[None, :]).astype(jnp.bfloat16)
    partial_rows = anc_partial.astype(jnp.bfloat16).reshape(levels, seg_len, 2 * HD)
    homeward = jnp.einsum("ok,krc->orc", homeward_pick, partial_rows, preferred_element_type=jnp.float32).astype(
        jnp.bfloat16
    )
    homeward = homeward.reshape(seg_count * leaf_count, rows_here, 2 * HD)
    returned = lax.all_to_all(homeward, ("seg", "leaf"), split_axis=0, concat_axis=0, tiled=True)
    returned = returned.astype(jnp.float32).reshape(seg_count, kv_heads, pair_count, rows_here, 2 * HD).sum(axis=2)
    collected = jnp.einsum(
        "gs,ghrc->shrc", serve_pick.astype(jnp.float32), returned, preferred_element_type=jnp.float32
    )
    inner_key_grad = collected[..., :HD].transpose(0, 2, 1, 3).reshape(slot_count, rows_here, key_width)
    inner_value_grad = collected[..., HD:].transpose(0, 2, 1, 3).reshape(slot_count, rows_here, key_width)
    return (
        attention,
        query_grad,
        leaf_key_grad,
        leaf_value_grad,
        inner_key_grad.astype(jnp.bfloat16),
        inner_value_grad.astype(jnp.bfloat16),
    )


def solution(mesh):
    spec = P("seg", "leaf", None)
    return jax.shard_map(
        on_device,
        mesh=mesh,
        in_specs=(spec, spec, spec, spec, spec, spec, P(), P()),
        out_specs=(spec, spec, spec, spec, spec, spec),
        check_vma=False,
    )
```

```python
import math

import jax
import jax.numpy as jnp
from jax import lax
from jax.experimental import pallas as pl
from jax.experimental.pallas import tpu as pltpu
from jax.sharding import PartitionSpec as P

HD = 128


NEG_FILL = -1e30


def attend_kernel(mask_ref, q_ref, g_ref, ko_ref, vo_ref, ka_ref, va_ref,
                  o_ref, dq_ref, dko_ref, dvo_ref, dka_ref, dva_ref, dko_acc, dvo_acc):
    leaf_i = pl.program_id(0)
    head_i = pl.program_id(1)
    row_i = pl.program_id(2)
    head_count = pl.num_programs(1)
    row_count = pl.num_programs(2)
    block_rows = q_ref.shape[0]
    seg_len = ko_ref.shape[0]
    scale = 1.0 / math.sqrt(q_ref.shape[-1])

    @pl.when((leaf_i == 0) & (head_i == 0) & (row_i == 0))
    def _():
        dka_ref[...] = jnp.zeros_like(dka_ref)
        dva_ref[...] = jnp.zeros_like(dva_ref)

    @pl.when((head_i == 0) & (row_i == 0))
    def _():
        dko_acc[...] = jnp.zeros_like(dko_acc)
        dvo_acc[...] = jnp.zeros_like(dvo_acc)

    nt = (((1,), (1,)), ((), ()))
    tn = (((0,), (0,)), ((), ()))
    q = q_ref[...]
    g = g_ref[...]
    ka = ka_ref[...]
    va = va_ref[...]
    ko = ko_ref[...]
    vo = vo_ref[...]
    s_a = lax.dot_general(q, ka, nt, preferred_element_type=jnp.float32) * scale
    s_o = lax.dot_general(q, ko, nt, preferred_element_type=jnp.float32) * scale
    s_a = jnp.where(mask_ref[...] > 0.5, s_a, NEG_FILL)
    rows = row_i * block_rows + lax.broadcasted_iota(jnp.int32, (block_rows, seg_len), 0)
    cols = lax.broadcasted_iota(jnp.int32, (block_rows, seg_len), 1)
    s_o = jnp.where(cols <= rows, s_o, NEG_FILL)
    m = jnp.maximum(jnp.max(s_a, axis=1, keepdims=True), jnp.max(s_o, axis=1, keepdims=True))
    w_a = jnp.exp(s_a - m)
    w_o = jnp.exp(s_o - m)
    total = jnp.sum(w_a, axis=1, keepdims=True) + jnp.sum(w_o, axis=1, keepdims=True)
    inv = 1.0 / total
    p_a = w_a * inv
    p_o = w_o * inv
    pb_a = p_a.astype(jnp.bfloat16)
    pb_o = p_o.astype(jnp.bfloat16)
    o = jnp.dot(pb_a, va, preferred_element_type=jnp.float32) + jnp.dot(pb_o, vo, preferred_element_type=jnp.float32)
    o_b = o.astype(jnp.bfloat16)
    o_ref[...] = o_b
    delta = jnp.sum(g.astype(jnp.float32) * o_b.astype(jnp.float32), axis=1, keepdims=True)
    dp_a = lax.dot_general(g, va, nt, preferred_element_type=jnp.float32)
    dp_o = lax.dot_general(g, vo, nt, preferred_element_type=jnp.float32)
    ds_a = (p_a * (dp_a - delta)).astype(jnp.bfloat16)
    ds_o = (p_o * (dp_o - delta)).astype(jnp.bfloat16)
    dq = (jnp.dot(ds_a, ka, preferred_element_type=jnp.float32) + jnp.dot(ds_o, ko, preferred_element_type=jnp.float32)) * scale
    dq_ref[...] = dq.astype(jnp.bfloat16)
    dka_ref[...] += lax.dot_general(ds_a, q, tn, preferred_element_type=jnp.float32)
    dva_ref[...] += lax.dot_general(pb_a, g, tn, preferred_element_type=jnp.float32)
    dko_acc[...] += lax.dot_general(ds_o, q, tn, preferred_element_type=jnp.float32)
    dvo_acc[...] += lax.dot_general(pb_o, g, tn, preferred_element_type=jnp.float32)

    @pl.when((head_i == head_count - 1) & (row_i == row_count - 1))
    def _():
        dko_ref[...] = dko_acc[...] * scale
        dvo_ref[...] = dvo_acc[...]

    @pl.when((leaf_i == pl.num_programs(0) - 1) & (head_i == head_count - 1) & (row_i == row_count - 1))
    def _():
        dka_ref[...] = dka_ref[...] * scale


def attend_all(anc_mask, packed, anc_rows, heads, block_rows=512):
    leaves, seg_len, _ = packed.shape
    anc = anc_rows.shape[0]
    grid = (leaves, heads, seg_len // block_rows)
    qspec = pl.BlockSpec((None, block_rows, HD), lambda l, h, r: (l, r, h))
    gspec = pl.BlockSpec((None, block_rows, HD), lambda l, h, r: (l, r, heads + h))
    kospec = pl.BlockSpec((None, seg_len, HD), lambda l, h, r: (l, 0, 2 * heads))
    vospec = pl.BlockSpec((None, seg_len, HD), lambda l, h, r: (l, 0, 2 * heads + 1))
    kaspec = pl.BlockSpec((anc, HD), lambda l, h, r: (0, 0))
    vaspec = pl.BlockSpec((anc, HD), lambda l, h, r: (0, 1))
    maskspec = pl.BlockSpec((1, anc), lambda l, h, r: (0, 0))
    ownspec = pl.BlockSpec((None, seg_len, HD), lambda l, h, r: (l, 0, 0))
    ancspec = pl.BlockSpec((anc, HD), lambda l, h, r: (0, 0))
    out_rows = jax.ShapeDtypeStruct((leaves, seg_len, heads * HD), jnp.bfloat16)
    own_grad = jax.ShapeDtypeStruct((leaves, seg_len, HD), jnp.float32)
    anc_grad = jax.ShapeDtypeStruct((anc, HD), jnp.float32)
    return pl.pallas_call(
        attend_kernel,
        grid=grid,
        in_specs=[maskspec, qspec, gspec, kospec, vospec, kaspec, vaspec],
        out_specs=[qspec, qspec, ownspec, ownspec, ancspec, ancspec],
        out_shape=[out_rows, out_rows, own_grad, own_grad, anc_grad, anc_grad],
        scratch_shapes=[pltpu.VMEM((seg_len, HD), jnp.float32), pltpu.VMEM((seg_len, HD), jnp.float32)],
        compiler_params=pltpu.CompilerParams(dimension_semantics=("arbitrary", "arbitrary", "arbitrary")),
    )(anc_mask, packed, packed, packed, packed, anc_rows, anc_rows)


def on_device(queries, leaf_keys, leaf_values, inner_keys, inner_values, out_grad, ancestors, depths):
    seg_count = lax.axis_size("seg")
    leaf_count = lax.axis_size("leaf")
    seg_here = lax.axis_index("seg")
    leaf_here = lax.axis_index("leaf")
    leaf_dev, rows_here, query_width = queries.shape
    slot_count = inner_keys.shape[0]
    key_width = leaf_keys.shape[2]
    kv_heads = key_width // HD
    group_heads = query_width // key_width
    head_width = group_heads * HD
    seg_len = rows_here * leaf_count
    levels = ancestors.shape[1]
    pair_count = leaf_count // kv_heads
    pair_leaves = leaf_dev // pair_count
    my_pair = leaf_here % pair_count

    group_lists = ancestors[::leaf_dev]
    group_depth = depths[::leaf_dev]
    owners = group_lists // slot_count
    slot_of = group_lists % slot_count
    level_ids = jnp.arange(levels, dtype=jnp.int32)
    alive_levels = level_ids[None, :] < group_depth[:, None]
    served = alive_levels & (owners == seg_here)
    slot_ids = jnp.arange(slot_count, dtype=jnp.int32)
    serve_pick = jnp.sum(
        (served[:, :, None] & (slot_of[:, :, None] == slot_ids[None, None, :])).astype(jnp.float32),
        axis=1,
    ).astype(jnp.bfloat16)
    stored = jnp.concatenate([inner_keys, inner_values], axis=2)
    outgoing = jnp.einsum("gs,src->grc", serve_pick, stored, preferred_element_type=jnp.float32).astype(
        jnp.bfloat16
    )
    my_owners = jnp.take(owners, seg_here, axis=0)
    my_alive = jnp.take(alive_levels, seg_here, axis=0)
    out_heads = jnp.concatenate(
        [
            outgoing[:, :, :key_width].reshape(seg_count, rows_here, kv_heads, 1, HD),
            outgoing[:, :, key_width:].reshape(seg_count, rows_here, kv_heads, 1, HD),
        ],
        axis=3,
    ).reshape(seg_count, rows_here, kv_heads, 2 * HD).transpose(0, 2, 1, 3)
    anc_send = out_heads.reshape(seg_count * kv_heads, rows_here, 2 * HD)
    parity_groups = [
        [s * leaf_count + j for s in range(seg_count) for j in range(leaf_count) if j % pair_count == q]
        for q in range(pair_count)
    ]
    anc_half = lax.all_to_all(
        anc_send, ("seg", "leaf"), split_axis=0, concat_axis=0, tiled=True, axis_index_groups=parity_groups
    )
    anc_half = anc_half.reshape(seg_count, leaf_count // pair_count, rows_here, 2 * HD)
    mine = jnp.where(
        my_alive[:, None, None, None], jnp.take(anc_half, my_owners, axis=0), jnp.zeros((), jnp.bfloat16)
    )
    swap = [(j, j + 1 - 2 * (j % 2)) for j in range(leaf_count)]
    theirs = lax.ppermute(mine, "leaf", swap)
    my_parity = leaf_here % pair_count
    even = jnp.where(my_parity == 0, mine, theirs)
    odd = jnp.where(my_parity == 0, theirs, mine)
    anc_got = jnp.stack([even, odd], axis=2).reshape(levels * seg_len, 2 * HD)
    anc_mask = jnp.repeat(my_alive, seg_len).astype(jnp.float32)[None, :]

    def to_heads(x, width):
        shaped = x.reshape(pair_count, pair_leaves, rows_here, kv_heads, width)
        return shaped.transpose(3, 0, 1, 2, 4).reshape(leaf_count, pair_leaves, rows_here, width)

    packed = jnp.concatenate(
        [to_heads(queries, head_width), to_heads(out_grad, head_width), to_heads(leaf_keys, HD), to_heads(leaf_values, HD)],
        axis=3,
    )
    homes = []
    anc_partial = None
    for chunk in range(pair_leaves):
        got = lax.all_to_all(packed[:, chunk], "leaf", split_axis=0, concat_axis=0, tiled=True)
        got = got.reshape(1, seg_len, packed.shape[3])
        res, dq, dko, dvo, dka, dva = attend_all(anc_mask, got, anc_got, group_heads)
        part = jnp.concatenate([dka, dva], axis=1)
        anc_partial = part if anc_partial is None else anc_partial + part
        back = jnp.concatenate([res, dq, dko.astype(jnp.bfloat16), dvo.astype(jnp.bfloat16)], axis=2)
        back = back.reshape(leaf_count, rows_here, back.shape[2])
        homes.append(lax.all_to_all(back, "leaf", split_axis=0, concat_axis=0, tiled=True))
    home = jnp.stack(homes, axis=1)
    home = home.reshape(kv_heads, pair_count, pair_leaves, rows_here, home.shape[3])

    def to_rows(x):
        width = x.shape[-1]
        return x.transpose(1, 2, 3, 0, 4).reshape(leaf_dev, rows_here, kv_heads * width)

    attention = to_rows(home[..., :head_width])
    query_grad = to_rows(home[..., head_width : 2 * head_width])
    leaf_key_grad = to_rows(home[..., 2 * head_width : 2 * head_width + HD])
    leaf_value_grad = to_rows(home[..., 2 * head_width + HD :])

    seg_ids = jnp.arange(seg_count, dtype=jnp.int32)
    homeward_pick = ((my_owners[None, :] == seg_ids[:, None]) & my_alive[None, :]).astype(jnp.bfloat16)
    partial_rows = anc_partial.astype(jnp.bfloat16).reshape(levels, seg_len, 2 * HD)
    homeward = jnp.einsum("ok,krc->orc", homeward_pick, partial_rows, preferred_element_type=jnp.float32).astype(
        jnp.bfloat16
    )
    homeward = homeward.reshape(seg_count * leaf_count, rows_here, 2 * HD)
    returned = lax.all_to_all(homeward, ("seg", "leaf"), split_axis=0, concat_axis=0, tiled=True)
    returned = returned.astype(jnp.float32).reshape(seg_count, kv_heads, pair_count, rows_here, 2 * HD).sum(axis=2)
    collected = jnp.einsum(
        "gs,ghrc->shrc", serve_pick.astype(jnp.float32), returned, preferred_element_type=jnp.float32
    )
    inner_key_grad = collected[..., :HD].transpose(0, 2, 1, 3).reshape(slot_count, rows_here, key_width)
    inner_value_grad = collected[..., HD:].transpose(0, 2, 1, 3).reshape(slot_count, rows_here, key_width)
    return (
        attention,
        query_grad,
        leaf_key_grad,
        leaf_value_grad,
        inner_key_grad.astype(jnp.bfloat16),
        inner_value_grad.astype(jnp.bfloat16),
    )


def solution(mesh):
    spec = P("seg", "leaf", None)
    return jax.shard_map(
        on_device,
        mesh=mesh,
        in_specs=(spec, spec, spec, spec, spec, spec, P(), P()),
        out_specs=(spec, spec, spec, spec, spec, spec),
        check_vma=False,
    )
```

```python
import math

import jax
import jax.numpy as jnp
from jax import lax
from jax.experimental import pallas as pl
from jax.experimental.pallas import tpu as pltpu
from jax.sharding import PartitionSpec as P

HD = 128


NEG_FILL = -1e30


def attend_kernel(mask_ref, q_ref, g_ref, ko_ref, vo_ref, ka_ref, va_ref,
                  back_ref, dka_ref, dva_ref, dko_acc, dvo_acc):
    leaf_i = pl.program_id(0)
    head_i = pl.program_id(1)
    row_i = pl.program_id(2)
    head_count = pl.num_programs(1)
    row_count = pl.num_programs(2)
    block_rows = q_ref.shape[0]
    seg_len = ko_ref.shape[0]
    scale = 1.0 / math.sqrt(q_ref.shape[-1])

    @pl.when((leaf_i == 0) & (head_i == 0) & (row_i == 0))
    def _():
        dka_ref[...] = jnp.zeros_like(dka_ref)
        dva_ref[...] = jnp.zeros_like(dva_ref)

    @pl.when((head_i == 0) & (row_i == 0))
    def _():
        dko_acc[...] = jnp.zeros_like(dko_acc)
        dvo_acc[...] = jnp.zeros_like(dvo_acc)

    nt = (((1,), (1,)), ((), ()))
    tn = (((0,), (0,)), ((), ()))
    q = q_ref[...]
    g = g_ref[...]
    ka = ka_ref[...]
    va = va_ref[...]
    ko = ko_ref[...]
    vo = vo_ref[...]
    s_a = lax.dot_general(q, ka, nt, preferred_element_type=jnp.float32) * scale
    s_o = lax.dot_general(q, ko, nt, preferred_element_type=jnp.float32) * scale
    s_a = jnp.where(mask_ref[...] > 0.5, s_a, NEG_FILL)
    rows = row_i * block_rows + lax.broadcasted_iota(jnp.int32, (block_rows, seg_len), 0)
    cols = lax.broadcasted_iota(jnp.int32, (block_rows, seg_len), 1)
    s_o = jnp.where(cols <= rows, s_o, NEG_FILL)
    m = jnp.maximum(jnp.max(s_a, axis=1, keepdims=True), jnp.max(s_o, axis=1, keepdims=True))
    w_a = jnp.exp(s_a - m)
    w_o = jnp.exp(s_o - m)
    total = jnp.sum(w_a, axis=1, keepdims=True) + jnp.sum(w_o, axis=1, keepdims=True)
    inv = 1.0 / total
    p_a = w_a * inv
    p_o = w_o * inv
    pb_a = p_a.astype(jnp.bfloat16)
    pb_o = p_o.astype(jnp.bfloat16)
    o = jnp.dot(pb_a, va, preferred_element_type=jnp.float32) + jnp.dot(pb_o, vo, preferred_element_type=jnp.float32)
    o_b = o.astype(jnp.bfloat16)
    row_span = pl.ds(pl.multiple_of(row_i * block_rows, block_rows), block_rows)
    back_ref[row_span, pl.ds(pl.multiple_of(head_i * HD, HD), HD)] = o_b
    delta = jnp.sum(g.astype(jnp.float32) * o_b.astype(jnp.float32), axis=1, keepdims=True)
    dp_a = lax.dot_general(g, va, nt, preferred_element_type=jnp.float32)
    dp_o = lax.dot_general(g, vo, nt, preferred_element_type=jnp.float32)
    ds_a = (p_a * (dp_a - delta)).astype(jnp.bfloat16)
    ds_o = (p_o * (dp_o - delta)).astype(jnp.bfloat16)
    dq = (jnp.dot(ds_a, ka, preferred_element_type=jnp.float32) + jnp.dot(ds_o, ko, preferred_element_type=jnp.float32)) * scale
    back_ref[row_span, pl.ds(pl.multiple_of((head_count + head_i) * HD, HD), HD)] = dq.astype(jnp.bfloat16)
    dka_ref[...] += lax.dot_general(ds_a, q, tn, preferred_element_type=jnp.float32)
    dva_ref[...] += lax.dot_general(pb_a, g, tn, preferred_element_type=jnp.float32)
    dko_acc[...] += lax.dot_general(ds_o, q, tn, preferred_element_type=jnp.float32)
    dvo_acc[...] += lax.dot_general(pb_o, g, tn, preferred_element_type=jnp.float32)

    @pl.when((head_i == head_count - 1) & (row_i == row_count - 1))
    def _():
        back_ref[:, 2 * head_count * HD : (2 * head_count + 1) * HD] = (dko_acc[...] * scale).astype(jnp.bfloat16)
        back_ref[:, (2 * head_count + 1) * HD :] = dvo_acc[...].astype(jnp.bfloat16)

    @pl.when((leaf_i == pl.num_programs(0) - 1) & (head_i == head_count - 1) & (row_i == row_count - 1))
    def _():
        dka_ref[...] = dka_ref[...] * scale


def attend_all(anc_mask, packed, anc_rows, heads, block_rows=512):
    leaves, seg_len, _ = packed.shape
    anc = anc_rows.shape[0]
    grid = (leaves, heads, seg_len // block_rows)
    qspec = pl.BlockSpec((None, block_rows, HD), lambda l, h, r: (l, r, h))
    gspec = pl.BlockSpec((None, block_rows, HD), lambda l, h, r: (l, r, heads + h))
    kospec = pl.BlockSpec((None, seg_len, HD), lambda l, h, r: (l, 0, 2 * heads))
    vospec = pl.BlockSpec((None, seg_len, HD), lambda l, h, r: (l, 0, 2 * heads + 1))
    kaspec = pl.BlockSpec((anc, HD), lambda l, h, r: (0, 0))
    vaspec = pl.BlockSpec((anc, HD), lambda l, h, r: (0, 1))
    maskspec = pl.BlockSpec((1, anc), lambda l, h, r: (0, 0))
    ownspec = pl.BlockSpec((None, seg_len, HD), lambda l, h, r: (l, 0, 0))
    ancspec = pl.BlockSpec((anc, HD), lambda l, h, r: (0, 0))
    back_rows = jax.ShapeDtypeStruct((leaves, seg_len, (2 * heads + 2) * HD), jnp.bfloat16)
    backspec = pl.BlockSpec((None, seg_len, (2 * heads + 2) * HD), lambda l, h, r: (l, 0, 0))
    anc_grad = jax.ShapeDtypeStruct((anc, HD), jnp.float32)
    return pl.pallas_call(
        attend_kernel,
        grid=grid,
        in_specs=[maskspec, qspec, gspec, kospec, vospec, kaspec, vaspec],
        out_specs=[backspec, ancspec, ancspec],
        out_shape=[back_rows, anc_grad, anc_grad],
        scratch_shapes=[pltpu.VMEM((seg_len, HD), jnp.float32), pltpu.VMEM((seg_len, HD), jnp.float32)],
        compiler_params=pltpu.CompilerParams(dimension_semantics=("arbitrary", "arbitrary", "arbitrary")),
    )(anc_mask, packed, packed, packed, packed, anc_rows, anc_rows)


def on_device(queries, leaf_keys, leaf_values, inner_keys, inner_values, out_grad, ancestors, depths):
    seg_count = lax.axis_size("seg")
    leaf_count = lax.axis_size("leaf")
    seg_here = lax.axis_index("seg")
    leaf_here = lax.axis_index("leaf")
    leaf_dev, rows_here, query_width = queries.shape
    slot_count = inner_keys.shape[0]
    key_width = leaf_keys.shape[2]
    kv_heads = key_width // HD
    group_heads = query_width // key_width
    head_width = group_heads * HD
    seg_len = rows_here * leaf_count
    levels = ancestors.shape[1]
    pair_count = leaf_count // kv_heads
    pair_leaves = leaf_dev // pair_count
    my_pair = leaf_here % pair_count

    group_lists = ancestors[::leaf_dev]
    group_depth = depths[::leaf_dev]
    owners = group_lists // slot_count
    slot_of = group_lists % slot_count
    level_ids = jnp.arange(levels, dtype=jnp.int32)
    alive_levels = level_ids[None, :] < group_depth[:, None]
    served = alive_levels & (owners == seg_here)
    slot_ids = jnp.arange(slot_count, dtype=jnp.int32)
    serve_pick = jnp.sum(
        (served[:, :, None] & (slot_of[:, :, None] == slot_ids[None, None, :])).astype(jnp.float32),
        axis=1,
    ).astype(jnp.bfloat16)
    stored = jnp.concatenate([inner_keys, inner_values], axis=2)
    outgoing = jnp.einsum("gs,src->grc", serve_pick, stored, preferred_element_type=jnp.float32).astype(
        jnp.bfloat16
    )
    my_owners = jnp.take(owners, seg_here, axis=0)
    my_alive = jnp.take(alive_levels, seg_here, axis=0)
    out_heads = jnp.concatenate(
        [
            outgoing[:, :, :key_width].reshape(seg_count, rows_here, kv_heads, 1, HD),
            outgoing[:, :, key_width:].reshape(seg_count, rows_here, kv_heads, 1, HD),
        ],
        axis=3,
    ).reshape(seg_count, rows_here, kv_heads, 2 * HD).transpose(0, 2, 1, 3)
    anc_send = jnp.broadcast_to(
        out_heads[:, :, None], (seg_count, kv_heads, pair_count, rows_here, 2 * HD)
    ).reshape(seg_count * leaf_count, rows_here, 2 * HD)
    anc_arrived = lax.all_to_all(anc_send, ("seg", "leaf"), split_axis=0, concat_axis=0, tiled=True)
    anc_arrived = anc_arrived.reshape(seg_count, leaf_count * rows_here, 2 * HD)
    anc_got = jnp.where(
        my_alive[:, None, None], jnp.take(anc_arrived, my_owners, axis=0), jnp.zeros((), jnp.bfloat16)
    ).reshape(levels * seg_len, 2 * HD)
    anc_mask = jnp.repeat(my_alive, seg_len).astype(jnp.float32)[None, :]

    def to_heads(x, width):
        shaped = x.reshape(pair_count, pair_leaves, rows_here, kv_heads, width)
        return shaped.transpose(3, 0, 1, 2, 4).reshape(leaf_count, pair_leaves, rows_here, width)

    packed = jnp.concatenate(
        [to_heads(queries, head_width), to_heads(out_grad, head_width), to_heads(leaf_keys, HD), to_heads(leaf_values, HD)],
        axis=3,
    )
    homes = []
    anc_partial = None
    for chunk in range(pair_leaves):
        got = lax.all_to_all(packed[:, chunk], "leaf", split_axis=0, concat_axis=0, tiled=True)
        got = got.reshape(1, seg_len, packed.shape[3])
        back, dka, dva = attend_all(anc_mask, got, anc_got, group_heads)
        part = jnp.concatenate([dka, dva], axis=1)
        anc_partial = part if anc_partial is None else anc_partial + part
        back = back.reshape(leaf_count, rows_here, back.shape[2])
        homes.append(lax.all_to_all(back, "leaf", split_axis=0, concat_axis=0, tiled=True))
    home = jnp.stack(homes, axis=1)
    home = home.reshape(kv_heads, pair_count, pair_leaves, rows_here, home.shape[3])

    def to_rows(x):
        width = x.shape[-1]
        return x.transpose(1, 2, 3, 0, 4).reshape(leaf_dev, rows_here, kv_heads * width)

    attention = to_rows(home[..., :head_width])
    query_grad = to_rows(home[..., head_width : 2 * head_width])
    leaf_key_grad = to_rows(home[..., 2 * head_width : 2 * head_width + HD])
    leaf_value_grad = to_rows(home[..., 2 * head_width + HD :])

    seg_ids = jnp.arange(seg_count, dtype=jnp.int32)
    homeward_pick = ((my_owners[None, :] == seg_ids[:, None]) & my_alive[None, :]).astype(jnp.bfloat16)
    partial_rows = anc_partial.astype(jnp.bfloat16).reshape(levels, seg_len, 2 * HD)
    homeward = jnp.einsum("ok,krc->orc", homeward_pick, partial_rows, preferred_element_type=jnp.float32).astype(
        jnp.bfloat16
    )
    homeward = homeward.reshape(seg_count * leaf_count, rows_here, 2 * HD)
    returned = lax.all_to_all(homeward, ("seg", "leaf"), split_axis=0, concat_axis=0, tiled=True)
    returned = returned.astype(jnp.float32).reshape(seg_count, kv_heads, pair_count, rows_here, 2 * HD).sum(axis=2)
    collected = jnp.einsum(
        "gs,ghrc->shrc", serve_pick.astype(jnp.float32), returned, preferred_element_type=jnp.float32
    )
    inner_key_grad = collected[..., :HD].transpose(0, 2, 1, 3).reshape(slot_count, rows_here, key_width)
    inner_value_grad = collected[..., HD:].transpose(0, 2, 1, 3).reshape(slot_count, rows_here, key_width)
    return (
        attention,
        query_grad,
        leaf_key_grad,
        leaf_value_grad,
        inner_key_grad.astype(jnp.bfloat16),
        inner_value_grad.astype(jnp.bfloat16),
    )


def solution(mesh):
    spec = P("seg", "leaf", None)
    return jax.shard_map(
        on_device,
        mesh=mesh,
        in_specs=(spec, spec, spec, spec, spec, spec, P(), P()),
        out_specs=(spec, spec, spec, spec, spec, spec),
        check_vma=False,
    )
```

```python
import math

import jax
import jax.numpy as jnp
from jax import lax
from jax.experimental import pallas as pl
from jax.experimental.pallas import tpu as pltpu
from jax.sharding import PartitionSpec as P

HD = 128


NEG_FILL = -1e30


def attend_kernel(owner_ref, mask_ref, q_ref, g_ref, ko_ref, vo_ref, *refs):
    levels = (len(refs) - 5) // 2
    ka_refs, va_refs = refs[:levels], refs[levels : 2 * levels]
    back_ref, dka_ref, dva_ref, dko_acc, dvo_acc = refs[2 * levels :]
    leaf_i = pl.program_id(0)
    head_i = pl.program_id(1)
    row_i = pl.program_id(2)
    head_count = pl.num_programs(1)
    row_count = pl.num_programs(2)
    block_rows = q_ref.shape[0]
    seg_len = ko_ref.shape[0]
    scale = 1.0 / math.sqrt(q_ref.shape[-1])

    @pl.when((leaf_i == 0) & (head_i == 0) & (row_i == 0))
    def _():
        dka_ref[...] = jnp.zeros_like(dka_ref)
        dva_ref[...] = jnp.zeros_like(dva_ref)

    @pl.when((head_i == 0) & (row_i == 0))
    def _():
        dko_acc[...] = jnp.zeros_like(dko_acc)
        dvo_acc[...] = jnp.zeros_like(dvo_acc)

    nt = (((1,), (1,)), ((), ()))
    tn = (((0,), (0,)), ((), ()))
    q = q_ref[...]
    g = g_ref[...]
    ka = jnp.concatenate([r[...] for r in ka_refs], axis=0)
    va = jnp.concatenate([r[...] for r in va_refs], axis=0)
    ko = ko_ref[...]
    vo = vo_ref[...]
    s_a = lax.dot_general(q, ka, nt, preferred_element_type=jnp.float32) * scale
    s_o = lax.dot_general(q, ko, nt, preferred_element_type=jnp.float32) * scale
    s_a = jnp.where(mask_ref[...] > 0.5, s_a, NEG_FILL)
    rows = row_i * block_rows + lax.broadcasted_iota(jnp.int32, (block_rows, seg_len), 0)
    cols = lax.broadcasted_iota(jnp.int32, (block_rows, seg_len), 1)
    s_o = jnp.where(cols <= rows, s_o, NEG_FILL)
    m = jnp.maximum(jnp.max(s_a, axis=1, keepdims=True), jnp.max(s_o, axis=1, keepdims=True))
    w_a = jnp.exp(s_a - m)
    w_o = jnp.exp(s_o - m)
    total = jnp.sum(w_a, axis=1, keepdims=True) + jnp.sum(w_o, axis=1, keepdims=True)
    inv = 1.0 / total
    p_a = w_a * inv
    p_o = w_o * inv
    pb_a = p_a.astype(jnp.bfloat16)
    pb_o = p_o.astype(jnp.bfloat16)
    o = jnp.dot(pb_a, va, preferred_element_type=jnp.float32) + jnp.dot(pb_o, vo, preferred_element_type=jnp.float32)
    o_b = o.astype(jnp.bfloat16)
    row_span = pl.ds(pl.multiple_of(row_i * block_rows, block_rows), block_rows)
    back_ref[row_span, pl.ds(pl.multiple_of(head_i * HD, HD), HD)] = o_b
    delta = jnp.sum(g.astype(jnp.float32) * o_b.astype(jnp.float32), axis=1, keepdims=True)
    dp_a = lax.dot_general(g, va, nt, preferred_element_type=jnp.float32)
    dp_o = lax.dot_general(g, vo, nt, preferred_element_type=jnp.float32)
    ds_a = (p_a * (dp_a - delta)).astype(jnp.bfloat16)
    ds_o = (p_o * (dp_o - delta)).astype(jnp.bfloat16)
    dq = (jnp.dot(ds_a, ka, preferred_element_type=jnp.float32) + jnp.dot(ds_o, ko, preferred_element_type=jnp.float32)) * scale
    back_ref[row_span, pl.ds(pl.multiple_of((head_count + head_i) * HD, HD), HD)] = dq.astype(jnp.bfloat16)
    dka_ref[...] += lax.dot_general(ds_a, q, tn, preferred_element_type=jnp.float32)
    dva_ref[...] += lax.dot_general(pb_a, g, tn, preferred_element_type=jnp.float32)
    dko_acc[...] += lax.dot_general(ds_o, q, tn, preferred_element_type=jnp.float32)
    dvo_acc[...] += lax.dot_general(pb_o, g, tn, preferred_element_type=jnp.float32)

    @pl.when((head_i == head_count - 1) & (row_i == row_count - 1))
    def _():
        back_ref[:, 2 * head_count * HD : (2 * head_count + 1) * HD] = (dko_acc[...] * scale).astype(jnp.bfloat16)
        back_ref[:, (2 * head_count + 1) * HD :] = dvo_acc[...].astype(jnp.bfloat16)

    @pl.when((leaf_i == pl.num_programs(0) - 1) & (head_i == head_count - 1) & (row_i == row_count - 1))
    def _():
        dka_ref[...] = dka_ref[...] * scale


def attend_all(anc_mask, packed, anc_blocks, anc_owner, heads, block_rows=512):
    leaves, seg_len, _ = packed.shape
    levels = anc_owner.shape[0]
    anc = levels * seg_len
    grid = (leaves, heads, seg_len // block_rows)
    qspec = pl.BlockSpec((None, block_rows, HD), lambda l, h, r, own: (l, r, h))
    gspec = pl.BlockSpec((None, block_rows, HD), lambda l, h, r, own: (l, r, heads + h))
    kospec = pl.BlockSpec((None, seg_len, HD), lambda l, h, r, own: (l, 0, 2 * heads))
    vospec = pl.BlockSpec((None, seg_len, HD), lambda l, h, r, own: (l, 0, 2 * heads + 1))
    maskspec = pl.BlockSpec((1, anc), lambda l, h, r, own: (0, 0))
    ancspec = pl.BlockSpec((anc, HD), lambda l, h, r, own: (0, 0))

    def level_spec(level, column):
        return pl.BlockSpec((None, seg_len, HD), lambda l, h, r, own: (own[level], 0, column))

    kaspecs = [level_spec(level, 0) for level in range(levels)]
    vaspecs = [level_spec(level, 1) for level in range(levels)]
    back_rows = jax.ShapeDtypeStruct((leaves, seg_len, (2 * heads + 2) * HD), jnp.bfloat16)
    backspec = pl.BlockSpec((None, seg_len, (2 * heads + 2) * HD), lambda l, h, r, own: (l, 0, 0))
    anc_grad = jax.ShapeDtypeStruct((anc, HD), jnp.float32)
    return pl.pallas_call(
        attend_kernel,
        grid_spec=pltpu.PrefetchScalarGridSpec(
            num_scalar_prefetch=1,
            grid=grid,
            in_specs=[maskspec, qspec, gspec, kospec, vospec] + kaspecs + vaspecs,
            out_specs=[backspec, ancspec, ancspec],
            scratch_shapes=[pltpu.VMEM((seg_len, HD), jnp.float32), pltpu.VMEM((seg_len, HD), jnp.float32)],
        ),
        out_shape=[back_rows, anc_grad, anc_grad],
        compiler_params=pltpu.CompilerParams(dimension_semantics=("arbitrary", "arbitrary", "arbitrary")),
    )(anc_owner, anc_mask, packed, packed, packed, packed, *([anc_blocks] * (2 * levels)))


def on_device(queries, leaf_keys, leaf_values, inner_keys, inner_values, out_grad, ancestors, depths):
    seg_count = lax.axis_size("seg")
    leaf_count = lax.axis_size("leaf")
    seg_here = lax.axis_index("seg")
    leaf_here = lax.axis_index("leaf")
    leaf_dev, rows_here, query_width = queries.shape
    slot_count = inner_keys.shape[0]
    key_width = leaf_keys.shape[2]
    kv_heads = key_width // HD
    group_heads = query_width // key_width
    head_width = group_heads * HD
    seg_len = rows_here * leaf_count
    levels = ancestors.shape[1]
    pair_count = leaf_count // kv_heads
    pair_leaves = leaf_dev // pair_count
    my_pair = leaf_here % pair_count

    group_lists = ancestors[::leaf_dev]
    group_depth = depths[::leaf_dev]
    owners = group_lists // slot_count
    slot_of = group_lists % slot_count
    level_ids = jnp.arange(levels, dtype=jnp.int32)
    alive_levels = level_ids[None, :] < group_depth[:, None]
    served = alive_levels & (owners == seg_here)
    slot_ids = jnp.arange(slot_count, dtype=jnp.int32)
    serve_pick = jnp.sum(
        (served[:, :, None] & (slot_of[:, :, None] == slot_ids[None, None, :])).astype(jnp.float32),
        axis=1,
    ).astype(jnp.bfloat16)
    stored = jnp.concatenate([inner_keys, inner_values], axis=2)
    outgoing = jnp.einsum("gs,src->grc", serve_pick, stored, preferred_element_type=jnp.float32).astype(
        jnp.bfloat16
    )
    my_owners = jnp.take(owners, seg_here, axis=0)
    my_alive = jnp.take(alive_levels, seg_here, axis=0)
    out_heads = jnp.concatenate(
        [
            outgoing[:, :, :key_width].reshape(seg_count, rows_here, kv_heads, 1, HD),
            outgoing[:, :, key_width:].reshape(seg_count, rows_here, kv_heads, 1, HD),
        ],
        axis=3,
    ).reshape(seg_count, rows_here, kv_heads, 2 * HD).transpose(0, 2, 1, 3)
    anc_send = jnp.broadcast_to(
        out_heads[:, :, None], (seg_count, kv_heads, pair_count, rows_here, 2 * HD)
    ).reshape(seg_count * leaf_count, rows_here, 2 * HD)
    anc_arrived = lax.all_to_all(anc_send, ("seg", "leaf"), split_axis=0, concat_axis=0, tiled=True)
    anc_arrived = anc_arrived.reshape(seg_count, leaf_count * rows_here, 2 * HD)
    anc_mask = jnp.repeat(my_alive, seg_len).astype(jnp.float32)[None, :]

    def to_heads(x, width):
        shaped = x.reshape(pair_count, pair_leaves, rows_here, kv_heads, width)
        return shaped.transpose(3, 0, 1, 2, 4).reshape(leaf_count, pair_leaves, rows_here, width)

    packed = jnp.concatenate(
        [to_heads(queries, head_width), to_heads(out_grad, head_width), to_heads(leaf_keys, HD), to_heads(leaf_values, HD)],
        axis=3,
    )
    homes = []
    anc_partial = None
    for chunk in range(pair_leaves):
        got = lax.all_to_all(packed[:, chunk], "leaf", split_axis=0, concat_axis=0, tiled=True)
        got = got.reshape(1, seg_len, packed.shape[3])
        back, dka, dva = attend_all(anc_mask, got, anc_arrived, my_owners.astype(jnp.int32), group_heads)
        part = jnp.concatenate([dka, dva], axis=1)
        anc_partial = part if anc_partial is None else anc_partial + part
        back = back.reshape(leaf_count, rows_here, back.shape[2])
        homes.append(lax.all_to_all(back, "leaf", split_axis=0, concat_axis=0, tiled=True))
    home = jnp.stack(homes, axis=1)
    home = home.reshape(kv_heads, pair_count, pair_leaves, rows_here, home.shape[3])

    def to_rows(x):
        width = x.shape[-1]
        return x.transpose(1, 2, 3, 0, 4).reshape(leaf_dev, rows_here, kv_heads * width)

    attention = to_rows(home[..., :head_width])
    query_grad = to_rows(home[..., head_width : 2 * head_width])
    leaf_key_grad = to_rows(home[..., 2 * head_width : 2 * head_width + HD])
    leaf_value_grad = to_rows(home[..., 2 * head_width + HD :])

    seg_ids = jnp.arange(seg_count, dtype=jnp.int32)
    homeward_pick = ((my_owners[None, :] == seg_ids[:, None]) & my_alive[None, :]).astype(jnp.bfloat16)
    partial_rows = anc_partial.astype(jnp.bfloat16).reshape(levels, seg_len, 2 * HD)
    homeward = jnp.einsum("ok,krc->orc", homeward_pick, partial_rows, preferred_element_type=jnp.float32).astype(
        jnp.bfloat16
    )
    homeward = homeward.reshape(seg_count * leaf_count, rows_here, 2 * HD)
    returned = lax.all_to_all(homeward, ("seg", "leaf"), split_axis=0, concat_axis=0, tiled=True)
    returned = returned.astype(jnp.float32).reshape(seg_count, kv_heads, pair_count, rows_here, 2 * HD).sum(axis=2)
    collected = jnp.einsum(
        "gs,ghrc->shrc", serve_pick.astype(jnp.float32), returned, preferred_element_type=jnp.float32
    )
    inner_key_grad = collected[..., :HD].transpose(0, 2, 1, 3).reshape(slot_count, rows_here, key_width)
    inner_value_grad = collected[..., HD:].transpose(0, 2, 1, 3).reshape(slot_count, rows_here, key_width)
    return (
        attention,
        query_grad,
        leaf_key_grad,
        leaf_value_grad,
        inner_key_grad.astype(jnp.bfloat16),
        inner_value_grad.astype(jnp.bfloat16),
    )


def solution(mesh):
    spec = P("seg", "leaf", None)
    return jax.shard_map(
        on_device,
        mesh=mesh,
        in_specs=(spec, spec, spec, spec, spec, spec, P(), P()),
        out_specs=(spec, spec, spec, spec, spec, spec),
        check_vma=False,
    )
```

```python
import math

import jax
import jax.numpy as jnp
from jax import lax
from jax.experimental import pallas as pl
from jax.experimental.pallas import tpu as pltpu
from jax.sharding import PartitionSpec as P

HD = 128


NEG_FILL = -1e30


def attend_kernel(owner_ref, mask_ref, q_ref, g_ref, ko_ref, vo_ref, *refs):
    levels = (len(refs) - 7) // 2
    ka_refs, va_refs = refs[:levels], refs[levels : 2 * levels]
    back_ref, dka_ref, dva_ref, dko_acc, dvo_acc, ka_all, va_all = refs[2 * levels :]
    leaf_i = pl.program_id(0)
    head_i = pl.program_id(1)
    row_i = pl.program_id(2)
    head_count = pl.num_programs(1)
    row_count = pl.num_programs(2)
    block_rows = q_ref.shape[0]
    seg_len = ko_ref.shape[0]
    scale = 1.0 / math.sqrt(q_ref.shape[-1])

    @pl.when((leaf_i == 0) & (head_i == 0) & (row_i == 0))
    def _():
        dka_ref[...] = jnp.zeros_like(dka_ref)
        dva_ref[...] = jnp.zeros_like(dva_ref)

    @pl.when((head_i == 0) & (row_i == 0))
    def _():
        dko_acc[...] = jnp.zeros_like(dko_acc)
        dvo_acc[...] = jnp.zeros_like(dvo_acc)

    nt = (((1,), (1,)), ((), ()))
    tn = (((0,), (0,)), ((), ()))
    q = q_ref[...]
    g = g_ref[...]
    @pl.when((leaf_i == 0) & (head_i == 0) & (row_i == 0))
    def _():
        for level in range(levels):
            ka_all[level * seg_len : (level + 1) * seg_len, :] = ka_refs[level][...]
            va_all[level * seg_len : (level + 1) * seg_len, :] = va_refs[level][...]

    ka = ka_all[...]
    va = va_all[...]
    ko = ko_ref[...]
    vo = vo_ref[...]
    s_a = lax.dot_general(q, ka, nt, preferred_element_type=jnp.float32) * scale
    s_o = lax.dot_general(q, ko, nt, preferred_element_type=jnp.float32) * scale
    s_a = jnp.where(mask_ref[...] > 0.5, s_a, NEG_FILL)
    rows = row_i * block_rows + lax.broadcasted_iota(jnp.int32, (block_rows, seg_len), 0)
    cols = lax.broadcasted_iota(jnp.int32, (block_rows, seg_len), 1)
    s_o = jnp.where(cols <= rows, s_o, NEG_FILL)
    m = jnp.maximum(jnp.max(s_a, axis=1, keepdims=True), jnp.max(s_o, axis=1, keepdims=True))
    w_a = jnp.exp(s_a - m)
    w_o = jnp.exp(s_o - m)
    total = jnp.sum(w_a, axis=1, keepdims=True) + jnp.sum(w_o, axis=1, keepdims=True)
    inv = 1.0 / total
    p_a = w_a * inv
    p_o = w_o * inv
    pb_a = p_a.astype(jnp.bfloat16)
    pb_o = p_o.astype(jnp.bfloat16)
    o = jnp.dot(pb_a, va, preferred_element_type=jnp.float32) + jnp.dot(pb_o, vo, preferred_element_type=jnp.float32)
    o_b = o.astype(jnp.bfloat16)
    row_span = pl.ds(pl.multiple_of(row_i * block_rows, block_rows), block_rows)
    back_ref[row_span, pl.ds(pl.multiple_of(head_i * HD, HD), HD)] = o_b
    delta = jnp.sum(g.astype(jnp.float32) * o_b.astype(jnp.float32), axis=1, keepdims=True)
    dp_a = lax.dot_general(g, va, nt, preferred_element_type=jnp.float32)
    dp_o = lax.dot_general(g, vo, nt, preferred_element_type=jnp.float32)
    ds_a = (p_a * (dp_a - delta)).astype(jnp.bfloat16)
    ds_o = (p_o * (dp_o - delta)).astype(jnp.bfloat16)
    dq = (jnp.dot(ds_a, ka, preferred_element_type=jnp.float32) + jnp.dot(ds_o, ko, preferred_element_type=jnp.float32)) * scale
    back_ref[row_span, pl.ds(pl.multiple_of((head_count + head_i) * HD, HD), HD)] = dq.astype(jnp.bfloat16)
    dka_ref[...] += lax.dot_general(ds_a, q, tn, preferred_element_type=jnp.float32)
    dva_ref[...] += lax.dot_general(pb_a, g, tn, preferred_element_type=jnp.float32)
    dko_acc[...] += lax.dot_general(ds_o, q, tn, preferred_element_type=jnp.float32)
    dvo_acc[...] += lax.dot_general(pb_o, g, tn, preferred_element_type=jnp.float32)

    @pl.when((head_i == head_count - 1) & (row_i == row_count - 1))
    def _():
        back_ref[:, 2 * head_count * HD : (2 * head_count + 1) * HD] = (dko_acc[...] * scale).astype(jnp.bfloat16)
        back_ref[:, (2 * head_count + 1) * HD :] = dvo_acc[...].astype(jnp.bfloat16)

    @pl.when((leaf_i == pl.num_programs(0) - 1) & (head_i == head_count - 1) & (row_i == row_count - 1))
    def _():
        dka_ref[...] = dka_ref[...] * scale


def attend_all(anc_mask, packed, anc_blocks, anc_owner, heads, block_rows=512):
    leaves, seg_len, _ = packed.shape
    levels = anc_owner.shape[0]
    anc = levels * seg_len
    grid = (leaves, heads, seg_len // block_rows)
    qspec = pl.BlockSpec((None, block_rows, HD), lambda l, h, r, own: (l, r, h))
    gspec = pl.BlockSpec((None, block_rows, HD), lambda l, h, r, own: (l, r, heads + h))
    kospec = pl.BlockSpec((None, seg_len, HD), lambda l, h, r, own: (l, 0, 2 * heads))
    vospec = pl.BlockSpec((None, seg_len, HD), lambda l, h, r, own: (l, 0, 2 * heads + 1))
    maskspec = pl.BlockSpec((1, anc), lambda l, h, r, own: (0, 0))
    ancspec = pl.BlockSpec((anc, HD), lambda l, h, r, own: (0, 0))

    def level_spec(level, column):
        return pl.BlockSpec((None, seg_len, HD), lambda l, h, r, own: (own[level], 0, column))

    kaspecs = [level_spec(level, 0) for level in range(levels)]
    vaspecs = [level_spec(level, 1) for level in range(levels)]
    back_rows = jax.ShapeDtypeStruct((leaves, seg_len, (2 * heads + 2) * HD), jnp.bfloat16)
    backspec = pl.BlockSpec((None, seg_len, (2 * heads + 2) * HD), lambda l, h, r, own: (l, 0, 0))
    anc_grad = jax.ShapeDtypeStruct((anc, HD), jnp.float32)
    return pl.pallas_call(
        attend_kernel,
        grid_spec=pltpu.PrefetchScalarGridSpec(
            num_scalar_prefetch=1,
            grid=grid,
            in_specs=[maskspec, qspec, gspec, kospec, vospec] + kaspecs + vaspecs,
            out_specs=[backspec, ancspec, ancspec],
            scratch_shapes=[
                pltpu.VMEM((seg_len, HD), jnp.float32),
                pltpu.VMEM((seg_len, HD), jnp.float32),
                pltpu.VMEM((anc, HD), anc_blocks.dtype),
                pltpu.VMEM((anc, HD), anc_blocks.dtype),
            ],
        ),
        out_shape=[back_rows, anc_grad, anc_grad],
        compiler_params=pltpu.CompilerParams(dimension_semantics=("arbitrary", "arbitrary", "arbitrary")),
    )(anc_owner, anc_mask, packed, packed, packed, packed, *([anc_blocks] * (2 * levels)))


def on_device(queries, leaf_keys, leaf_values, inner_keys, inner_values, out_grad, ancestors, depths):
    seg_count = lax.axis_size("seg")
    leaf_count = lax.axis_size("leaf")
    seg_here = lax.axis_index("seg")
    leaf_here = lax.axis_index("leaf")
    leaf_dev, rows_here, query_width = queries.shape
    slot_count = inner_keys.shape[0]
    key_width = leaf_keys.shape[2]
    kv_heads = key_width // HD
    group_heads = query_width // key_width
    head_width = group_heads * HD
    seg_len = rows_here * leaf_count
    levels = ancestors.shape[1]
    pair_count = leaf_count // kv_heads
    pair_leaves = leaf_dev // pair_count
    my_pair = leaf_here % pair_count

    group_lists = ancestors[::leaf_dev]
    group_depth = depths[::leaf_dev]
    owners = group_lists // slot_count
    slot_of = group_lists % slot_count
    level_ids = jnp.arange(levels, dtype=jnp.int32)
    alive_levels = level_ids[None, :] < group_depth[:, None]
    served = alive_levels & (owners == seg_here)
    slot_ids = jnp.arange(slot_count, dtype=jnp.int32)
    serve_pick = jnp.sum(
        (served[:, :, None] & (slot_of[:, :, None] == slot_ids[None, None, :])).astype(jnp.float32),
        axis=1,
    ).astype(jnp.bfloat16)
    stored = jnp.concatenate([inner_keys, inner_values], axis=2)
    outgoing = jnp.einsum("gs,src->grc", serve_pick, stored, preferred_element_type=jnp.float32).astype(
        jnp.bfloat16
    )
    my_owners = jnp.take(owners, seg_here, axis=0)
    my_alive = jnp.take(alive_levels, seg_here, axis=0)
    out_heads = jnp.concatenate(
        [
            outgoing[:, :, :key_width].reshape(seg_count, rows_here, kv_heads, 1, HD),
            outgoing[:, :, key_width:].reshape(seg_count, rows_here, kv_heads, 1, HD),
        ],
        axis=3,
    ).reshape(seg_count, rows_here, kv_heads, 2 * HD).transpose(0, 2, 1, 3)
    anc_send = jnp.broadcast_to(
        out_heads[:, :, None], (seg_count, kv_heads, pair_count, rows_here, 2 * HD)
    ).reshape(seg_count * leaf_count, rows_here, 2 * HD)
    anc_arrived = lax.all_to_all(anc_send, ("seg", "leaf"), split_axis=0, concat_axis=0, tiled=True)
    anc_arrived = anc_arrived.reshape(seg_count, leaf_count * rows_here, 2 * HD)
    anc_mask = jnp.repeat(my_alive, seg_len).astype(jnp.float32)[None, :]

    def to_heads(x, width):
        shaped = x.reshape(pair_count, pair_leaves, rows_here, kv_heads, width)
        return shaped.transpose(3, 0, 1, 2, 4).reshape(leaf_count, pair_leaves, rows_here, width)

    packed = jnp.concatenate(
        [to_heads(queries, head_width), to_heads(out_grad, head_width), to_heads(leaf_keys, HD), to_heads(leaf_values, HD)],
        axis=3,
    )
    homes = []
    anc_partial = None
    for chunk in range(pair_leaves):
        got = lax.all_to_all(packed[:, chunk], "leaf", split_axis=0, concat_axis=0, tiled=True)
        got = got.reshape(1, seg_len, packed.shape[3])
        back, dka, dva = attend_all(anc_mask, got, anc_arrived, my_owners.astype(jnp.int32), group_heads)
        part = jnp.concatenate([dka, dva], axis=1)
        anc_partial = part if anc_partial is None else anc_partial + part
        back = back.reshape(leaf_count, rows_here, back.shape[2])
        homes.append(lax.all_to_all(back, "leaf", split_axis=0, concat_axis=0, tiled=True))
    home = jnp.stack(homes, axis=1)
    home = home.reshape(kv_heads, pair_count, pair_leaves, rows_here, home.shape[3])

    def to_rows(x):
        width = x.shape[-1]
        return x.transpose(1, 2, 3, 0, 4).reshape(leaf_dev, rows_here, kv_heads * width)

    attention = to_rows(home[..., :head_width])
    query_grad = to_rows(home[..., head_width : 2 * head_width])
    leaf_key_grad = to_rows(home[..., 2 * head_width : 2 * head_width + HD])
    leaf_value_grad = to_rows(home[..., 2 * head_width + HD :])

    seg_ids = jnp.arange(seg_count, dtype=jnp.int32)
    homeward_pick = ((my_owners[None, :] == seg_ids[:, None]) & my_alive[None, :]).astype(jnp.bfloat16)
    partial_rows = anc_partial.astype(jnp.bfloat16).reshape(levels, seg_len, 2 * HD)
    homeward = jnp.einsum("ok,krc->orc", homeward_pick, partial_rows, preferred_element_type=jnp.float32).astype(
        jnp.bfloat16
    )
    homeward = homeward.reshape(seg_count * leaf_count, rows_here, 2 * HD)
    returned = lax.all_to_all(homeward, ("seg", "leaf"), split_axis=0, concat_axis=0, tiled=True)
    returned = returned.astype(jnp.float32).reshape(seg_count, kv_heads, pair_count, rows_here, 2 * HD).sum(axis=2)
    collected = jnp.einsum(
        "gs,ghrc->shrc", serve_pick.astype(jnp.float32), returned, preferred_element_type=jnp.float32
    )
    inner_key_grad = collected[..., :HD].transpose(0, 2, 1, 3).reshape(slot_count, rows_here, key_width)
    inner_value_grad = collected[..., HD:].transpose(0, 2, 1, 3).reshape(slot_count, rows_here, key_width)
    return (
        attention,
        query_grad,
        leaf_key_grad,
        leaf_value_grad,
        inner_key_grad.astype(jnp.bfloat16),
        inner_value_grad.astype(jnp.bfloat16),
    )


def solution(mesh):
    spec = P("seg", "leaf", None)
    return jax.shard_map(
        on_device,
        mesh=mesh,
        in_specs=(spec, spec, spec, spec, spec, spec, P(), P()),
        out_specs=(spec, spec, spec, spec, spec, spec),
        check_vma=False,
    )
```

```python
import math

import jax
import jax.numpy as jnp
from jax import lax
from jax.experimental import pallas as pl
from jax.experimental.pallas import tpu as pltpu
from jax.sharding import PartitionSpec as P

HD = 128


NEG_FILL = -1e30


def attend_kernel(owner_ref, mask_ref, q_ref, g_ref, ko_ref, vo_ref, *refs):
    levels = (len(refs) - 5) // 2
    ka_refs, va_refs = refs[:levels], refs[levels : 2 * levels]
    back_ref, dka_ref, dva_ref, dko_acc, dvo_acc = refs[2 * levels :]
    leaf_i = pl.program_id(0)
    head_i = pl.program_id(1)
    row_i = pl.program_id(2)
    head_count = pl.num_programs(1)
    row_count = pl.num_programs(2)
    block_rows = q_ref.shape[0]
    seg_len = ko_ref.shape[0]
    scale = 1.0 / math.sqrt(q_ref.shape[-1])

    @pl.when((leaf_i == 0) & (head_i == 0) & (row_i == 0))
    def _():
        dka_ref[...] = jnp.zeros_like(dka_ref)
        dva_ref[...] = jnp.zeros_like(dva_ref)

    @pl.when((head_i == 0) & (row_i == 0))
    def _():
        dko_acc[...] = jnp.zeros_like(dko_acc)
        dvo_acc[...] = jnp.zeros_like(dvo_acc)

    nt = (((1,), (1,)), ((), ()))
    tn = (((0,), (0,)), ((), ()))
    q = q_ref[...]
    g = g_ref[...]
    ka = jnp.concatenate([r[...] for r in ka_refs], axis=0)
    va = jnp.concatenate([r[...] for r in va_refs], axis=0)
    ko = ko_ref[...]
    vo = vo_ref[...]
    s_a = lax.dot_general(q, ka, nt, preferred_element_type=jnp.float32) * scale
    s_o = lax.dot_general(q, ko, nt, preferred_element_type=jnp.float32) * scale
    s_a = s_a + mask_ref[...]
    rows = row_i * block_rows + lax.broadcasted_iota(jnp.int32, (block_rows, seg_len), 0)
    cols = lax.broadcasted_iota(jnp.int32, (block_rows, seg_len), 1)
    s_o = jnp.where(cols <= rows, s_o, NEG_FILL)
    m = jnp.maximum(jnp.max(s_a, axis=1, keepdims=True), jnp.max(s_o, axis=1, keepdims=True))
    w_a = jnp.exp(s_a - m)
    w_o = jnp.exp(s_o - m)
    total = jnp.sum(w_a, axis=1, keepdims=True) + jnp.sum(w_o, axis=1, keepdims=True)
    inv = 1.0 / total
    p_a = w_a * inv
    p_o = w_o * inv
    pb_a = p_a.astype(jnp.bfloat16)
    pb_o = p_o.astype(jnp.bfloat16)
    o = jnp.dot(pb_a, va, preferred_element_type=jnp.float32) + jnp.dot(pb_o, vo, preferred_element_type=jnp.float32)
    o_b = o.astype(jnp.bfloat16)
    row_span = pl.ds(pl.multiple_of(row_i * block_rows, block_rows), block_rows)
    back_ref[row_span, pl.ds(pl.multiple_of(head_i * HD, HD), HD)] = o_b
    delta = jnp.sum(g.astype(jnp.float32) * o_b.astype(jnp.float32), axis=1, keepdims=True)
    dp_a = lax.dot_general(g, va, nt, preferred_element_type=jnp.float32)
    dp_o = lax.dot_general(g, vo, nt, preferred_element_type=jnp.float32)
    ds_a = (p_a * (dp_a - delta)).astype(jnp.bfloat16)
    ds_o = (p_o * (dp_o - delta)).astype(jnp.bfloat16)
    dq = (jnp.dot(ds_a, ka, preferred_element_type=jnp.float32) + jnp.dot(ds_o, ko, preferred_element_type=jnp.float32)) * scale
    back_ref[row_span, pl.ds(pl.multiple_of((head_count + head_i) * HD, HD), HD)] = dq.astype(jnp.bfloat16)
    dka_ref[...] += lax.dot_general(ds_a, q, tn, preferred_element_type=jnp.float32)
    dva_ref[...] += lax.dot_general(pb_a, g, tn, preferred_element_type=jnp.float32)
    dko_acc[...] += lax.dot_general(ds_o, q, tn, preferred_element_type=jnp.float32)
    dvo_acc[...] += lax.dot_general(pb_o, g, tn, preferred_element_type=jnp.float32)

    @pl.when((head_i == head_count - 1) & (row_i == row_count - 1))
    def _():
        back_ref[:, 2 * head_count * HD : (2 * head_count + 1) * HD] = (dko_acc[...] * scale).astype(jnp.bfloat16)
        back_ref[:, (2 * head_count + 1) * HD :] = dvo_acc[...].astype(jnp.bfloat16)

    @pl.when((leaf_i == pl.num_programs(0) - 1) & (head_i == head_count - 1) & (row_i == row_count - 1))
    def _():
        dka_ref[...] = dka_ref[...] * scale


def attend_all(anc_mask, packed, anc_blocks, anc_owner, heads, block_rows=512):
    leaves, seg_len, _ = packed.shape
    levels = anc_owner.shape[0]
    anc = levels * seg_len
    grid = (leaves, heads, seg_len // block_rows)
    qspec = pl.BlockSpec((None, block_rows, HD), lambda l, h, r, own: (l, r, h))
    gspec = pl.BlockSpec((None, block_rows, HD), lambda l, h, r, own: (l, r, heads + h))
    kospec = pl.BlockSpec((None, seg_len, HD), lambda l, h, r, own: (l, 0, 2 * heads))
    vospec = pl.BlockSpec((None, seg_len, HD), lambda l, h, r, own: (l, 0, 2 * heads + 1))
    maskspec = pl.BlockSpec((1, anc), lambda l, h, r, own: (0, 0))
    ancspec = pl.BlockSpec((anc, HD), lambda l, h, r, own: (0, 0))

    def level_spec(level, column):
        return pl.BlockSpec((None, seg_len, HD), lambda l, h, r, own: (own[level], 0, column))

    kaspecs = [level_spec(level, 0) for level in range(levels)]
    vaspecs = [level_spec(level, 1) for level in range(levels)]
    back_rows = jax.ShapeDtypeStruct((leaves, seg_len, (2 * heads + 2) * HD), jnp.bfloat16)
    backspec = pl.BlockSpec((None, seg_len, (2 * heads + 2) * HD), lambda l, h, r, own: (l, 0, 0))
    anc_grad = jax.ShapeDtypeStruct((anc, HD), jnp.float32)
    return pl.pallas_call(
        attend_kernel,
        grid_spec=pltpu.PrefetchScalarGridSpec(
            num_scalar_prefetch=1,
            grid=grid,
            in_specs=[maskspec, qspec, gspec, kospec, vospec] + kaspecs + vaspecs,
            out_specs=[backspec, ancspec, ancspec],
            scratch_shapes=[pltpu.VMEM((seg_len, HD), jnp.float32), pltpu.VMEM((seg_len, HD), jnp.float32)],
        ),
        out_shape=[back_rows, anc_grad, anc_grad],
        compiler_params=pltpu.CompilerParams(dimension_semantics=("arbitrary", "arbitrary", "arbitrary")),
    )(anc_owner, anc_mask, packed, packed, packed, packed, *([anc_blocks] * (2 * levels)))


def on_device(queries, leaf_keys, leaf_values, inner_keys, inner_values, out_grad, ancestors, depths):
    seg_count = lax.axis_size("seg")
    leaf_count = lax.axis_size("leaf")
    seg_here = lax.axis_index("seg")
    leaf_here = lax.axis_index("leaf")
    leaf_dev, rows_here, query_width = queries.shape
    slot_count = inner_keys.shape[0]
    key_width = leaf_keys.shape[2]
    kv_heads = key_width // HD
    group_heads = query_width // key_width
    head_width = group_heads * HD
    seg_len = rows_here * leaf_count
    levels = ancestors.shape[1]
    pair_count = leaf_count // kv_heads
    pair_leaves = leaf_dev // pair_count
    my_pair = leaf_here % pair_count

    group_lists = ancestors[::leaf_dev]
    group_depth = depths[::leaf_dev]
    owners = group_lists // slot_count
    slot_of = group_lists % slot_count
    level_ids = jnp.arange(levels, dtype=jnp.int32)
    alive_levels = level_ids[None, :] < group_depth[:, None]
    served = alive_levels & (owners == seg_here)
    slot_ids = jnp.arange(slot_count, dtype=jnp.int32)
    serve_pick = jnp.sum(
        (served[:, :, None] & (slot_of[:, :, None] == slot_ids[None, None, :])).astype(jnp.float32),
        axis=1,
    ).astype(jnp.bfloat16)
    stored = jnp.concatenate([inner_keys, inner_values], axis=2)
    outgoing = jnp.einsum("gs,src->grc", serve_pick, stored, preferred_element_type=jnp.float32).astype(
        jnp.bfloat16
    )
    my_owners = jnp.take(owners, seg_here, axis=0)
    my_alive = jnp.take(alive_levels, seg_here, axis=0)
    out_heads = jnp.concatenate(
        [
            outgoing[:, :, :key_width].reshape(seg_count, rows_here, kv_heads, 1, HD),
            outgoing[:, :, key_width:].reshape(seg_count, rows_here, kv_heads, 1, HD),
        ],
        axis=3,
    ).reshape(seg_count, rows_here, kv_heads, 2 * HD).transpose(0, 2, 1, 3)
    anc_send = jnp.broadcast_to(
        out_heads[:, :, None], (seg_count, kv_heads, pair_count, rows_here, 2 * HD)
    ).reshape(seg_count * leaf_count, rows_here, 2 * HD)
    anc_arrived = lax.all_to_all(anc_send, ("seg", "leaf"), split_axis=0, concat_axis=0, tiled=True)
    anc_arrived = anc_arrived.reshape(seg_count, leaf_count * rows_here, 2 * HD)
    anc_mask = jnp.where(jnp.repeat(my_alive, seg_len), 0.0, NEG_FILL).astype(jnp.float32)[None, :]

    def to_heads(x, width):
        shaped = x.reshape(pair_count, pair_leaves, rows_here, kv_heads, width)
        return shaped.transpose(3, 0, 1, 2, 4).reshape(leaf_count, pair_leaves, rows_here, width)

    packed = jnp.concatenate(
        [to_heads(queries, head_width), to_heads(out_grad, head_width), to_heads(leaf_keys, HD), to_heads(leaf_values, HD)],
        axis=3,
    )
    homes = []
    anc_partial = None
    for chunk in range(pair_leaves):
        got = lax.all_to_all(packed[:, chunk], "leaf", split_axis=0, concat_axis=0, tiled=True)
        got = got.reshape(1, seg_len, packed.shape[3])
        back, dka, dva = attend_all(anc_mask, got, anc_arrived, my_owners.astype(jnp.int32), group_heads)
        part = jnp.concatenate([dka, dva], axis=1)
        anc_partial = part if anc_partial is None else anc_partial + part
        back = back.reshape(leaf_count, rows_here, back.shape[2])
        homes.append(lax.all_to_all(back, "leaf", split_axis=0, concat_axis=0, tiled=True))
    home = jnp.stack(homes, axis=1)
    home = home.reshape(kv_heads, pair_count, pair_leaves, rows_here, home.shape[3])

    def to_rows(x):
        width = x.shape[-1]
        return x.transpose(1, 2, 3, 0, 4).reshape(leaf_dev, rows_here, kv_heads * width)

    attention = to_rows(home[..., :head_width])
    query_grad = to_rows(home[..., head_width : 2 * head_width])
    leaf_key_grad = to_rows(home[..., 2 * head_width : 2 * head_width + HD])
    leaf_value_grad = to_rows(home[..., 2 * head_width + HD :])

    seg_ids = jnp.arange(seg_count, dtype=jnp.int32)
    homeward_pick = ((my_owners[None, :] == seg_ids[:, None]) & my_alive[None, :]).astype(jnp.bfloat16)
    partial_rows = anc_partial.astype(jnp.bfloat16).reshape(levels, seg_len, 2 * HD)
    homeward = jnp.einsum("ok,krc->orc", homeward_pick, partial_rows, preferred_element_type=jnp.float32).astype(
        jnp.bfloat16
    )
    homeward = homeward.reshape(seg_count * leaf_count, rows_here, 2 * HD)
    returned = lax.all_to_all(homeward, ("seg", "leaf"), split_axis=0, concat_axis=0, tiled=True)
    returned = returned.astype(jnp.float32).reshape(seg_count, kv_heads, pair_count, rows_here, 2 * HD).sum(axis=2)
    collected = jnp.einsum(
        "gs,ghrc->shrc", serve_pick.astype(jnp.float32), returned, preferred_element_type=jnp.float32
    )
    inner_key_grad = collected[..., :HD].transpose(0, 2, 1, 3).reshape(slot_count, rows_here, key_width)
    inner_value_grad = collected[..., HD:].transpose(0, 2, 1, 3).reshape(slot_count, rows_here, key_width)
    return (
        attention,
        query_grad,
        leaf_key_grad,
        leaf_value_grad,
        inner_key_grad.astype(jnp.bfloat16),
        inner_value_grad.astype(jnp.bfloat16),
    )


def solution(mesh):
    spec = P("seg", "leaf", None)
    return jax.shard_map(
        on_device,
        mesh=mesh,
        in_specs=(spec, spec, spec, spec, spec, spec, P(), P()),
        out_specs=(spec, spec, spec, spec, spec, spec),
        check_vma=False,
    )
```

```python
import math

import jax
import jax.numpy as jnp
from jax import lax
from jax.experimental import pallas as pl
from jax.experimental.pallas import tpu as pltpu
from jax.sharding import PartitionSpec as P

HD = 128


NEG_FILL = -1e30


def attend_kernel(owner_ref, mask_ref, causal_ref, q_ref, g_ref, ko_ref, vo_ref, *refs):
    levels = (len(refs) - 5) // 2
    ka_refs, va_refs = refs[:levels], refs[levels : 2 * levels]
    back_ref, dka_ref, dva_ref, dko_acc, dvo_acc = refs[2 * levels :]
    leaf_i = pl.program_id(0)
    head_i = pl.program_id(1)
    row_i = pl.program_id(2)
    head_count = pl.num_programs(1)
    row_count = pl.num_programs(2)
    block_rows = q_ref.shape[0]
    seg_len = ko_ref.shape[0]
    scale = 1.0 / math.sqrt(q_ref.shape[-1])

    @pl.when((leaf_i == 0) & (head_i == 0) & (row_i == 0))
    def _():
        dka_ref[...] = jnp.zeros_like(dka_ref)
        dva_ref[...] = jnp.zeros_like(dva_ref)

    @pl.when((head_i == 0) & (row_i == 0))
    def _():
        dko_acc[...] = jnp.zeros_like(dko_acc)
        dvo_acc[...] = jnp.zeros_like(dvo_acc)

    nt = (((1,), (1,)), ((), ()))
    tn = (((0,), (0,)), ((), ()))
    q = q_ref[...]
    g = g_ref[...]
    ka = jnp.concatenate([r[...] for r in ka_refs], axis=0)
    va = jnp.concatenate([r[...] for r in va_refs], axis=0)
    ko = ko_ref[...]
    vo = vo_ref[...]
    s_a = lax.dot_general(q, ka, nt, preferred_element_type=jnp.float32) * scale
    s_o = lax.dot_general(q, ko, nt, preferred_element_type=jnp.float32) * scale
    s_a = s_a + mask_ref[...]
    s_o = s_o + causal_ref[...]
    m = jnp.maximum(jnp.max(s_a, axis=1, keepdims=True), jnp.max(s_o, axis=1, keepdims=True))
    w_a = jnp.exp(s_a - m)
    w_o = jnp.exp(s_o - m)
    total = jnp.sum(w_a, axis=1, keepdims=True) + jnp.sum(w_o, axis=1, keepdims=True)
    inv = 1.0 / total
    p_a = w_a * inv
    p_o = w_o * inv
    pb_a = p_a.astype(jnp.bfloat16)
    pb_o = p_o.astype(jnp.bfloat16)
    o = jnp.dot(pb_a, va, preferred_element_type=jnp.float32) + jnp.dot(pb_o, vo, preferred_element_type=jnp.float32)
    o_b = o.astype(jnp.bfloat16)
    row_span = pl.ds(pl.multiple_of(row_i * block_rows, block_rows), block_rows)
    back_ref[row_span, pl.ds(pl.multiple_of(head_i * HD, HD), HD)] = o_b
    delta = jnp.sum(g.astype(jnp.float32) * o_b.astype(jnp.float32), axis=1, keepdims=True)
    dp_a = lax.dot_general(g, va, nt, preferred_element_type=jnp.float32)
    dp_o = lax.dot_general(g, vo, nt, preferred_element_type=jnp.float32)
    ds_a = (p_a * (dp_a - delta)).astype(jnp.bfloat16)
    ds_o = (p_o * (dp_o - delta)).astype(jnp.bfloat16)
    dq = (jnp.dot(ds_a, ka, preferred_element_type=jnp.float32) + jnp.dot(ds_o, ko, preferred_element_type=jnp.float32)) * scale
    back_ref[row_span, pl.ds(pl.multiple_of((head_count + head_i) * HD, HD), HD)] = dq.astype(jnp.bfloat16)
    dka_ref[...] += lax.dot_general(ds_a, q, tn, preferred_element_type=jnp.float32)
    dva_ref[...] += lax.dot_general(pb_a, g, tn, preferred_element_type=jnp.float32)
    dko_acc[...] += lax.dot_general(ds_o, q, tn, preferred_element_type=jnp.float32)
    dvo_acc[...] += lax.dot_general(pb_o, g, tn, preferred_element_type=jnp.float32)

    @pl.when((head_i == head_count - 1) & (row_i == row_count - 1))
    def _():
        back_ref[:, 2 * head_count * HD : (2 * head_count + 1) * HD] = (dko_acc[...] * scale).astype(jnp.bfloat16)
        back_ref[:, (2 * head_count + 1) * HD :] = dvo_acc[...].astype(jnp.bfloat16)

    @pl.when((leaf_i == pl.num_programs(0) - 1) & (head_i == head_count - 1) & (row_i == row_count - 1))
    def _():
        dka_ref[...] = dka_ref[...] * scale


def attend_all(anc_mask, packed, anc_blocks, anc_owner, heads, block_rows=512):
    leaves, seg_len, _ = packed.shape
    levels = anc_owner.shape[0]
    anc = levels * seg_len
    grid = (leaves, heads, seg_len // block_rows)
    qspec = pl.BlockSpec((None, block_rows, HD), lambda l, h, r, own: (l, r, h))
    gspec = pl.BlockSpec((None, block_rows, HD), lambda l, h, r, own: (l, r, heads + h))
    kospec = pl.BlockSpec((None, seg_len, HD), lambda l, h, r, own: (l, 0, 2 * heads))
    vospec = pl.BlockSpec((None, seg_len, HD), lambda l, h, r, own: (l, 0, 2 * heads + 1))
    maskspec = pl.BlockSpec((1, anc), lambda l, h, r, own: (0, 0))
    causalspec = pl.BlockSpec((block_rows, seg_len), lambda l, h, r, own: (r, 0))
    positions = lax.broadcasted_iota(jnp.int32, (seg_len, seg_len), 0) + anc_owner[0] * 0
    causal = jnp.where(lax.broadcasted_iota(jnp.int32, (seg_len, seg_len), 1) <= positions, 0.0, NEG_FILL).astype(jnp.float32)
    ancspec = pl.BlockSpec((anc, HD), lambda l, h, r, own: (0, 0))

    def level_spec(level, column):
        return pl.BlockSpec((None, seg_len, HD), lambda l, h, r, own: (own[level], 0, column))

    kaspecs = [level_spec(level, 0) for level in range(levels)]
    vaspecs = [level_spec(level, 1) for level in range(levels)]
    back_rows = jax.ShapeDtypeStruct((leaves, seg_len, (2 * heads + 2) * HD), jnp.bfloat16)
    backspec = pl.BlockSpec((None, seg_len, (2 * heads + 2) * HD), lambda l, h, r, own: (l, 0, 0))
    anc_grad = jax.ShapeDtypeStruct((anc, HD), jnp.float32)
    return pl.pallas_call(
        attend_kernel,
        grid_spec=pltpu.PrefetchScalarGridSpec(
            num_scalar_prefetch=1,
            grid=grid,
            in_specs=[maskspec, causalspec, qspec, gspec, kospec, vospec] + kaspecs + vaspecs,
            out_specs=[backspec, ancspec, ancspec],
            scratch_shapes=[pltpu.VMEM((seg_len, HD), jnp.float32), pltpu.VMEM((seg_len, HD), jnp.float32)],
        ),
        out_shape=[back_rows, anc_grad, anc_grad],
        compiler_params=pltpu.CompilerParams(dimension_semantics=("arbitrary", "arbitrary", "arbitrary")),
    )(anc_owner, anc_mask, causal, packed, packed, packed, packed, *([anc_blocks] * (2 * levels)))


def on_device(queries, leaf_keys, leaf_values, inner_keys, inner_values, out_grad, ancestors, depths):
    seg_count = lax.axis_size("seg")
    leaf_count = lax.axis_size("leaf")
    seg_here = lax.axis_index("seg")
    leaf_here = lax.axis_index("leaf")
    leaf_dev, rows_here, query_width = queries.shape
    slot_count = inner_keys.shape[0]
    key_width = leaf_keys.shape[2]
    kv_heads = key_width // HD
    group_heads = query_width // key_width
    head_width = group_heads * HD
    seg_len = rows_here * leaf_count
    levels = ancestors.shape[1]
    pair_count = leaf_count // kv_heads
    pair_leaves = leaf_dev // pair_count
    my_pair = leaf_here % pair_count

    group_lists = ancestors[::leaf_dev]
    group_depth = depths[::leaf_dev]
    owners = group_lists // slot_count
    slot_of = group_lists % slot_count
    level_ids = jnp.arange(levels, dtype=jnp.int32)
    alive_levels = level_ids[None, :] < group_depth[:, None]
    served = alive_levels & (owners == seg_here)
    slot_ids = jnp.arange(slot_count, dtype=jnp.int32)
    serve_pick = jnp.sum(
        (served[:, :, None] & (slot_of[:, :, None] == slot_ids[None, None, :])).astype(jnp.float32),
        axis=1,
    ).astype(jnp.bfloat16)
    stored = jnp.concatenate([inner_keys, inner_values], axis=2)
    outgoing = jnp.einsum("gs,src->grc", serve_pick, stored, preferred_element_type=jnp.float32).astype(
        jnp.bfloat16
    )
    my_owners = jnp.take(owners, seg_here, axis=0)
    my_alive = jnp.take(alive_levels, seg_here, axis=0)
    out_heads = jnp.concatenate(
        [
            outgoing[:, :, :key_width].reshape(seg_count, rows_here, kv_heads, 1, HD),
            outgoing[:, :, key_width:].reshape(seg_count, rows_here, kv_heads, 1, HD),
        ],
        axis=3,
    ).reshape(seg_count, rows_here, kv_heads, 2 * HD).transpose(0, 2, 1, 3)
    anc_send = jnp.broadcast_to(
        out_heads[:, :, None], (seg_count, kv_heads, pair_count, rows_here, 2 * HD)
    ).reshape(seg_count * leaf_count, rows_here, 2 * HD)
    anc_arrived = lax.all_to_all(anc_send, ("seg", "leaf"), split_axis=0, concat_axis=0, tiled=True)
    anc_arrived = anc_arrived.reshape(seg_count, leaf_count * rows_here, 2 * HD)
    anc_mask = jnp.where(jnp.repeat(my_alive, seg_len), 0.0, NEG_FILL).astype(jnp.float32)[None, :]

    def to_heads(x, width):
        shaped = x.reshape(pair_count, pair_leaves, rows_here, kv_heads, width)
        return shaped.transpose(3, 0, 1, 2, 4).reshape(leaf_count, pair_leaves, rows_here, width)

    packed = jnp.concatenate(
        [to_heads(queries, head_width), to_heads(out_grad, head_width), to_heads(leaf_keys, HD), to_heads(leaf_values, HD)],
        axis=3,
    )
    homes = []
    anc_partial = None
    for chunk in range(pair_leaves):
        got = lax.all_to_all(packed[:, chunk], "leaf", split_axis=0, concat_axis=0, tiled=True)
        got = got.reshape(1, seg_len, packed.shape[3])
        back, dka, dva = attend_all(anc_mask, got, anc_arrived, my_owners.astype(jnp.int32), group_heads)
        part = jnp.concatenate([dka, dva], axis=1)
        anc_partial = part if anc_partial is None else anc_partial + part
        back = back.reshape(leaf_count, rows_here, back.shape[2])
        homes.append(lax.all_to_all(back, "leaf", split_axis=0, concat_axis=0, tiled=True))
    home = jnp.stack(homes, axis=1)
    home = home.reshape(kv_heads, pair_count, pair_leaves, rows_here, home.shape[3])

    def to_rows(x):
        width = x.shape[-1]
        return x.transpose(1, 2, 3, 0, 4).reshape(leaf_dev, rows_here, kv_heads * width)

    attention = to_rows(home[..., :head_width])
    query_grad = to_rows(home[..., head_width : 2 * head_width])
    leaf_key_grad = to_rows(home[..., 2 * head_width : 2 * head_width + HD])
    leaf_value_grad = to_rows(home[..., 2 * head_width + HD :])

    seg_ids = jnp.arange(seg_count, dtype=jnp.int32)
    homeward_pick = ((my_owners[None, :] == seg_ids[:, None]) & my_alive[None, :]).astype(jnp.bfloat16)
    partial_rows = anc_partial.astype(jnp.bfloat16).reshape(levels, seg_len, 2 * HD)
    homeward = jnp.einsum("ok,krc->orc", homeward_pick, partial_rows, preferred_element_type=jnp.float32).astype(
        jnp.bfloat16
    )
    homeward = homeward.reshape(seg_count * leaf_count, rows_here, 2 * HD)
    returned = lax.all_to_all(homeward, ("seg", "leaf"), split_axis=0, concat_axis=0, tiled=True)
    returned = returned.astype(jnp.float32).reshape(seg_count, kv_heads, pair_count, rows_here, 2 * HD).sum(axis=2)
    collected = jnp.einsum(
        "gs,ghrc->shrc", serve_pick.astype(jnp.float32), returned, preferred_element_type=jnp.float32
    )
    inner_key_grad = collected[..., :HD].transpose(0, 2, 1, 3).reshape(slot_count, rows_here, key_width)
    inner_value_grad = collected[..., HD:].transpose(0, 2, 1, 3).reshape(slot_count, rows_here, key_width)
    return (
        attention,
        query_grad,
        leaf_key_grad,
        leaf_value_grad,
        inner_key_grad.astype(jnp.bfloat16),
        inner_value_grad.astype(jnp.bfloat16),
    )


def solution(mesh):
    spec = P("seg", "leaf", None)
    return jax.shard_map(
        on_device,
        mesh=mesh,
        in_specs=(spec, spec, spec, spec, spec, spec, P(), P()),
        out_specs=(spec, spec, spec, spec, spec, spec),
        check_vma=False,
    )
```
